32 devices in a mesh: dp: 16 (over z, y, x), mp: 2 (over core).
Axes of the slice: x: 2, y: 2, z: 4, core: 2. Of those that a mesh axis runs over, the one named last changes fastest.
Arguments:
- text_input: bfloat16 [16384, 768], P(('dp', 'mp')), may hold values from -6 to 6
- layout_input: bfloat16 [16384, 192], P(('dp', 'mp')), may hold values from -6 to 6
- repeated: int32 [16384], P('dp'), may hold values 0 or 1
- key_mask: int32 [16384], P('dp'), may hold values 0 or 1
- text_qkv: bfloat16 [3, 768, 768], P(None, None, 'mp'), may hold values from -0.21875 to 0.21875
- text_qvbias: bfloat16 [2, 768], P(None, 'mp'), may hold values from -3 to 3
- text_wout: bfloat16 [768, 768], P('mp'), may hold values from -1.75 to 1.75
- text_outbias: bfloat16 [2, 768], replicated, may hold values from -2 to 2
- text_wup: bfloat16 [768, 3072], P(None, 'mp'), may hold values from -0.21875 to 0.21875
- text_upbias: bfloat16 [3072], P('mp'), may hold values from -3 to 3
- text_wdown: bfloat16 [3072, 768], P('mp'), may hold values from -0.21875 to 0.21875
- text_gains: bfloat16 [2, 768], replicated, may hold values from 0.5 to 1.5
- text_shifts: bfloat16 [2, 768], replicated, may hold values from -2 to 2
- layout_qkv: bfloat16 [3, 192, 192], P(None, None, 'mp'), may hold values from -0.4375 to 0.4375
- layout_qvbias: bfloat16 [2, 192], P(None, 'mp'), may hold values from -3 to 3
- layout_wout: bfloat16 [192, 192], P('mp'), may hold values from -1.75 to 1.75
- layout_outbias: bfloat16 [2, 192], replicated, may hold values from -2 to 2
- layout_wup: bfloat16 [192, 768], P(None, 'mp'), may hold values from -0.4375 to 0.4375
- layout_upbias: bfloat16 [768], P('mp'), may hold values from -3 to 3
- layout_wdown: bfloat16 [768, 192], P('mp'), may hold values from -0.4375 to 0.4375
- layout_gains: bfloat16 [2, 192], replicated, may hold values from 0.5 to 1.5
- layout_shifts: bfloat16 [2, 192], replicated, may hold values from -2 to 2
- text_cotan: bfloat16 [16384, 768], P(('dp', 'mp')), may hold values from -6 to 6
- layout_cotan: bfloat16 [16384, 192], P(('dp', 'mp')), may hold values from -6 to 6
Outputs:
- text_result: bfloat16 [16384, 768], P(('dp', 'mp'))
- layout_result: bfloat16 [16384, 192], P(('dp', 'mp'))
- text_dinput: bfloat16 [16384, 768], P(('dp', 'mp'))
- layout_dinput: bfloat16 [16384, 192], P(('dp', 'mp'))
- text_qkv_grad: float32 [3, 768, 768], P(None, 'dp', 'mp')
- text_qvbias_grad: float32 [2, 768], P(None, 'mp')
- text_wout_grad: float32 [768, 768], P('mp', 'dp')
- text_outbias_grad: float32 [2, 768], replicated
- text_wup_grad: float32 [768, 3072], P('dp', 'mp')
- text_upbias_grad: float32 [3072], P('mp')
- text_wdown_grad: float32 [3072, 768], P('mp', 'dp')
- text_gains_grad: float32 [2, 768], replicated
- text_shifts_grad: float32 [2, 768], replicated
- layout_qkv_grad: float32 [3, 192, 192], P(None, None, 'mp')
- layout_qvbias_grad: float32 [2, 192], P(None, 'mp')
- layout_wout_grad: float32 [192, 192], P('mp')
- layout_outbias_grad: float32 [2, 192], replicated
- layout_wup_grad: float32 [192, 768], P(None, 'mp')
- layout_upbias_grad: float32 [768], P('mp')
- layout_wdown_grad: float32 [768, 192], P('mp')
- layout_gains_grad: float32 [2, 192], replicated
- layout_shifts_grad: float32 [2, 192], replicated
The draws below stay inside these ranges and needn't reach their ends.
All inputs are finite; a program needn't handle non-finite values. No bound on the sum of `repeated` or of `key_mask` on one device may be relied on, other than what follows from the above.
Results may differ from the reference program's by a relative error of at most 0.02.
The reference program's roundings to bfloat16 on the way count: a program that leaves them out, or rounds other values in their place, can miss the bound.
Values may be sent and summed in bfloat16 or wider, within the bound.
No kernel may reach another device: no remote copies, remote signals or barrier semaphores. Data moves between devices by JAX's collectives and lax.ppermute only.
A program may use at most 128 MiB of HBM per device.

```python
import jax
import jax.numpy as jnp
from jax import lax

D = 768
H = 12
DL = 192
FF = 3072
FFL = 768
WINDOW = 512
WINDOWS_DEV = 2
ROWS = 16384
N_DP = 16


def with_ends(array, rng, smallest, largest):
    extent = array.shape
    spot = [jax.random.randint(jax.random.fold_in(rng, axis), (), 0, extent[axis]) for axis in range(len(extent))]
    array = array.at[tuple(spot)].set(smallest)
    longest = extent.index(max(extent))
    spot[longest] = (spot[longest] + 1) % extent[longest]
    return array.at[tuple(spot)].set(largest)


def spiked(entries, rng, source, target, parts, factor):
    def block_of(axis_at):
        return (jnp.arange(entries.shape[axis_at]) // (entries.shape[axis_at] // parts)).reshape((-1,) + (1,) * (entries.ndim - 1 - axis_at))

    first = jax.random.permutation(rng, parts)[block_of(target)]
    other_side = (block_of(target) + parts // 2) % parts
    return jnp.where((block_of(source) == first) | (block_of(source) == other_side), factor * entries, entries)


def block_levels(rng, dims, shards, least, top_value):
    level = 1.0
    for dim, parts in shards:
        steps = jax.random.uniform(jax.random.fold_in(jax.random.fold_in(rng, 6), dim), (parts,), jnp.float32, least / len(shards), top_value / len(shards))
        level = level * jnp.repeat(jnp.exp(steps), dims[dim] // parts).reshape((-1,) + (1,) * (len(dims) - 1 - dim))
    return level


def bell_draw(own_key, shape, spread, reach, cuts=(), dtype=jnp.bfloat16):
    array = jax.random.normal(own_key, shape, jnp.float32) * spread
    if len(cuts) > 0:
        array = block_levels(own_key, shape, cuts, -0.22, 0.18) * array
    return jnp.clip(array, min=-reach, max=reach).astype(dtype)


def heavy_noise(own_key, extent, scale, limit, shards, heavy, dtype=jnp.bfloat16):
    values = scale * jax.random.normal(own_key, extent, jnp.float32)
    if shards:
        values = values * block_levels(own_key, extent, shards, -0.22, 0.18)
    return jnp.clip(spiked(values, jax.random.fold_in(own_key, 3), *heavy), -limit, limit).astype(dtype)


def setup_inputs(seed: int = 0) -> dict:
    streams_of = jax.random.split(jax.random.key(seed), 25)
    return {
        "text_input": heavy_noise(streams_of[0], (ROWS, D), 1.0, 6.0, ((0, 32),), (0, 1, 32, 2.75)),
        "layout_input": bell_draw(streams_of[1], (ROWS, DL), 1.0, 6.0, ((0, 32),)),
        "repeated": with_ends((jax.random.randint(streams_of[2], (ROWS,), 0, 4) < 1).astype(jnp.int32), jax.random.fold_in(streams_of[2], 1), 0, 1),
        "key_mask": with_ends((jax.random.randint(streams_of[3], (ROWS,), 0, 8) < 7).astype(jnp.int32), jax.random.fold_in(streams_of[3], 1), 0, 1),
        "text_qkv": bell_draw(streams_of[4], (3, D, D), D ** -0.5, 0.21875, ((2, 2),)),
        "text_qvbias": bell_draw(streams_of[5], (2, D), 0.5, 3.0, ((1, 2),)),
        "text_wout": bell_draw(streams_of[6], (D, D), (D // 64) ** -0.5, 1.75, ((0, 2),)),
        "text_outbias": bell_draw(streams_of[7], (2, D), 0.3, 2.0),
        "text_wup": bell_draw(streams_of[8], (D, FF), D ** -0.5, 0.21875, ((1, 2),)),
        "text_upbias": bell_draw(streams_of[9], (FF,), 0.5, 3.0, ((0, 2),)),
        "text_wdown": bell_draw(streams_of[10], (FF, D), (FF // 4) ** -0.5, 0.21875, ((0, 2),)),
        "text_gains": jnp.clip(1.0 + 0.1 * jax.random.normal(streams_of[11], (2, D), jnp.float32), 0.5, 1.5).astype(jnp.bfloat16),
        "text_shifts": bell_draw(streams_of[12], (2, D), 0.3, 2.0),
        "layout_qkv": bell_draw(streams_of[13], (3, DL, DL), DL ** -0.5, 0.4375, ((2, 2),)),
        "layout_qvbias": bell_draw(streams_of[14], (2, DL), 0.5, 3.0, ((1, 2),)),
        "layout_wout": bell_draw(streams_of[15], (DL, DL), (DL // 16) ** -0.5, 1.75, ((0, 2),)),
        "layout_outbias": bell_draw(streams_of[16], (2, DL), 0.3, 2.0),
        "layout_wup": bell_draw(streams_of[17], (DL, FFL), DL ** -0.5, 0.4375, ((1, 2),)),
        "layout_upbias": bell_draw(streams_of[18], (FFL,), 0.5, 3.0, ((0, 2),)),
        "layout_wdown": bell_draw(streams_of[19], (FFL, DL), (FFL // 4) ** -0.5, 0.4375, ((0, 2),)),
        "layout_gains": jnp.clip(1.0 + 0.1 * jax.random.normal(streams_of[20], (2, DL), jnp.float32), 0.5, 1.5).astype(jnp.bfloat16),
        "layout_shifts": bell_draw(streams_of[21], (2, DL), 0.3, 2.0),
        "text_cotan": heavy_noise(streams_of[22], (ROWS, D), 1.0, 6.0, ((0, 32),), (0, 1, 32, 2.75)),
        "layout_cotan": bell_draw(streams_of[23], (ROWS, DL), 1.0, 6.0, ((0, 32),)),
    }


EPSILON = 1e-05
MASKED = -1000000000.0

@jax.custom_vjp
def low(v):
    return lax.optimization_barrier(v.astype(jnp.bfloat16)).astype(jnp.float32)

@jax.custom_vjp
def low_back(v):
    return v

def low_keep(v):
    return (low(v), None)

def low_pass(kept, grad):
    return (grad,)

def back_keep(v):
    return (v, None)

def back_low(kept, grad):
    return (low(grad),)
low.defvjp(low_keep, low_pass)
low_back.defvjp(back_keep, back_low)

def matmul(left, right):
    return jnp.dot(left, right, precision=lax.Precision.HIGHEST, preferred_element_type=jnp.float32)

def layer_norm(values, gain, shift):
    centered = values - lax.optimization_barrier(jnp.mean(values, axis=-1, keepdims=True))
    variance = lax.optimization_barrier(jnp.mean(centered * centered, axis=-1, keepdims=True))
    return centered * lax.rsqrt(variance + EPSILON) * gain + shift

def gelu(values):
    return 0.5 * values * (1.0 + lax.erf(values * 0.7071067811865476))

def headed(values, width):
    return values.reshape(-1, WINDOW, H, width // H)

def project_path(rows, weights):
    queries = low(low_back(matmul(rows, weights[0][0]) + weights[1][0]))
    key_rows = low(low_back(matmul(rows, weights[0][1])))
    value_rows = low(low_back(matmul(rows, weights[0][2]) + weights[1][1]))
    return (queries, key_rows, value_rows)

def finish_path(rows, context, weights):
    attended = low_back(matmul(context, weights[2]) + weights[3][0])
    normed = layer_norm(rows + attended, weights[7][0], weights[8][0])
    hidden = low_back(matmul(low(normed), weights[4]) + weights[5])
    branch = low_back(matmul(low(gelu(hidden)), weights[6]) + weights[3][1])
    return layer_norm(normed + branch, weights[7][1], weights[8][1])

def layer(text_rows, layout_rows, text_weights, layout_weights, usable):
    text_queries, text_keys, text_values = project_path(text_rows, text_weights)
    layout_queries, layout_keys, layout_values = project_path(layout_rows, layout_weights)
    scores = jnp.einsum('cqhd,ckhd->chqk', headed(text_queries, D), headed(text_keys, D), precision=lax.Precision.HIGHEST) * (D // H) ** (-0.5)
    scores = scores + jnp.einsum('cqhd,ckhd->chqk', headed(layout_queries, DL), headed(layout_keys, DL), precision=lax.Precision.HIGHEST) * (DL // H) ** (-0.5)
    scores = low_back(scores)
    scores = jnp.where(usable[:, None, None, :], scores, MASKED)
    probs = low(jax.nn.softmax(scores, axis=-1))
    text_context = jnp.einsum('chqk,ckhd->cqhd', probs, headed(text_values, D), precision=lax.Precision.HIGHEST).reshape(-1, D)
    layout_context = jnp.einsum('chqk,ckhd->cqhd', probs, headed(layout_values, DL), precision=lax.Precision.HIGHEST).reshape(-1, DL)
    text_context = low(low_back(text_context))
    layout_context = low(low_back(layout_context))
    return (finish_path(text_rows, text_context, text_weights), finish_path(layout_rows, layout_context, layout_weights))

def reference(text_input, layout_input, repeated, key_mask, text_qkv, text_qvbias, text_wout, text_outbias, text_wup, text_upbias, text_wdown, text_gains, text_shifts, layout_qkv, layout_qvbias, layout_wout, layout_outbias, layout_wup, layout_upbias, layout_wdown, layout_gains, layout_shifts, text_cotan, layout_cotan):
    text_weights = tuple((weight.astype(jnp.float32) for weight in (text_qkv, text_qvbias, text_wout, text_outbias, text_wup, text_upbias, text_wdown, text_gains, text_shifts)))
    layout_weights = tuple((weight.astype(jnp.float32) for weight in (layout_qkv, layout_qvbias, layout_wout, layout_outbias, layout_wup, layout_upbias, layout_wdown, layout_gains, layout_shifts)))
    group_rows = WINDOWS_DEV * WINDOW
    usable = jnp.logical_and(key_mask == 1, repeated == 0).reshape(N_DP, WINDOWS_DEV, WINDOW)
    text_groups = text_input.astype(jnp.float32).reshape(N_DP, group_rows, D)
    layout_groups = layout_input.astype(jnp.float32).reshape(N_DP, group_rows, DL)
    text_cot_groups = text_cotan.astype(jnp.float32).reshape(N_DP, group_rows, D)
    layout_cot_groups = layout_cotan.astype(jnp.float32).reshape(N_DP, group_rows, DL)

    def group_step(totals, pieces):
        text_rows, layout_rows, usable_rows, text_grad, layout_grad = pieces

        def forward(text_part, layout_part, text_params, layout_params):
            return layer(text_part, layout_part, text_params, layout_params, usable_rows)
        results, pullback = jax.vjp(forward, text_rows, layout_rows, text_weights, layout_weights)
        grads = pullback((text_grad, layout_grad))
        totals = jax.tree.map(jnp.add, totals, (grads[2], grads[3]))
        return (totals, (results[0].astype(jnp.bfloat16), results[1].astype(jnp.bfloat16), grads[0].astype(jnp.bfloat16), grads[1].astype(jnp.bfloat16)))
    zeros = jax.tree.map(jnp.zeros_like, (text_weights, layout_weights))
    totals, produced = lax.scan(group_step, zeros, (text_groups, layout_groups, usable, text_cot_groups, layout_cot_groups))
    text_totals, layout_totals = totals
    return (produced[0].reshape(-1, D), produced[1].reshape(-1, DL), produced[2].reshape(-1, D), produced[3].reshape(-1, DL), text_totals[0], text_totals[1], text_totals[2], text_totals[3], text_totals[4], text_totals[5], text_totals[6], text_totals[7], text_totals[8], layout_totals[0], layout_totals[1], layout_totals[2], layout_totals[3], layout_totals[4], layout_totals[5], layout_totals[6], layout_totals[7], layout_totals[8])
```

```python
import jax
import jax.numpy as jnp
from jax import lax
from jax.sharding import PartitionSpec as P

D = 768
H = 12
DL = 192
WINDOW = 512


EPSILON = 1e-05
MASKED = -1000000000.0


def layer_norm(values, gain, shift):
    centered = values - jnp.mean(values, axis=-1, keepdims=True)
    variance = jnp.mean(centered * centered, axis=-1, keepdims=True)
    return centered * lax.rsqrt(variance + EPSILON) * gain + shift


def gelu(values):
    return 0.5 * values * (1.0 + lax.erf(values * 0.7071067811865476))


def project_path(rows, weight_qkv, biases):
    joined = jnp.einsum("rd,kde->kre", rows, weight_qkv, preferred_element_type=jnp.float32)
    queries = (joined[0] + biases[0]).astype(jnp.bfloat16)
    key_rows = joined[1].astype(jnp.bfloat16)
    value_rows = (joined[2] + biases[1]).astype(jnp.bfloat16)
    return (queries, key_rows, value_rows)


def blocked(values, head_size):
    return values.reshape(-1, WINDOW, values.shape[-1] // head_size, head_size)


def unblocked(values):
    return values.reshape(-1, values.shape[-2] * values.shape[-1])


def coupled_scores(text_queries, text_keys, layout_queries, layout_keys, usable):
    scores = jnp.einsum(
        "qhd,khd->hqk", text_queries, text_keys, preferred_element_type=jnp.float32
    ) * (D // H) ** (-0.5)
    scores = scores + jnp.einsum(
        "qhd,khd->hqk", layout_queries, layout_keys, preferred_element_type=jnp.float32
    ) * (DL // H) ** (-0.5)
    return jnp.where(usable[None, None, :], scores, MASKED)


def attend_window(pieces):
    text_queries, text_keys, text_values, layout_queries, layout_keys, layout_values, usable = (
        pieces
    )
    scores = coupled_scores(text_queries, text_keys, layout_queries, layout_keys, usable)
    peak = jnp.max(scores, axis=-1, keepdims=True)
    powers = jnp.exp(scores - peak)
    total = jnp.sum(powers, axis=-1, keepdims=True)
    probs = (powers / total).astype(jnp.bfloat16)
    text_context = jnp.einsum(
        "hqk,khd->qhd", probs, text_values, preferred_element_type=jnp.float32
    ).astype(jnp.bfloat16)
    layout_context = jnp.einsum(
        "hqk,khd->qhd", probs, layout_values, preferred_element_type=jnp.float32
    ).astype(jnp.bfloat16)
    return (text_context, layout_context, peak + jnp.log(total))


def attend_back(pieces):
    (
        text_queries,
        text_keys,
        text_values,
        layout_queries,
        layout_keys,
        layout_values,
        usable,
        log_totals,
        text_cgrad,
        layout_cgrad,
    ) = pieces
    text_scale = (D // H) ** (-0.5)
    layout_scale = (DL // H) ** (-0.5)
    scores = coupled_scores(text_queries, text_keys, layout_queries, layout_keys, usable)
    probs = jnp.exp(scores - log_totals)
    probs_low = probs.astype(jnp.bfloat16)
    probs_grad = jnp.einsum(
        "qhd,khd->hqk", text_cgrad, text_values, preferred_element_type=jnp.float32
    )
    probs_grad = probs_grad + jnp.einsum(
        "qhd,khd->hqk", layout_cgrad, layout_values, preferred_element_type=jnp.float32
    )
    scores_grad = (
        probs * (probs_grad - jnp.sum(probs_grad * probs, axis=-1, keepdims=True))
    ).astype(jnp.bfloat16)
    text_vgrad = jnp.einsum(
        "hqk,qhd->khd", probs_low, text_cgrad, preferred_element_type=jnp.float32
    ).astype(jnp.bfloat16)
    layout_vgrad = jnp.einsum(
        "hqk,qhd->khd", probs_low, layout_cgrad, preferred_element_type=jnp.float32
    ).astype(jnp.bfloat16)
    text_qgrad = (
        jnp.einsum("hqk,khd->qhd", scores_grad, text_keys, preferred_element_type=jnp.float32)
        * text_scale
    ).astype(jnp.bfloat16)
    text_kgrad = (
        jnp.einsum("hqk,qhd->khd", scores_grad, text_queries, preferred_element_type=jnp.float32)
        * text_scale
    ).astype(jnp.bfloat16)
    layout_qgrad = (
        jnp.einsum("hqk,khd->qhd", scores_grad, layout_keys, preferred_element_type=jnp.float32)
        * layout_scale
    ).astype(jnp.bfloat16)
    layout_kgrad = (
        jnp.einsum("hqk,qhd->khd", scores_grad, layout_queries, preferred_element_type=jnp.float32)
        * layout_scale
    ).astype(jnp.bfloat16)
    return (text_qgrad, text_kgrad, text_vgrad, layout_qgrad, layout_kgrad, layout_vgrad)


def feed_forward(full_rows, w_up, up_bias, w_down):
    hidden = jnp.dot(full_rows, w_up, preferred_element_type=jnp.float32) + up_bias
    active, gelu_back = jax.vjp(gelu, hidden)
    active_low = active.astype(jnp.bfloat16)
    return (active_low, gelu_back, jnp.dot(active_low, w_down, preferred_element_type=jnp.float32))


def feed_back(full_rows, active_low, gelu_back, full_grad, w_up, w_down, down_spec="rf,rd->fd"):
    grad_down = jnp.einsum(down_spec, active_low, full_grad, preferred_element_type=jnp.float32)
    active_grad = jnp.einsum("rd,fd->rf", full_grad, w_down, preferred_element_type=jnp.float32)
    hidden_grad = gelu_back(active_grad)[0].astype(jnp.bfloat16)
    grad_up = jnp.einsum("rd,rf->df", full_rows, hidden_grad, preferred_element_type=jnp.float32)
    grad_bias = jnp.sum(hidden_grad, axis=0, dtype=jnp.float32)
    normed_part = jnp.einsum("rf,df->rd", hidden_grad, w_up, preferred_element_type=jnp.float32)
    return (grad_up, grad_bias, grad_down, normed_part)


def input_back(rows, weight_qkv, query_grad, key_grad, value_grad, stack_axis=0):
    grad_qkv = jnp.stack(
        [
            jnp.einsum("rd,re->de", rows, piece, preferred_element_type=jnp.float32)
            for piece in (query_grad, key_grad, value_grad)
        ],
        axis=stack_axis,
    )
    input_part = jnp.einsum(
        "re,de->rd", query_grad, weight_qkv[0], preferred_element_type=jnp.float32
    )
    input_part = input_part + jnp.einsum(
        "re,de->rd", key_grad, weight_qkv[1], preferred_element_type=jnp.float32
    )
    input_part = input_part + jnp.einsum(
        "re,de->rd", value_grad, weight_qkv[2], preferred_element_type=jnp.float32
    )
    grad_bias = jnp.stack(
        [
            jnp.sum(query_grad, axis=0, dtype=jnp.float32),
            jnp.sum(value_grad, axis=0, dtype=jnp.float32),
        ]
    )
    return (grad_qkv, grad_bias, input_part)


def xor_sum(values, axis, size):
    step = 1
    while step < size:
        values = values + lax.ppermute(
            values, axis, [(i, i ^ step) for i in range(size)]
        )
        step *= 2
    return values


def xor_exchange(values, step, size):
    return lax.ppermute(values, "dp", [(i, i ^ step) for i in range(size)])


def bit_orders(bits, colours):
    if bits <= 1:
        return [list(range(bits))] * colours
    main = list(range(bits - 1))
    orders = []
    for colour in range(colours):
        shift = colour % len(main)
        orders.append(main[shift:] + main[:shift] + [bits - 1])
    return orders


def halve(chunk, order, me, size, bits):
    axes = list(range(bits - 1, -1, -1))
    for bit in order:
        where = axes.index(bit)
        mine = (me >> bit) & 1
        keep = lax.dynamic_index_in_dim(chunk, mine, axis=where, keepdims=False)
        send = lax.dynamic_index_in_dim(chunk, 1 - mine, axis=where, keepdims=False)
        chunk = keep + xor_exchange(send, 1 << bit, size)
        axes.pop(where)
    return chunk


def double(block, order, me, size, bits):
    held = []
    for bit in reversed(order):
        other = xor_exchange(block, 1 << bit, size)
        mine = (me >> bit) & 1
        block = jnp.where(mine == 0, jnp.stack([block, other]), jnp.stack([other, block]))
        held.insert(0, bit)
    canonical = list(range(bits - 1, -1, -1))
    block = jnp.transpose(block, [held.index(bit) for bit in canonical] + [len(held)])
    return block.reshape(-1)


def dp_reduce(scattered, replicated, size, colours=3):
    bits = size.bit_length() - 1
    me = lax.axis_index("dp")
    rows = [piece.reshape(size, -1) for piece in scattered]
    widths = [row.shape[1] for row in rows]
    flat = jnp.concatenate([piece.reshape(-1) for piece in replicated])
    pad = (-flat.shape[0]) % size
    flat = jnp.pad(flat, (0, pad))
    rep_width = flat.shape[0] // size
    joined = jnp.concatenate(rows + [flat.reshape(size, rep_width)], axis=1)
    total = joined.shape[1]
    bounds = [total * colour // colours for colour in range(colours + 1)]
    bounds = [bound // 128 * 128 for bound in bounds[:-1]] + [total]
    orders = bit_orders(bits, colours)
    shaped = joined.reshape((2,) * bits + (total,))
    reduced = jnp.concatenate(
        [
            halve(shaped[..., bounds[c] : bounds[c + 1]], orders[c], me, size, bits)
            for c in range(colours)
        ]
    )
    scattered_out = []
    offset = 0
    for piece, width in zip(scattered, widths):
        share = reduced[offset : offset + width]
        scattered_out.append(share.reshape((piece.shape[0] // size,) + piece.shape[1:]))
        offset += width
    rep_block = reduced[offset : offset + rep_width]
    full = double(rep_block, orders[0], me, size, bits)[: flat.shape[0] - pad]
    replicated_out = []
    offset = 0
    for piece in replicated:
        replicated_out.append(full[offset : offset + piece.size].reshape(piece.shape))
        offset += piece.size
    return scattered_out, replicated_out


def body(
    text_input,
    layout_input,
    repeated,
    key_mask,
    text_qkv,
    text_qvbias,
    text_wout,
    text_outbias,
    text_wup,
    text_upbias,
    text_wdown,
    text_gains,
    text_shifts,
    layout_qkv,
    layout_qvbias,
    layout_wout,
    layout_outbias,
    layout_wup,
    layout_upbias,
    layout_wdown,
    layout_gains,
    layout_shifts,
    text_cotan,
    layout_cotan,
):
    text_head = D // H
    layout_head = DL // H
    usable_group = jnp.logical_and(key_mask == 1, repeated == 0).reshape(-1, WINDOW)
    text_rows, layout_rows = (
        lax.all_gather(text_input, "mp", axis=0, tiled=True),
        lax.all_gather(layout_input, "mp", axis=0, tiled=True),
    )
    text_queries, text_keys, text_values = project_path(text_rows, text_qkv, text_qvbias)
    layout_queries, layout_keys, layout_values = project_path(
        layout_rows, layout_qkv, layout_qvbias
    )
    blocks = (
        blocked(text_queries, text_head),
        blocked(text_keys, text_head),
        blocked(text_values, text_head),
        blocked(layout_queries, layout_head),
        blocked(layout_keys, layout_head),
        blocked(layout_values, layout_head),
        usable_group,
    )
    text_context, layout_context, log_totals = lax.map(attend_window, blocks)
    text_context = unblocked(text_context)
    layout_context = unblocked(layout_context)
    text_mixed_part = jnp.dot(text_context, text_wout, preferred_element_type=jnp.float32)
    layout_mixed_part = jnp.dot(layout_context, layout_wout, preferred_element_type=jnp.float32)
    text_mixed, layout_mixed = (
        lax.psum_scatter(
            text_mixed_part.astype(jnp.bfloat16), "mp", scatter_dimension=0, tiled=True
        ).astype(jnp.float32),
        lax.psum_scatter(
            layout_mixed_part.astype(jnp.bfloat16), "mp", scatter_dimension=0, tiled=True
        ).astype(jnp.float32),
    )
    text_gain = text_gains.astype(jnp.float32)
    text_shift = text_shifts.astype(jnp.float32)
    layout_gain = layout_gains.astype(jnp.float32)
    layout_shift = layout_shifts.astype(jnp.float32)
    text_normed, text_first_back = jax.vjp(
        layer_norm,
        text_input.astype(jnp.float32) + text_mixed + text_outbias[0],
        text_gain[0],
        text_shift[0],
    )
    layout_normed, layout_first_back = jax.vjp(
        layer_norm,
        layout_input.astype(jnp.float32) + layout_mixed + layout_outbias[0],
        layout_gain[0],
        layout_shift[0],
    )
    text_full, layout_full = (
        lax.all_gather(text_normed.astype(jnp.bfloat16), "mp", axis=0, tiled=True),
        lax.all_gather(layout_normed.astype(jnp.bfloat16), "mp", axis=0, tiled=True),
    )
    text_active, text_gelu_back, text_branch_part = feed_forward(
        text_full, text_wup, text_upbias, text_wdown
    )
    layout_active, layout_gelu_back, layout_branch_part = feed_forward(
        layout_full, layout_wup, layout_upbias, layout_wdown
    )
    text_branch, layout_branch = (
        lax.psum_scatter(
            text_branch_part.astype(jnp.bfloat16), "mp", scatter_dimension=0, tiled=True
        ).astype(jnp.float32),
        lax.psum_scatter(
            layout_branch_part.astype(jnp.bfloat16), "mp", scatter_dimension=0, tiled=True
        ).astype(jnp.float32),
    )
    text_final, text_final_back = jax.vjp(
        layer_norm, text_normed + text_branch + text_outbias[1], text_gain[1], text_shift[1]
    )
    layout_final, layout_final_back = jax.vjp(
        layer_norm,
        layout_normed + layout_branch + layout_outbias[1],
        layout_gain[1],
        layout_shift[1],
    )
    text_sum_grad, text_gain_second, text_shift_second = text_final_back(
        text_cotan.astype(jnp.float32)
    )
    layout_sum_grad, layout_gain_second, layout_shift_second = layout_final_back(
        layout_cotan.astype(jnp.float32)
    )
    text_branch_grad = text_sum_grad.astype(jnp.bfloat16)
    layout_branch_grad = layout_sum_grad.astype(jnp.bfloat16)
    text_full_grad, layout_full_grad = (
        lax.all_gather(text_branch_grad, "mp", axis=0, tiled=True),
        lax.all_gather(layout_branch_grad, "mp", axis=0, tiled=True),
    )
    text_wup_grad, text_upbias_grad, text_wdown_grad_t, text_normed_part = feed_back(
        text_full, text_active, text_gelu_back, text_full_grad, text_wup, text_wdown, "rf,rd->df"
    )
    layout_wup_grad, layout_upbias_grad, layout_wdown_grad, layout_normed_part = feed_back(
        layout_full, layout_active, layout_gelu_back, layout_full_grad, layout_wup, layout_wdown
    )
    text_normed_grad, layout_normed_grad = (
        lax.psum_scatter(
            text_normed_part.astype(jnp.bfloat16), "mp", scatter_dimension=0, tiled=True
        ).astype(jnp.float32),
        lax.psum_scatter(
            layout_normed_part.astype(jnp.bfloat16), "mp", scatter_dimension=0, tiled=True
        ).astype(jnp.float32),
    )
    text_mixed_grad, text_gain_first, text_shift_first = text_first_back(
        text_normed_grad + text_sum_grad
    )
    layout_mixed_grad, layout_gain_first, layout_shift_first = layout_first_back(
        layout_normed_grad + layout_sum_grad
    )
    text_mixed_low = text_mixed_grad.astype(jnp.bfloat16)
    layout_mixed_low = layout_mixed_grad.astype(jnp.bfloat16)
    text_wide_grad, layout_wide_grad = (
        lax.all_gather(text_mixed_low, "mp", axis=0, tiled=True),
        lax.all_gather(layout_mixed_low, "mp", axis=0, tiled=True),
    )
    text_wout_grad_t = jnp.einsum(
        "re,rd->de", text_context, text_wide_grad, preferred_element_type=jnp.float32
    )
    layout_wout_grad = jnp.einsum(
        "re,rd->ed", layout_context, layout_wide_grad, preferred_element_type=jnp.float32
    )
    text_context_grad = jnp.einsum(
        "rd,ed->re", text_wide_grad, text_wout, preferred_element_type=jnp.float32
    ).astype(jnp.bfloat16)
    layout_context_grad = jnp.einsum(
        "rd,ed->re", layout_wide_grad, layout_wout, preferred_element_type=jnp.float32
    ).astype(jnp.bfloat16)
    back_blocks = blocks + (
        log_totals,
        blocked(text_context_grad, text_head),
        blocked(layout_context_grad, layout_head),
    )
    text_qgrad, text_kgrad, text_vgrad, layout_qgrad, layout_kgrad, layout_vgrad = lax.map(
        attend_back, back_blocks
    )
    text_qkv_grad_t, text_qvbias_grad, text_input_part = input_back(
        text_rows,
        text_qkv,
        unblocked(text_qgrad),
        unblocked(text_kgrad),
        unblocked(text_vgrad),
        stack_axis=1,
    )
    layout_qkv_grad, layout_qvbias_grad, layout_input_part = input_back(
        layout_rows,
        layout_qkv,
        unblocked(layout_qgrad),
        unblocked(layout_kgrad),
        unblocked(layout_vgrad),
    )
    text_input_sum, layout_input_sum = (
        lax.psum_scatter(
            text_input_part.astype(jnp.bfloat16), "mp", scatter_dimension=0, tiled=True
        ).astype(jnp.float32),
        lax.psum_scatter(
            layout_input_part.astype(jnp.bfloat16), "mp", scatter_dimension=0, tiled=True
        ).astype(jnp.float32),
    )
    text_dinput = (text_mixed_grad + text_input_sum).astype(jnp.bfloat16)
    layout_dinput = (layout_mixed_grad + layout_input_sum).astype(jnp.bfloat16)
    n_dp = lax.axis_size("dp")
    n_mp = lax.axis_size("mp")
    small = jnp.concatenate(
        [
            part.reshape(-1)
            for part in (
                jnp.stack(
                    [
                        jnp.sum(text_mixed_low, axis=0, dtype=jnp.float32),
                        jnp.sum(text_branch_grad, axis=0, dtype=jnp.float32),
                    ]
                ),
                jnp.stack([text_gain_first, text_gain_second]),
                jnp.stack([text_shift_first, text_shift_second]),
                jnp.stack(
                    [
                        jnp.sum(layout_mixed_low, axis=0, dtype=jnp.float32),
                        jnp.sum(layout_branch_grad, axis=0, dtype=jnp.float32),
                    ]
                ),
                jnp.stack([layout_gain_first, layout_gain_second]),
                jnp.stack([layout_shift_first, layout_shift_second]),
            )
        ]
    )
    small = xor_sum(small, "mp", n_mp)
    scattered = (
        text_qkv_grad_t,
        text_wout_grad_t,
        text_wup_grad,
        text_wdown_grad_t,
    )
    replicated = (
        text_qvbias_grad,
        text_upbias_grad,
        layout_qkv_grad,
        layout_qvbias_grad,
        layout_wout_grad,
        layout_wup_grad,
        layout_upbias_grad,
        layout_wdown_grad,
        small,
    )
    scattered_out, replicated_out = dp_reduce(scattered, replicated, n_dp)
    qkv_share = jnp.transpose(scattered_out[0], (1, 0, 2))
    wout_share = scattered_out[1].T
    wup_share = scattered_out[2]
    wdown_share = scattered_out[3].T
    summed = replicated_out[:8]
    small_sum = replicated_out[8]
    sizes = (2 * D, 2 * D, 2 * D, 2 * DL, 2 * DL, 2 * DL)
    shared = []
    offset = 0
    for size in sizes:
        shared.append(small_sum[offset : offset + size].reshape(2, -1))
        offset += size
    return (
        text_final.astype(jnp.bfloat16),
        layout_final.astype(jnp.bfloat16),
        text_dinput,
        layout_dinput,
        qkv_share,
        summed[0],
        wout_share,
        shared[0],
        wup_share,
        summed[1],
        wdown_share,
        shared[1],
        shared[2],
        summed[2],
        summed[3],
        summed[4],
        shared[3],
        summed[5],
        summed[6],
        summed[7],
        shared[4],
        shared[5],
    )


def solution(mesh):
    in_specs = (
        P(("dp", "mp"), None),
        P(("dp", "mp"), None),
        P("dp"),
        P("dp"),
        P(None, None, "mp"),
        P(None, "mp"),
        P("mp", None),
        P(),
        P(None, "mp"),
        P("mp"),
        P("mp", None),
        P(),
        P(),
        P(None, None, "mp"),
        P(None, "mp"),
        P("mp", None),
        P(),
        P(None, "mp"),
        P("mp"),
        P("mp", None),
        P(),
        P(),
        P(("dp", "mp"), None),
        P(("dp", "mp"), None),
    )
    out_specs = (
        P(("dp", "mp"), None),
        P(("dp", "mp"), None),
        P(("dp", "mp"), None),
        P(("dp", "mp"), None),
        P(None, "dp", "mp"),
        P(None, "mp"),
        P("mp", "dp"),
        P(),
        P("dp", "mp"),
        P("mp"),
        P("mp", "dp"),
        P(),
        P(),
        P(None, None, "mp"),
        P(None, "mp"),
        P("mp", None),
        P(),
        P(None, "mp"),
        P("mp"),
        P("mp", None),
        P(),
        P(),
    )
    return jax.shard_map(body, mesh=mesh, in_specs=in_specs, out_specs=out_specs, check_vma=False)
```

```python
import jax
import jax.numpy as jnp
from jax import lax
from jax.sharding import PartitionSpec as P

D = 768
H = 12
DL = 192
WINDOW = 512


EPSILON = 1e-05
MASKED = -1000000000.0


def layer_norm(values, gain, shift):
    centered = values - jnp.mean(values, axis=-1, keepdims=True)
    variance = jnp.mean(centered * centered, axis=-1, keepdims=True)
    return centered * lax.rsqrt(variance + EPSILON) * gain + shift


def gelu(values):
    return 0.5 * values * (1.0 + lax.erf(values * 0.7071067811865476))


def project_path(rows, weight_qkv, biases):
    joined = jnp.einsum("rd,kde->kre", rows, weight_qkv, preferred_element_type=jnp.float32)
    queries = (joined[0] + biases[0]).astype(jnp.bfloat16)
    key_rows = joined[1].astype(jnp.bfloat16)
    value_rows = (joined[2] + biases[1]).astype(jnp.bfloat16)
    return (queries, key_rows, value_rows)


def blocked(values, head_size):
    return values.reshape(-1, WINDOW, values.shape[-1] // head_size, head_size)


def unblocked(values):
    return values.reshape(-1, values.shape[-2] * values.shape[-1])


def coupled_scores(text_queries, text_keys, layout_queries, layout_keys, usable):
    scores = jnp.einsum(
        "qhd,khd->hqk", text_queries, text_keys, preferred_element_type=jnp.float32
    ) * (D // H) ** (-0.5)
    scores = scores + jnp.einsum(
        "qhd,khd->hqk", layout_queries, layout_keys, preferred_element_type=jnp.float32
    ) * (DL // H) ** (-0.5)
    return jnp.where(usable[None, None, :], scores, MASKED)


def attend_window(pieces):
    text_queries, text_keys, text_values, layout_queries, layout_keys, layout_values, usable = (
        pieces
    )
    scores = coupled_scores(text_queries, text_keys, layout_queries, layout_keys, usable)
    peak = jnp.max(scores, axis=-1, keepdims=True)
    powers = jnp.exp(scores - peak)
    total = jnp.sum(powers, axis=-1, keepdims=True)
    probs = (powers / total).astype(jnp.bfloat16)
    text_context = jnp.einsum(
        "hqk,khd->qhd", probs, text_values, preferred_element_type=jnp.float32
    ).astype(jnp.bfloat16)
    layout_context = jnp.einsum(
        "hqk,khd->qhd", probs, layout_values, preferred_element_type=jnp.float32
    ).astype(jnp.bfloat16)
    return (text_context, layout_context, peak + jnp.log(total))


def attend_back(pieces):
    (
        text_queries,
        text_keys,
        text_values,
        layout_queries,
        layout_keys,
        layout_values,
        usable,
        log_totals,
        text_cgrad,
        layout_cgrad,
    ) = pieces
    text_scale = (D // H) ** (-0.5)
    layout_scale = (DL // H) ** (-0.5)
    scores = coupled_scores(text_queries, text_keys, layout_queries, layout_keys, usable)
    probs = jnp.exp(scores - log_totals)
    probs_low = probs.astype(jnp.bfloat16)
    probs_grad = jnp.einsum(
        "qhd,khd->hqk", text_cgrad, text_values, preferred_element_type=jnp.float32
    )
    probs_grad = probs_grad + jnp.einsum(
        "qhd,khd->hqk", layout_cgrad, layout_values, preferred_element_type=jnp.float32
    )
    scores_grad = (
        probs * (probs_grad - jnp.sum(probs_grad * probs, axis=-1, keepdims=True))
    ).astype(jnp.bfloat16)
    text_vgrad = jnp.einsum(
        "hqk,qhd->khd", probs_low, text_cgrad, preferred_element_type=jnp.float32
    ).astype(jnp.bfloat16)
    layout_vgrad = jnp.einsum(
        "hqk,qhd->khd", probs_low, layout_cgrad, preferred_element_type=jnp.float32
    ).astype(jnp.bfloat16)
    text_qgrad = (
        jnp.einsum("hqk,khd->qhd", scores_grad, text_keys, preferred_element_type=jnp.float32)
        * text_scale
    ).astype(jnp.bfloat16)
    text_kgrad = (
        jnp.einsum("hqk,qhd->khd", scores_grad, text_queries, preferred_element_type=jnp.float32)
        * text_scale
    ).astype(jnp.bfloat16)
    layout_qgrad = (
        jnp.einsum("hqk,khd->qhd", scores_grad, layout_keys, preferred_element_type=jnp.float32)
        * layout_scale
    ).astype(jnp.bfloat16)
    layout_kgrad = (
        jnp.einsum("hqk,qhd->khd", scores_grad, layout_queries, preferred_element_type=jnp.float32)
        * layout_scale
    ).astype(jnp.bfloat16)
    return (text_qgrad, text_kgrad, text_vgrad, layout_qgrad, layout_kgrad, layout_vgrad)


def feed_forward(full_rows, w_up, up_bias, w_down):
    hidden = jnp.dot(full_rows, w_up, preferred_element_type=jnp.float32) + up_bias
    active, gelu_back = jax.vjp(gelu, hidden)
    active_low = active.astype(jnp.bfloat16)
    return (active_low, gelu_back, jnp.dot(active_low, w_down, preferred_element_type=jnp.float32))


def feed_back(full_rows, active_low, gelu_back, full_grad, w_up, w_down, down_spec="rf,rd->fd"):
    grad_down = jnp.einsum(down_spec, active_low, full_grad, preferred_element_type=jnp.float32)
    active_grad = jnp.einsum("rd,fd->rf", full_grad, w_down, preferred_element_type=jnp.float32)
    hidden_grad = gelu_back(active_grad)[0].astype(jnp.bfloat16)
    grad_up = jnp.einsum("rd,rf->df", full_rows, hidden_grad, preferred_element_type=jnp.float32)
    grad_bias = jnp.sum(hidden_grad, axis=0, dtype=jnp.float32)
    normed_part = jnp.einsum("rf,df->rd", hidden_grad, w_up, preferred_element_type=jnp.float32)
    return (grad_up, grad_bias, grad_down, normed_part)


def input_back(rows, weight_qkv, query_grad, key_grad, value_grad, stack_axis=0):
    grad_qkv = jnp.stack(
        [
            jnp.einsum("rd,re->de", rows, piece, preferred_element_type=jnp.float32)
            for piece in (query_grad, key_grad, value_grad)
        ],
        axis=stack_axis,
    )
    input_part = jnp.einsum(
        "re,de->rd", query_grad, weight_qkv[0], preferred_element_type=jnp.float32
    )
    input_part = input_part + jnp.einsum(
        "re,de->rd", key_grad, weight_qkv[1], preferred_element_type=jnp.float32
    )
    input_part = input_part + jnp.einsum(
        "re,de->rd", value_grad, weight_qkv[2], preferred_element_type=jnp.float32
    )
    grad_bias = jnp.stack(
        [
            jnp.sum(query_grad, axis=0, dtype=jnp.float32),
            jnp.sum(value_grad, axis=0, dtype=jnp.float32),
        ]
    )
    return (grad_qkv, grad_bias, input_part)


def xor_sum(values, axis, size):
    step = 1
    while step < size:
        values = values + lax.ppermute(
            values, axis, [(i, i ^ step) for i in range(size)]
        )
        step *= 2
    return values


def xor_exchange(values, step, size):
    return lax.ppermute(values, "dp", [(i, i ^ step) for i in range(size)])


def bit_orders(bits, colours):
    if bits <= 1:
        return [list(range(bits))] * colours
    main = list(range(bits - 1))
    orders = []
    for colour in range(colours):
        shift = colour % len(main)
        orders.append(main[shift:] + main[:shift] + [bits - 1])
    return orders


def halve(chunk, order, me, size, bits, wire):
    axes = list(range(bits - 1, -1, -1))
    for bit in order:
        where = axes.index(bit)
        mine = (me >> bit) & 1
        keep = lax.dynamic_index_in_dim(chunk, mine, axis=where, keepdims=False)
        send = lax.dynamic_index_in_dim(chunk, 1 - mine, axis=where, keepdims=False)
        chunk = keep + xor_exchange(send.astype(wire), 1 << bit, size).astype(chunk.dtype)
        axes.pop(where)
    return chunk


def double(block, order, me, size, bits):
    held = []
    for bit in reversed(order):
        other = xor_exchange(block, 1 << bit, size)
        mine = (me >> bit) & 1
        block = jnp.where(mine == 0, jnp.stack([block, other]), jnp.stack([other, block]))
        held.insert(0, bit)
    canonical = list(range(bits - 1, -1, -1))
    block = jnp.transpose(block, [held.index(bit) for bit in canonical] + [len(held)])
    return block.reshape(-1)


def dp_reduce(scattered, colours_of, replicated, size, wire):
    bits = size.bit_length() - 1
    me = lax.axis_index("dp")
    orders = bit_orders(bits, 3)
    scattered_out = []
    for piece, colour in zip(scattered, colours_of):
        shaped = piece.reshape((2,) * bits + (piece.shape[0] // size,) + piece.shape[1:])
        scattered_out.append(halve(shaped, orders[colour], me, size, bits, wire))
    flat = jnp.concatenate([piece.reshape(-1) for piece in replicated])
    pad = (-flat.shape[0]) % size
    flat = jnp.pad(flat, (0, pad))
    shaped = flat.reshape((2,) * bits + (flat.shape[0] // size,))
    block = halve(shaped, orders[0], me, size, bits, wire)
    full = double(block, orders[0], me, size, bits)[: flat.shape[0] - pad]
    replicated_out = []
    offset = 0
    for piece in replicated:
        replicated_out.append(full[offset : offset + piece.size].reshape(piece.shape))
        offset += piece.size
    return scattered_out, replicated_out

def body(
    text_input,
    layout_input,
    repeated,
    key_mask,
    text_qkv,
    text_qvbias,
    text_wout,
    text_outbias,
    text_wup,
    text_upbias,
    text_wdown,
    text_gains,
    text_shifts,
    layout_qkv,
    layout_qvbias,
    layout_wout,
    layout_outbias,
    layout_wup,
    layout_upbias,
    layout_wdown,
    layout_gains,
    layout_shifts,
    text_cotan,
    layout_cotan,
):
    text_head = D // H
    layout_head = DL // H
    usable_group = jnp.logical_and(key_mask == 1, repeated == 0).reshape(-1, WINDOW)
    text_rows, layout_rows = (
        lax.all_gather(text_input, "mp", axis=0, tiled=True),
        lax.all_gather(layout_input, "mp", axis=0, tiled=True),
    )
    text_queries, text_keys, text_values = project_path(text_rows, text_qkv, text_qvbias)
    layout_queries, layout_keys, layout_values = project_path(
        layout_rows, layout_qkv, layout_qvbias
    )
    blocks = (
        blocked(text_queries, text_head),
        blocked(text_keys, text_head),
        blocked(text_values, text_head),
        blocked(layout_queries, layout_head),
        blocked(layout_keys, layout_head),
        blocked(layout_values, layout_head),
        usable_group,
    )
    text_context, layout_context, log_totals = lax.map(attend_window, blocks)
    text_context = unblocked(text_context)
    layout_context = unblocked(layout_context)
    text_mixed_part = jnp.dot(text_context, text_wout, preferred_element_type=jnp.float32)
    layout_mixed_part = jnp.dot(layout_context, layout_wout, preferred_element_type=jnp.float32)
    text_mixed, layout_mixed = (
        lax.psum_scatter(
            text_mixed_part.astype(jnp.bfloat16), "mp", scatter_dimension=0, tiled=True
        ).astype(jnp.float32),
        lax.psum_scatter(
            layout_mixed_part.astype(jnp.bfloat16), "mp", scatter_dimension=0, tiled=True
        ).astype(jnp.float32),
    )
    text_gain = text_gains.astype(jnp.float32)
    text_shift = text_shifts.astype(jnp.float32)
    layout_gain = layout_gains.astype(jnp.float32)
    layout_shift = layout_shifts.astype(jnp.float32)
    text_normed, text_first_back = jax.vjp(
        layer_norm,
        text_input.astype(jnp.float32) + text_mixed + text_outbias[0],
        text_gain[0],
        text_shift[0],
    )
    layout_normed, layout_first_back = jax.vjp(
        layer_norm,
        layout_input.astype(jnp.float32) + layout_mixed + layout_outbias[0],
        layout_gain[0],
        layout_shift[0],
    )
    text_full, layout_full = (
        lax.all_gather(text_normed.astype(jnp.bfloat16), "mp", axis=0, tiled=True),
        lax.all_gather(layout_normed.astype(jnp.bfloat16), "mp", axis=0, tiled=True),
    )
    text_active, text_gelu_back, text_branch_part = feed_forward(
        text_full, text_wup, text_upbias, text_wdown
    )
    layout_active, layout_gelu_back, layout_branch_part = feed_forward(
        layout_full, layout_wup, layout_upbias, layout_wdown
    )
    text_branch, layout_branch = (
        lax.psum_scatter(
            text_branch_part.astype(jnp.bfloat16), "mp", scatter_dimension=0, tiled=True
        ).astype(jnp.float32),
        lax.psum_scatter(
            layout_branch_part.astype(jnp.bfloat16), "mp", scatter_dimension=0, tiled=True
        ).astype(jnp.float32),
    )
    text_final, text_final_back = jax.vjp(
        layer_norm, text_normed + text_branch + text_outbias[1], text_gain[1], text_shift[1]
    )
    layout_final, layout_final_back = jax.vjp(
        layer_norm,
        layout_normed + layout_branch + layout_outbias[1],
        layout_gain[1],
        layout_shift[1],
    )
    text_sum_grad, text_gain_second, text_shift_second = text_final_back(
        text_cotan.astype(jnp.float32)
    )
    layout_sum_grad, layout_gain_second, layout_shift_second = layout_final_back(
        layout_cotan.astype(jnp.float32)
    )
    text_branch_grad = text_sum_grad.astype(jnp.bfloat16)
    layout_branch_grad = layout_sum_grad.astype(jnp.bfloat16)
    text_full_grad, layout_full_grad = (
        lax.all_gather(text_branch_grad, "mp", axis=0, tiled=True),
        lax.all_gather(layout_branch_grad, "mp", axis=0, tiled=True),
    )
    text_wup_grad, text_upbias_grad, text_wdown_grad_t, text_normed_part = feed_back(
        text_full, text_active, text_gelu_back, text_full_grad, text_wup, text_wdown, "rf,rd->df"
    )
    layout_wup_grad, layout_upbias_grad, layout_wdown_grad, layout_normed_part = feed_back(
        layout_full, layout_active, layout_gelu_back, layout_full_grad, layout_wup, layout_wdown
    )
    text_normed_grad, layout_normed_grad = (
        lax.psum_scatter(
            text_normed_part.astype(jnp.bfloat16), "mp", scatter_dimension=0, tiled=True
        ).astype(jnp.float32),
        lax.psum_scatter(
            layout_normed_part.astype(jnp.bfloat16), "mp", scatter_dimension=0, tiled=True
        ).astype(jnp.float32),
    )
    text_mixed_grad, text_gain_first, text_shift_first = text_first_back(
        text_normed_grad + text_sum_grad
    )
    layout_mixed_grad, layout_gain_first, layout_shift_first = layout_first_back(
        layout_normed_grad + layout_sum_grad
    )
    text_mixed_low = text_mixed_grad.astype(jnp.bfloat16)
    layout_mixed_low = layout_mixed_grad.astype(jnp.bfloat16)
    text_wide_grad, layout_wide_grad = (
        lax.all_gather(text_mixed_low, "mp", axis=0, tiled=True),
        lax.all_gather(layout_mixed_low, "mp", axis=0, tiled=True),
    )
    text_wout_grad_t = jnp.einsum(
        "re,rd->de", text_context, text_wide_grad, preferred_element_type=jnp.float32
    )
    layout_wout_grad = jnp.einsum(
        "re,rd->ed", layout_context, layout_wide_grad, preferred_element_type=jnp.float32
    )
    text_context_grad = jnp.einsum(
        "rd,ed->re", text_wide_grad, text_wout, preferred_element_type=jnp.float32
    ).astype(jnp.bfloat16)
    layout_context_grad = jnp.einsum(
        "rd,ed->re", layout_wide_grad, layout_wout, preferred_element_type=jnp.float32
    ).astype(jnp.bfloat16)
    back_blocks = blocks + (
        log_totals,
        blocked(text_context_grad, text_head),
        blocked(layout_context_grad, layout_head),
    )
    text_qgrad, text_kgrad, text_vgrad, layout_qgrad, layout_kgrad, layout_vgrad = lax.map(
        attend_back, back_blocks
    )
    text_qkv_grad_t, text_qvbias_grad, text_input_part = input_back(
        text_rows,
        text_qkv,
        unblocked(text_qgrad),
        unblocked(text_kgrad),
        unblocked(text_vgrad),
        stack_axis=1,
    )
    layout_qkv_grad, layout_qvbias_grad, layout_input_part = input_back(
        layout_rows,
        layout_qkv,
        unblocked(layout_qgrad),
        unblocked(layout_kgrad),
        unblocked(layout_vgrad),
    )
    text_input_sum, layout_input_sum = (
        lax.psum_scatter(
            text_input_part.astype(jnp.bfloat16), "mp", scatter_dimension=0, tiled=True
        ).astype(jnp.float32),
        lax.psum_scatter(
            layout_input_part.astype(jnp.bfloat16), "mp", scatter_dimension=0, tiled=True
        ).astype(jnp.float32),
    )
    text_dinput = (text_mixed_grad + text_input_sum).astype(jnp.bfloat16)
    layout_dinput = (layout_mixed_grad + layout_input_sum).astype(jnp.bfloat16)
    n_dp = lax.axis_size("dp")
    n_mp = lax.axis_size("mp")
    small = jnp.concatenate(
        [
            part.reshape(-1)
            for part in (
                jnp.stack(
                    [
                        jnp.sum(text_mixed_low, axis=0, dtype=jnp.float32),
                        jnp.sum(text_branch_grad, axis=0, dtype=jnp.float32),
                    ]
                ),
                jnp.stack([text_gain_first, text_gain_second]),
                jnp.stack([text_shift_first, text_shift_second]),
                jnp.stack(
                    [
                        jnp.sum(layout_mixed_low, axis=0, dtype=jnp.float32),
                        jnp.sum(layout_branch_grad, axis=0, dtype=jnp.float32),
                    ]
                ),
                jnp.stack([layout_gain_first, layout_gain_second]),
                jnp.stack([layout_shift_first, layout_shift_second]),
            )
        ]
    )
    small = xor_sum(small, "mp", n_mp)
    scattered = (
        text_qkv_grad_t,
        text_wout_grad_t,
        text_wup_grad,
        text_wdown_grad_t,
    )
    replicated = (
        text_qvbias_grad,
        text_upbias_grad,
        layout_qkv_grad,
        layout_qvbias_grad,
        layout_wout_grad,
        layout_wup_grad,
        layout_upbias_grad,
        layout_wdown_grad,
        small,
    )
    scattered, replicated = lax.optimization_barrier((scattered, replicated))
    scattered_out, replicated_out = dp_reduce(
        scattered, (2, 2, 0, 1), replicated, n_dp, jnp.bfloat16
    )
    qkv_share = jnp.transpose(scattered_out[0], (1, 0, 2))
    wout_share = scattered_out[1].T
    wup_share = scattered_out[2]
    wdown_share = scattered_out[3].T
    summed = replicated_out[:8]
    small_sum = replicated_out[8]
    sizes = (2 * D, 2 * D, 2 * D, 2 * DL, 2 * DL, 2 * DL)
    shared = []
    offset = 0
    for size in sizes:
        shared.append(small_sum[offset : offset + size].reshape(2, -1))
        offset += size
    return (
        text_final.astype(jnp.bfloat16),
        layout_final.astype(jnp.bfloat16),
        text_dinput,
        layout_dinput,
        qkv_share,
        summed[0],
        wout_share,
        shared[0],
        wup_share,
        summed[1],
        wdown_share,
        shared[1],
        shared[2],
        summed[2],
        summed[3],
        summed[4],
        shared[3],
        summed[5],
        summed[6],
        summed[7],
        shared[4],
        shared[5],
    )


def solution(mesh):
    in_specs = (
        P(("dp", "mp"), None),
        P(("dp", "mp"), None),
        P("dp"),
        P("dp"),
        P(None, None, "mp"),
        P(None, "mp"),
        P("mp", None),
        P(),
        P(None, "mp"),
        P("mp"),
        P("mp", None),
        P(),
        P(),
        P(None, None, "mp"),
        P(None, "mp"),
        P("mp", None),
        P(),
        P(None, "mp"),
        P("mp"),
        P("mp", None),
        P(),
        P(),
        P(("dp", "mp"), None),
        P(("dp", "mp"), None),
    )
    out_specs = (
        P(("dp", "mp"), None),
        P(("dp", "mp"), None),
        P(("dp", "mp"), None),
        P(("dp", "mp"), None),
        P(None, "dp", "mp"),
        P(None, "mp"),
        P("mp", "dp"),
        P(),
        P("dp", "mp"),
        P("mp"),
        P("mp", "dp"),
        P(),
        P(),
        P(None, None, "mp"),
        P(None, "mp"),
        P("mp", None),
        P(),
        P(None, "mp"),
        P("mp"),
        P("mp", None),
        P(),
        P(),
    )
    return jax.shard_map(body, mesh=mesh, in_specs=in_specs, out_specs=out_specs, check_vma=False)
```

```python
import jax
import jax.numpy as jnp
from jax import lax
from jax.sharding import PartitionSpec as P

D = 768
H = 12
DL = 192
WINDOW = 512


EPSILON = 1e-05
MASKED = -1000000000.0


def layer_norm(values, gain, shift):
    centered = values - jnp.mean(values, axis=-1, keepdims=True)
    variance = jnp.mean(centered * centered, axis=-1, keepdims=True)
    return centered * lax.rsqrt(variance + EPSILON) * gain + shift


def gelu(values):
    return 0.5 * values * (1.0 + lax.erf(values * 0.7071067811865476))


def project_path(rows, weight_qkv, biases):
    joined = jnp.einsum("rd,kde->kre", rows, weight_qkv, preferred_element_type=jnp.float32)
    queries = (joined[0] + biases[0]).astype(jnp.bfloat16)
    key_rows = joined[1].astype(jnp.bfloat16)
    value_rows = (joined[2] + biases[1]).astype(jnp.bfloat16)
    return (queries, key_rows, value_rows)


def blocked(values, head_size):
    return values.reshape(-1, WINDOW, values.shape[-1] // head_size, head_size)


def unblocked(values):
    return values.reshape(-1, values.shape[-2] * values.shape[-1])


def coupled_scores(text_queries, text_keys, layout_queries, layout_keys, usable):
    scores = jnp.einsum(
        "qhd,khd->hqk", text_queries, text_keys, preferred_element_type=jnp.float32
    ) * (D // H) ** (-0.5)
    scores = scores + jnp.einsum(
        "qhd,khd->hqk", layout_queries, layout_keys, preferred_element_type=jnp.float32
    ) * (DL // H) ** (-0.5)
    return jnp.where(usable[None, None, :], scores, MASKED)


def attend_window(pieces):
    text_queries, text_keys, text_values, layout_queries, layout_keys, layout_values, usable = (
        pieces
    )
    scores = coupled_scores(text_queries, text_keys, layout_queries, layout_keys, usable)
    peak = jnp.max(scores, axis=-1, keepdims=True)
    powers = jnp.exp(scores - peak)
    total = jnp.sum(powers, axis=-1, keepdims=True)
    probs = (powers / total).astype(jnp.bfloat16)
    text_context = jnp.einsum(
        "hqk,khd->qhd", probs, text_values, preferred_element_type=jnp.float32
    ).astype(jnp.bfloat16)
    layout_context = jnp.einsum(
        "hqk,khd->qhd", probs, layout_values, preferred_element_type=jnp.float32
    ).astype(jnp.bfloat16)
    return (text_context, layout_context, peak + jnp.log(total))


def attend_back(pieces):
    (
        text_queries,
        text_keys,
        text_values,
        layout_queries,
        layout_keys,
        layout_values,
        usable,
        log_totals,
        text_cgrad,
        layout_cgrad,
    ) = pieces
    text_scale = (D // H) ** (-0.5)
    layout_scale = (DL // H) ** (-0.5)
    scores = coupled_scores(text_queries, text_keys, layout_queries, layout_keys, usable)
    probs = jnp.exp(scores - log_totals)
    probs_low = probs.astype(jnp.bfloat16)
    probs_grad = jnp.einsum(
        "qhd,khd->hqk", text_cgrad, text_values, preferred_element_type=jnp.float32
    )
    probs_grad = probs_grad + jnp.einsum(
        "qhd,khd->hqk", layout_cgrad, layout_values, preferred_element_type=jnp.float32
    )
    scores_grad = (
        probs * (probs_grad - jnp.sum(probs_grad * probs, axis=-1, keepdims=True))
    ).astype(jnp.bfloat16)
    text_vgrad = jnp.einsum(
        "hqk,qhd->khd", probs_low, text_cgrad, preferred_element_type=jnp.float32
    ).astype(jnp.bfloat16)
    layout_vgrad = jnp.einsum(
        "hqk,qhd->khd", probs_low, layout_cgrad, preferred_element_type=jnp.float32
    ).astype(jnp.bfloat16)
    text_qgrad = (
        jnp.einsum("hqk,khd->qhd", scores_grad, text_keys, preferred_element_type=jnp.float32)
        * text_scale
    ).astype(jnp.bfloat16)
    text_kgrad = (
        jnp.einsum("hqk,qhd->khd", scores_grad, text_queries, preferred_element_type=jnp.float32)
        * text_scale
    ).astype(jnp.bfloat16)
    layout_qgrad = (
        jnp.einsum("hqk,khd->qhd", scores_grad, layout_keys, preferred_element_type=jnp.float32)
        * layout_scale
    ).astype(jnp.bfloat16)
    layout_kgrad = (
        jnp.einsum("hqk,qhd->khd", scores_grad, layout_queries, preferred_element_type=jnp.float32)
        * layout_scale
    ).astype(jnp.bfloat16)
    return (text_qgrad, text_kgrad, text_vgrad, layout_qgrad, layout_kgrad, layout_vgrad)


def feed_forward(full_rows, w_up, up_bias, w_down):
    hidden = jnp.dot(full_rows, w_up, preferred_element_type=jnp.float32) + up_bias
    active, gelu_back = jax.vjp(gelu, hidden)
    active_low = active.astype(jnp.bfloat16)
    return (active_low, gelu_back, jnp.dot(active_low, w_down, preferred_element_type=jnp.float32))


def feed_back(full_rows, active_low, gelu_back, full_grad, w_up, w_down, down_spec="rf,rd->fd"):
    grad_down = jnp.einsum(down_spec, active_low, full_grad, preferred_element_type=jnp.float32)
    active_grad = jnp.einsum("rd,fd->rf", full_grad, w_down, preferred_element_type=jnp.float32)
    hidden_grad = gelu_back(active_grad)[0].astype(jnp.bfloat16)
    grad_up = jnp.einsum("rd,rf->df", full_rows, hidden_grad, preferred_element_type=jnp.float32)
    grad_bias = jnp.sum(hidden_grad, axis=0, dtype=jnp.float32)
    normed_part = jnp.einsum("rf,df->rd", hidden_grad, w_up, preferred_element_type=jnp.float32)
    return (grad_up, grad_bias, grad_down, normed_part)


def input_back(rows, weight_qkv, query_grad, key_grad, value_grad, stack_axis=0):
    grad_qkv = jnp.stack(
        [
            jnp.einsum("rd,re->de", rows, piece, preferred_element_type=jnp.float32)
            for piece in (query_grad, key_grad, value_grad)
        ],
        axis=stack_axis,
    )
    input_part = jnp.einsum(
        "re,de->rd", query_grad, weight_qkv[0], preferred_element_type=jnp.float32
    )
    input_part = input_part + jnp.einsum(
        "re,de->rd", key_grad, weight_qkv[1], preferred_element_type=jnp.float32
    )
    input_part = input_part + jnp.einsum(
        "re,de->rd", value_grad, weight_qkv[2], preferred_element_type=jnp.float32
    )
    grad_bias = jnp.stack(
        [
            jnp.sum(query_grad, axis=0, dtype=jnp.float32),
            jnp.sum(value_grad, axis=0, dtype=jnp.float32),
        ]
    )
    return (grad_qkv, grad_bias, input_part)


def xor_sum(values, axis, size):
    step = 1
    while step < size:
        values = values + lax.ppermute(
            values, axis, [(i, i ^ step) for i in range(size)]
        )
        step *= 2
    return values


def xor_exchange(values, step, size):
    return lax.ppermute(values, "dp", [(i, i ^ step) for i in range(size)])


def bit_orders(bits, colours):
    if bits <= 1:
        return [list(range(bits))] * colours
    main = list(range(bits - 1))
    orders = []
    for colour in range(colours):
        shift = colour % len(main)
        orders.append(main[shift:] + main[:shift] + [bits - 1])
    return orders


def halve(chunk, order, me, size, wire):
    for bit in order:
        mine = (me >> bit) & 1
        keep = lax.dynamic_index_in_dim(chunk, mine, axis=0, keepdims=False)
        send = lax.dynamic_index_in_dim(chunk, 1 - mine, axis=0, keepdims=False)
        chunk = keep + xor_exchange(send.astype(wire), 1 << bit, size).astype(chunk.dtype)
    return chunk


def double(block, order, me, size, bits):
    held = []
    for bit in reversed(order):
        other = xor_exchange(block, 1 << bit, size)
        mine = (me >> bit) & 1
        block = jnp.where(mine == 0, jnp.stack([block, other]), jnp.stack([other, block]))
        held.insert(0, bit)
    canonical = list(range(bits - 1, -1, -1))
    rest = list(range(len(held), block.ndim))
    block = jnp.transpose(block, [held.index(bit) for bit in canonical] + rest)
    return block.reshape((-1,) + block.shape[len(held) + 1 :])


def ordered(piece, order, size, bits):
    shaped = piece.reshape((2,) * bits + (piece.shape[0] // size,) + piece.shape[1:])
    canonical = list(range(bits - 1, -1, -1))
    rest = list(range(bits, shaped.ndim))
    return jnp.transpose(shaped, [canonical.index(bit) for bit in order] + rest)


def dp_reduce(scattered, colours_of, replicated, size, wire, lanes=128):
    bits = size.bit_length() - 1
    me = lax.axis_index("dp")
    orders = bit_orders(bits, 3)
    scattered_out = []
    for piece, colour in zip(scattered, colours_of):
        chunk = ordered(piece, orders[colour], size, bits)
        scattered_out.append(halve(chunk, orders[colour], me, size, wire))
    blocks = []
    for piece in replicated:
        flat = piece.reshape(-1)
        flat = jnp.pad(flat, (0, (-flat.shape[0]) % lanes))
        blocks.append(flat.reshape(-1, lanes))
    joined = jnp.concatenate(blocks)
    rows = joined.shape[0]
    joined = jnp.pad(joined, ((0, (-rows) % (size * 8)), (0, 0)))
    chunk = ordered(joined, orders[0], size, bits)
    block = halve(chunk, orders[0], me, size, wire)
    full = double(block, orders[0], me, size, bits)
    replicated_out = []
    offset = 0
    for piece in replicated:
        count = -(-piece.size // lanes)
        replicated_out.append(
            full[offset : offset + count].reshape(-1)[: piece.size].reshape(piece.shape)
        )
        offset += count
    return scattered_out, replicated_out

def body(
    text_input,
    layout_input,
    repeated,
    key_mask,
    text_qkv,
    text_qvbias,
    text_wout,
    text_outbias,
    text_wup,
    text_upbias,
    text_wdown,
    text_gains,
    text_shifts,
    layout_qkv,
    layout_qvbias,
    layout_wout,
    layout_outbias,
    layout_wup,
    layout_upbias,
    layout_wdown,
    layout_gains,
    layout_shifts,
    text_cotan,
    layout_cotan,
):
    text_head = D // H
    layout_head = DL // H
    usable_group = jnp.logical_and(key_mask == 1, repeated == 0).reshape(-1, WINDOW)
    text_rows, layout_rows = (
        lax.all_gather(text_input, "mp", axis=0, tiled=True),
        lax.all_gather(layout_input, "mp", axis=0, tiled=True),
    )
    text_queries, text_keys, text_values = project_path(text_rows, text_qkv, text_qvbias)
    layout_queries, layout_keys, layout_values = project_path(
        layout_rows, layout_qkv, layout_qvbias
    )
    blocks = (
        blocked(text_queries, text_head),
        blocked(text_keys, text_head),
        blocked(text_values, text_head),
        blocked(layout_queries, layout_head),
        blocked(layout_keys, layout_head),
        blocked(layout_values, layout_head),
        usable_group,
    )
    text_context, layout_context, log_totals = lax.map(attend_window, blocks)
    text_context = unblocked(text_context)
    layout_context = unblocked(layout_context)
    text_mixed_part = jnp.dot(text_context, text_wout, preferred_element_type=jnp.float32)
    layout_mixed_part = jnp.dot(layout_context, layout_wout, preferred_element_type=jnp.float32)
    text_mixed, layout_mixed = (
        lax.psum_scatter(
            text_mixed_part.astype(jnp.bfloat16), "mp", scatter_dimension=0, tiled=True
        ).astype(jnp.float32),
        lax.psum_scatter(
            layout_mixed_part.astype(jnp.bfloat16), "mp", scatter_dimension=0, tiled=True
        ).astype(jnp.float32),
    )
    text_gain = text_gains.astype(jnp.float32)
    text_shift = text_shifts.astype(jnp.float32)
    layout_gain = layout_gains.astype(jnp.float32)
    layout_shift = layout_shifts.astype(jnp.float32)
    text_normed, text_first_back = jax.vjp(
        layer_norm,
        text_input.astype(jnp.float32) + text_mixed + text_outbias[0],
        text_gain[0],
        text_shift[0],
    )
    layout_normed, layout_first_back = jax.vjp(
        layer_norm,
        layout_input.astype(jnp.float32) + layout_mixed + layout_outbias[0],
        layout_gain[0],
        layout_shift[0],
    )
    text_full, layout_full = (
        lax.all_gather(text_normed.astype(jnp.bfloat16), "mp", axis=0, tiled=True),
        lax.all_gather(layout_normed.astype(jnp.bfloat16), "mp", axis=0, tiled=True),
    )
    text_active, text_gelu_back, text_branch_part = feed_forward(
        text_full, text_wup, text_upbias, text_wdown
    )
    layout_active, layout_gelu_back, layout_branch_part = feed_forward(
        layout_full, layout_wup, layout_upbias, layout_wdown
    )
    text_branch, layout_branch = (
        lax.psum_scatter(
            text_branch_part.astype(jnp.bfloat16), "mp", scatter_dimension=0, tiled=True
        ).astype(jnp.float32),
        lax.psum_scatter(
            layout_branch_part.astype(jnp.bfloat16), "mp", scatter_dimension=0, tiled=True
        ).astype(jnp.float32),
    )
    text_final, text_final_back = jax.vjp(
        layer_norm, text_normed + text_branch + text_outbias[1], text_gain[1], text_shift[1]
    )
    layout_final, layout_final_back = jax.vjp(
        layer_norm,
        layout_normed + layout_branch + layout_outbias[1],
        layout_gain[1],
        layout_shift[1],
    )
    text_sum_grad, text_gain_second, text_shift_second = text_final_back(
        text_cotan.astype(jnp.float32)
    )
    layout_sum_grad, layout_gain_second, layout_shift_second = layout_final_back(
        layout_cotan.astype(jnp.float32)
    )
    text_branch_grad = text_sum_grad.astype(jnp.bfloat16)
    layout_branch_grad = layout_sum_grad.astype(jnp.bfloat16)
    text_full_grad, layout_full_grad = (
        lax.all_gather(text_branch_grad, "mp", axis=0, tiled=True),
        lax.all_gather(layout_branch_grad, "mp", axis=0, tiled=True),
    )
    text_wup_grad, text_upbias_grad, text_wdown_grad_t, text_normed_part = feed_back(
        text_full, text_active, text_gelu_back, text_full_grad, text_wup, text_wdown, "rf,rd->df"
    )
    layout_wup_grad, layout_upbias_grad, layout_wdown_grad, layout_normed_part = feed_back(
        layout_full, layout_active, layout_gelu_back, layout_full_grad, layout_wup, layout_wdown
    )
    text_normed_grad, layout_normed_grad = (
        lax.psum_scatter(
            text_normed_part.astype(jnp.bfloat16), "mp", scatter_dimension=0, tiled=True
        ).astype(jnp.float32),
        lax.psum_scatter(
            layout_normed_part.astype(jnp.bfloat16), "mp", scatter_dimension=0, tiled=True
        ).astype(jnp.float32),
    )
    text_mixed_grad, text_gain_first, text_shift_first = text_first_back(
        text_normed_grad + text_sum_grad
    )
    layout_mixed_grad, layout_gain_first, layout_shift_first = layout_first_back(
        layout_normed_grad + layout_sum_grad
    )
    text_mixed_low = text_mixed_grad.astype(jnp.bfloat16)
    layout_mixed_low = layout_mixed_grad.astype(jnp.bfloat16)
    text_wide_grad, layout_wide_grad = (
        lax.all_gather(text_mixed_low, "mp", axis=0, tiled=True),
        lax.all_gather(layout_mixed_low, "mp", axis=0, tiled=True),
    )
    text_wout_grad_t = jnp.einsum(
        "re,rd->de", text_context, text_wide_grad, preferred_element_type=jnp.float32
    )
    layout_wout_grad = jnp.einsum(
        "re,rd->ed", layout_context, layout_wide_grad, preferred_element_type=jnp.float32
    )
    text_context_grad = jnp.einsum(
        "rd,ed->re", text_wide_grad, text_wout, preferred_element_type=jnp.float32
    ).astype(jnp.bfloat16)
    layout_context_grad = jnp.einsum(
        "rd,ed->re", layout_wide_grad, layout_wout, preferred_element_type=jnp.float32
    ).astype(jnp.bfloat16)
    back_blocks = blocks + (
        log_totals,
        blocked(text_context_grad, text_head),
        blocked(layout_context_grad, layout_head),
    )
    text_qgrad, text_kgrad, text_vgrad, layout_qgrad, layout_kgrad, layout_vgrad = lax.map(
        attend_back, back_blocks
    )
    text_qkv_grad_t, text_qvbias_grad, text_input_part = input_back(
        text_rows,
        text_qkv,
        unblocked(text_qgrad),
        unblocked(text_kgrad),
        unblocked(text_vgrad),
        stack_axis=1,
    )
    layout_qkv_grad, layout_qvbias_grad, layout_input_part = input_back(
        layout_rows,
        layout_qkv,
        unblocked(layout_qgrad),
        unblocked(layout_kgrad),
        unblocked(layout_vgrad),
    )
    text_input_sum, layout_input_sum = (
        lax.psum_scatter(
            text_input_part.astype(jnp.bfloat16), "mp", scatter_dimension=0, tiled=True
        ).astype(jnp.float32),
        lax.psum_scatter(
            layout_input_part.astype(jnp.bfloat16), "mp", scatter_dimension=0, tiled=True
        ).astype(jnp.float32),
    )
    text_dinput = (text_mixed_grad + text_input_sum).astype(jnp.bfloat16)
    layout_dinput = (layout_mixed_grad + layout_input_sum).astype(jnp.bfloat16)
    n_dp = lax.axis_size("dp")
    n_mp = lax.axis_size("mp")
    small = jnp.concatenate(
        [
            part.reshape(-1)
            for part in (
                jnp.stack(
                    [
                        jnp.sum(text_mixed_low, axis=0, dtype=jnp.float32),
                        jnp.sum(text_branch_grad, axis=0, dtype=jnp.float32),
                    ]
                ),
                jnp.stack([text_gain_first, text_gain_second]),
                jnp.stack([text_shift_first, text_shift_second]),
                jnp.stack(
                    [
                        jnp.sum(layout_mixed_low, axis=0, dtype=jnp.float32),
                        jnp.sum(layout_branch_grad, axis=0, dtype=jnp.float32),
                    ]
                ),
                jnp.stack([layout_gain_first, layout_gain_second]),
                jnp.stack([layout_shift_first, layout_shift_second]),
            )
        ]
    )
    small = xor_sum(small, "mp", n_mp)
    scattered = (
        jnp.concatenate([text_qkv_grad_t, text_wout_grad_t[:, None, :]], axis=1),
        text_wup_grad,
        text_wdown_grad_t,
    )
    replicated = (
        text_qvbias_grad,
        text_upbias_grad,
        layout_qkv_grad,
        layout_qvbias_grad,
        layout_wout_grad,
        layout_wup_grad,
        layout_upbias_grad,
        layout_wdown_grad,
        small,
    )
    scattered, replicated = lax.optimization_barrier((scattered, replicated))
    scattered_out, replicated_out = dp_reduce(
        scattered, (2, 0, 1), replicated, n_dp, jnp.bfloat16
    )
    qkv_share = jnp.transpose(scattered_out[0][:, :3], (1, 0, 2))
    wout_share = scattered_out[0][:, 3].T
    wup_share = scattered_out[1]
    wdown_share = scattered_out[2].T
    summed = replicated_out[:8]
    small_sum = replicated_out[8]
    sizes = (2 * D, 2 * D, 2 * D, 2 * DL, 2 * DL, 2 * DL)
    shared = []
    offset = 0
    for size in sizes:
        shared.append(small_sum[offset : offset + size].reshape(2, -1))
        offset += size
    return (
        text_final.astype(jnp.bfloat16),
        layout_final.astype(jnp.bfloat16),
        text_dinput,
        layout_dinput,
        qkv_share,
        summed[0],
        wout_share,
        shared[0],
        wup_share,
        summed[1],
        wdown_share,
        shared[1],
        shared[2],
        summed[2],
        summed[3],
        summed[4],
        shared[3],
        summed[5],
        summed[6],
        summed[7],
        shared[4],
        shared[5],
    )


def solution(mesh):
    in_specs = (
        P(("dp", "mp"), None),
        P(("dp", "mp"), None),
        P("dp"),
        P("dp"),
        P(None, None, "mp"),
        P(None, "mp"),
        P("mp", None),
        P(),
        P(None, "mp"),
        P("mp"),
        P("mp", None),
        P(),
        P(),
        P(None, None, "mp"),
        P(None, "mp"),
        P("mp", None),
        P(),
        P(None, "mp"),
        P("mp"),
        P("mp", None),
        P(),
        P(),
        P(("dp", "mp"), None),
        P(("dp", "mp"), None),
    )
    out_specs = (
        P(("dp", "mp"), None),
        P(("dp", "mp"), None),
        P(("dp", "mp"), None),
        P(("dp", "mp"), None),
        P(None, "dp", "mp"),
        P(None, "mp"),
        P("mp", "dp"),
        P(),
        P("dp", "mp"),
        P("mp"),
        P("mp", "dp"),
        P(),
        P(),
        P(None, None, "mp"),
        P(None, "mp"),
        P("mp", None),
        P(),
        P(None, "mp"),
        P("mp"),
        P("mp", None),
        P(),
        P(),
    )
    return jax.shard_map(body, mesh=mesh, in_specs=in_specs, out_specs=out_specs, check_vma=False)
```

```python
import jax
import jax.numpy as jnp
from jax import lax
from jax.sharding import PartitionSpec as P


D = 768
H = 12
DL = 192
WINDOW = 512


EPSILON = 1e-05
MASKED = -1000000000.0


def layer_norm(values, gain, shift):
    centered = values - jnp.mean(values, axis=-1, keepdims=True)
    variance = jnp.mean(centered * centered, axis=-1, keepdims=True)
    return centered * lax.rsqrt(variance + EPSILON) * gain + shift


def gelu(values):
    return 0.5 * values * (1.0 + lax.erf(values * 0.7071067811865476))


def project_path(rows, weight_qkv, biases):
    joined = jnp.einsum("rd,kde->kre", rows, weight_qkv, preferred_element_type=jnp.float32)
    queries = (joined[0] + biases[0]).astype(jnp.bfloat16)
    key_rows = joined[1].astype(jnp.bfloat16)
    value_rows = (joined[2] + biases[1]).astype(jnp.bfloat16)
    return (queries, key_rows, value_rows)


def blocked(values, head_size):
    return values.reshape(-1, WINDOW, values.shape[-1] // head_size, head_size)


def unblocked(values):
    return values.reshape(-1, values.shape[-2] * values.shape[-1])


def coupled_scores(text_queries, text_keys, layout_queries, layout_keys, usable):
    scores = jnp.einsum(
        "qhd,khd->hqk", text_queries, text_keys, preferred_element_type=jnp.float32
    ) * (D // H) ** (-0.5)
    scores = scores + jnp.einsum(
        "qhd,khd->hqk", layout_queries, layout_keys, preferred_element_type=jnp.float32
    ) * (DL // H) ** (-0.5)
    return jnp.where(usable[None, None, :], scores, MASKED)


def attend_window(pieces):
    text_queries, text_keys, text_values, layout_queries, layout_keys, layout_values, usable = (
        pieces
    )
    scores = coupled_scores(text_queries, text_keys, layout_queries, layout_keys, usable)
    peak = jnp.max(scores, axis=-1, keepdims=True)
    powers = jnp.exp(scores - peak)
    total = jnp.sum(powers, axis=-1, keepdims=True)
    probs = (powers / total).astype(jnp.bfloat16)
    text_context = jnp.einsum(
        "hqk,khd->qhd", probs, text_values, preferred_element_type=jnp.float32
    ).astype(jnp.bfloat16)
    layout_context = jnp.einsum(
        "hqk,khd->qhd", probs, layout_values, preferred_element_type=jnp.float32
    ).astype(jnp.bfloat16)
    return (text_context, layout_context, peak + jnp.log(total))


def attend_back(pieces):
    (
        text_queries,
        text_keys,
        text_values,
        layout_queries,
        layout_keys,
        layout_values,
        usable,
        log_totals,
        text_cgrad,
        layout_cgrad,
    ) = pieces
    text_scale = (D // H) ** (-0.5)
    layout_scale = (DL // H) ** (-0.5)
    scores = coupled_scores(text_queries, text_keys, layout_queries, layout_keys, usable)
    probs = jnp.exp(scores - log_totals)
    probs_low = probs.astype(jnp.bfloat16)
    probs_grad = jnp.einsum(
        "qhd,khd->hqk", text_cgrad, text_values, preferred_element_type=jnp.float32
    )
    probs_grad = probs_grad + jnp.einsum(
        "qhd,khd->hqk", layout_cgrad, layout_values, preferred_element_type=jnp.float32
    )
    scores_grad = (
        probs * (probs_grad - jnp.sum(probs_grad * probs, axis=-1, keepdims=True))
    ).astype(jnp.bfloat16)
    text_vgrad = jnp.einsum(
        "hqk,qhd->khd", probs_low, text_cgrad, preferred_element_type=jnp.float32
    ).astype(jnp.bfloat16)
    layout_vgrad = jnp.einsum(
        "hqk,qhd->khd", probs_low, layout_cgrad, preferred_element_type=jnp.float32
    ).astype(jnp.bfloat16)
    text_qgrad = (
        jnp.einsum("hqk,khd->qhd", scores_grad, text_keys, preferred_element_type=jnp.float32)
        * text_scale
    ).astype(jnp.bfloat16)
    text_kgrad = (
        jnp.einsum("hqk,qhd->khd", scores_grad, text_queries, preferred_element_type=jnp.float32)
        * text_scale
    ).astype(jnp.bfloat16)
    layout_qgrad = (
        jnp.einsum("hqk,khd->qhd", scores_grad, layout_keys, preferred_element_type=jnp.float32)
        * layout_scale
    ).astype(jnp.bfloat16)
    layout_kgrad = (
        jnp.einsum("hqk,qhd->khd", scores_grad, layout_queries, preferred_element_type=jnp.float32)
        * layout_scale
    ).astype(jnp.bfloat16)
    return (text_qgrad, text_kgrad, text_vgrad, layout_qgrad, layout_kgrad, layout_vgrad)


def feed_forward(full_rows, w_up, up_bias, w_down):
    hidden = jnp.dot(full_rows, w_up, preferred_element_type=jnp.float32) + up_bias
    active, gelu_back = jax.vjp(gelu, hidden)
    active_low = active.astype(jnp.bfloat16)
    return (active_low, gelu_back, jnp.dot(active_low, w_down, preferred_element_type=jnp.float32))


def feed_back(full_rows, active_low, gelu_back, full_grad, w_up, w_down, down_spec="rf,rd->fd"):
    grad_down = jnp.einsum(down_spec, active_low, full_grad, preferred_element_type=jnp.float32)
    active_grad = jnp.einsum("rd,fd->rf", full_grad, w_down, preferred_element_type=jnp.float32)
    hidden_grad = gelu_back(active_grad)[0].astype(jnp.bfloat16)
    grad_up = jnp.einsum("rd,rf->df", full_rows, hidden_grad, preferred_element_type=jnp.float32)
    grad_bias = jnp.sum(hidden_grad, axis=0, dtype=jnp.float32)
    normed_part = jnp.einsum("rf,df->rd", hidden_grad, w_up, preferred_element_type=jnp.float32)
    return (grad_up, grad_bias, grad_down, normed_part)


def input_back(rows, weight_qkv, query_grad, key_grad, value_grad, stack_axis=0):
    grad_qkv = jnp.stack(
        [
            jnp.einsum("rd,re->de", rows, piece, preferred_element_type=jnp.float32)
            for piece in (query_grad, key_grad, value_grad)
        ],
        axis=stack_axis,
    )
    input_part = jnp.einsum(
        "re,de->rd", query_grad, weight_qkv[0], preferred_element_type=jnp.float32
    )
    input_part = input_part + jnp.einsum(
        "re,de->rd", key_grad, weight_qkv[1], preferred_element_type=jnp.float32
    )
    input_part = input_part + jnp.einsum(
        "re,de->rd", value_grad, weight_qkv[2], preferred_element_type=jnp.float32
    )
    grad_bias = jnp.stack(
        [
            jnp.sum(query_grad, axis=0, dtype=jnp.float32),
            jnp.sum(value_grad, axis=0, dtype=jnp.float32),
        ]
    )
    return (grad_qkv, grad_bias, input_part)


def xor_sum(values, axis, size):
    step = 1
    while step < size:
        values = values + lax.ppermute(
            values, axis, [(i, i ^ step) for i in range(size)]
        )
        step *= 2
    return values


def xor_exchange(values, step, size):
    return lax.ppermute(values, "dp", [(i, i ^ step) for i in range(size)])


def bit_orders(bits, colours):
    if bits <= 1:
        return [list(range(bits))] * colours
    main = list(range(bits - 1))
    orders = []
    for colour in range(colours):
        shift = colour % len(main)
        orders.append(main[shift:] + main[:shift] + [bits - 1])
    return orders


def halve(chunk, order, me, size, wire):
    for bit in order:
        mine = (me >> bit) & 1
        keep = lax.dynamic_index_in_dim(chunk, mine, axis=0, keepdims=False)
        send = lax.dynamic_index_in_dim(chunk, 1 - mine, axis=0, keepdims=False)
        received = xor_exchange(send.astype(wire), 1 << bit, size)
        chunk = keep + received.astype(chunk.dtype)
    return chunk


def double(block, order, me, size, bits):
    held = []
    for bit in reversed(order):
        other = xor_exchange(block, 1 << bit, size)
        mine = (me >> bit) & 1
        block = jnp.where(mine == 0, jnp.stack([block, other]), jnp.stack([other, block]))
        held.insert(0, bit)
    canonical = list(range(bits - 1, -1, -1))
    rest = list(range(len(held), block.ndim))
    block = jnp.transpose(block, [held.index(bit) for bit in canonical] + rest)
    return block.reshape((-1,) + block.shape[len(held) + 1 :])


def ordered(piece, order, size, bits):
    shaped = piece.reshape((2,) * bits + (piece.shape[0] // size,) + piece.shape[1:])
    canonical = list(range(bits - 1, -1, -1))
    rest = list(range(bits, shaped.ndim))
    return jnp.transpose(shaped, [canonical.index(bit) for bit in order] + rest)


def reduce_scattered(pieces, colours_of, size, wire):
    bits = size.bit_length() - 1
    me = lax.axis_index("dp")
    orders = bit_orders(bits, 3)
    out = []
    for piece, colour in zip(pieces, colours_of):
        chunk = ordered(piece, orders[colour], size, bits)
        out.append(halve(chunk, orders[colour], me, size, wire))
    return out


def reduce_replicated(replicated, size, wire, lanes=128):
    bits = size.bit_length() - 1
    me = lax.axis_index("dp")
    order = bit_orders(bits, 3)[0]
    blocks = []
    for piece in replicated:
        flat = piece.reshape(-1)
        flat = jnp.pad(flat, (0, (-flat.shape[0]) % lanes))
        blocks.append(flat.reshape(-1, lanes))
    joined = jnp.concatenate(blocks)
    rows = joined.shape[0]
    joined = jnp.pad(joined, ((0, (-rows) % (size * 8)), (0, 0)))
    chunk = ordered(joined, order, size, bits)
    block = halve(chunk, order, me, size, wire)
    full = double(block, order, me, size, bits)
    out = []
    offset = 0
    for piece in replicated:
        count = -(-piece.size // lanes)
        out.append(full[offset : offset + count].reshape(-1)[: piece.size].reshape(piece.shape))
        offset += count
    return out


def layer_body(
    text_input,
    layout_input,
    repeated,
    key_mask,
    text_qkv,
    text_qvbias,
    text_wout,
    text_outbias,
    text_wup,
    text_upbias,
    text_wdown,
    text_gains,
    text_shifts,
    layout_qkv,
    layout_qvbias,
    layout_wout,
    layout_outbias,
    layout_wup,
    layout_upbias,
    layout_wdown,
    layout_gains,
    layout_shifts,
    text_cotan,
    layout_cotan,
):
    text_head = D // H
    layout_head = DL // H
    usable_group = jnp.logical_and(key_mask == 1, repeated == 0).reshape(-1, WINDOW)
    text_rows, layout_rows = (
        lax.all_gather(text_input, "mp", axis=0, tiled=True),
        lax.all_gather(layout_input, "mp", axis=0, tiled=True),
    )
    text_queries, text_keys, text_values = project_path(text_rows, text_qkv, text_qvbias)
    layout_queries, layout_keys, layout_values = project_path(
        layout_rows, layout_qkv, layout_qvbias
    )
    blocks = (
        blocked(text_queries, text_head),
        blocked(text_keys, text_head),
        blocked(text_values, text_head),
        blocked(layout_queries, layout_head),
        blocked(layout_keys, layout_head),
        blocked(layout_values, layout_head),
        usable_group,
    )
    text_context, layout_context, log_totals = lax.map(attend_window, blocks)
    text_context = unblocked(text_context)
    layout_context = unblocked(layout_context)
    text_mixed_part = jnp.dot(text_context, text_wout, preferred_element_type=jnp.float32)
    layout_mixed_part = jnp.dot(layout_context, layout_wout, preferred_element_type=jnp.float32)
    text_mixed, layout_mixed = (
        lax.psum_scatter(
            text_mixed_part.astype(jnp.bfloat16), "mp", scatter_dimension=0, tiled=True
        ).astype(jnp.float32),
        lax.psum_scatter(
            layout_mixed_part.astype(jnp.bfloat16), "mp", scatter_dimension=0, tiled=True
        ).astype(jnp.float32),
    )
    text_gain = text_gains.astype(jnp.float32)
    text_shift = text_shifts.astype(jnp.float32)
    layout_gain = layout_gains.astype(jnp.float32)
    layout_shift = layout_shifts.astype(jnp.float32)
    text_normed, text_first_back = jax.vjp(
        layer_norm,
        text_input.astype(jnp.float32) + text_mixed + text_outbias[0],
        text_gain[0],
        text_shift[0],
    )
    layout_normed, layout_first_back = jax.vjp(
        layer_norm,
        layout_input.astype(jnp.float32) + layout_mixed + layout_outbias[0],
        layout_gain[0],
        layout_shift[0],
    )
    text_full, layout_full = (
        lax.all_gather(text_normed.astype(jnp.bfloat16), "mp", axis=0, tiled=True),
        lax.all_gather(layout_normed.astype(jnp.bfloat16), "mp", axis=0, tiled=True),
    )
    text_active, text_gelu_back, text_branch_part = feed_forward(
        text_full, text_wup, text_upbias, text_wdown
    )
    layout_active, layout_gelu_back, layout_branch_part = feed_forward(
        layout_full, layout_wup, layout_upbias, layout_wdown
    )
    text_branch, layout_branch = (
        lax.psum_scatter(
            text_branch_part.astype(jnp.bfloat16), "mp", scatter_dimension=0, tiled=True
        ).astype(jnp.float32),
        lax.psum_scatter(
            layout_branch_part.astype(jnp.bfloat16), "mp", scatter_dimension=0, tiled=True
        ).astype(jnp.float32),
    )
    text_final, text_final_back = jax.vjp(
        layer_norm, text_normed + text_branch + text_outbias[1], text_gain[1], text_shift[1]
    )
    layout_final, layout_final_back = jax.vjp(
        layer_norm,
        layout_normed + layout_branch + layout_outbias[1],
        layout_gain[1],
        layout_shift[1],
    )
    text_sum_grad, text_gain_second, text_shift_second = text_final_back(
        text_cotan.astype(jnp.float32)
    )
    layout_sum_grad, layout_gain_second, layout_shift_second = layout_final_back(
        layout_cotan.astype(jnp.float32)
    )
    text_branch_grad = text_sum_grad.astype(jnp.bfloat16)
    layout_branch_grad = layout_sum_grad.astype(jnp.bfloat16)
    text_full_grad, layout_full_grad = (
        lax.all_gather(text_branch_grad, "mp", axis=0, tiled=True),
        lax.all_gather(layout_branch_grad, "mp", axis=0, tiled=True),
    )
    text_wup_grad, text_upbias_grad, text_wdown_grad_t, text_normed_part = feed_back(
        text_full, text_active, text_gelu_back, text_full_grad, text_wup, text_wdown, "rf,rd->df"
    )
    n_dp = lax.axis_size("dp")
    wup_share, wdown_share_t = reduce_scattered(
        (text_wup_grad, text_wdown_grad_t), (0, 1), n_dp, jnp.bfloat16
    )
    layout_wup_grad, layout_upbias_grad, layout_wdown_grad, layout_normed_part = feed_back(
        layout_full, layout_active, layout_gelu_back, layout_full_grad, layout_wup, layout_wdown
    )
    text_normed_grad, layout_normed_grad = (
        lax.psum_scatter(
            text_normed_part.astype(jnp.bfloat16), "mp", scatter_dimension=0, tiled=True
        ).astype(jnp.float32),
        lax.psum_scatter(
            layout_normed_part.astype(jnp.bfloat16), "mp", scatter_dimension=0, tiled=True
        ).astype(jnp.float32),
    )
    text_mixed_grad, text_gain_first, text_shift_first = text_first_back(
        text_normed_grad + text_sum_grad
    )
    layout_mixed_grad, layout_gain_first, layout_shift_first = layout_first_back(
        layout_normed_grad + layout_sum_grad
    )
    text_mixed_low = text_mixed_grad.astype(jnp.bfloat16)
    layout_mixed_low = layout_mixed_grad.astype(jnp.bfloat16)
    text_wide_grad, layout_wide_grad = (
        lax.all_gather(text_mixed_low, "mp", axis=0, tiled=True),
        lax.all_gather(layout_mixed_low, "mp", axis=0, tiled=True),
    )
    text_wout_grad_t = jnp.einsum(
        "re,rd->de", text_context, text_wide_grad, preferred_element_type=jnp.float32
    )
    layout_wout_grad = jnp.einsum(
        "re,rd->ed", layout_context, layout_wide_grad, preferred_element_type=jnp.float32
    )
    text_context_grad = jnp.einsum(
        "rd,ed->re", text_wide_grad, text_wout, preferred_element_type=jnp.float32
    ).astype(jnp.bfloat16)
    layout_context_grad = jnp.einsum(
        "rd,ed->re", layout_wide_grad, layout_wout, preferred_element_type=jnp.float32
    ).astype(jnp.bfloat16)
    back_blocks = blocks + (
        log_totals,
        blocked(text_context_grad, text_head),
        blocked(layout_context_grad, layout_head),
    )
    text_qgrad, text_kgrad, text_vgrad, layout_qgrad, layout_kgrad, layout_vgrad = lax.map(
        attend_back, back_blocks
    )
    text_qkv_grad_t, text_qvbias_grad, text_input_part = input_back(
        text_rows,
        text_qkv,
        unblocked(text_qgrad),
        unblocked(text_kgrad),
        unblocked(text_vgrad),
        stack_axis=1,
    )
    layout_qkv_grad, layout_qvbias_grad, layout_input_part = input_back(
        layout_rows,
        layout_qkv,
        unblocked(layout_qgrad),
        unblocked(layout_kgrad),
        unblocked(layout_vgrad),
    )
    text_input_sum, layout_input_sum = (
        lax.psum_scatter(
            text_input_part.astype(jnp.bfloat16), "mp", scatter_dimension=0, tiled=True
        ).astype(jnp.float32),
        lax.psum_scatter(
            layout_input_part.astype(jnp.bfloat16), "mp", scatter_dimension=0, tiled=True
        ).astype(jnp.float32),
    )
    text_dinput = (text_mixed_grad + text_input_sum).astype(jnp.bfloat16)
    layout_dinput = (layout_mixed_grad + layout_input_sum).astype(jnp.bfloat16)
    n_mp = lax.axis_size("mp")
    small = jnp.concatenate(
        [
            part.reshape(-1)
            for part in (
                jnp.stack(
                    [
                        jnp.sum(text_mixed_low, axis=0, dtype=jnp.float32),
                        jnp.sum(text_branch_grad, axis=0, dtype=jnp.float32),
                    ]
                ),
                jnp.stack([text_gain_first, text_gain_second]),
                jnp.stack([text_shift_first, text_shift_second]),
                jnp.stack(
                    [
                        jnp.sum(layout_mixed_low, axis=0, dtype=jnp.float32),
                        jnp.sum(layout_branch_grad, axis=0, dtype=jnp.float32),
                    ]
                ),
                jnp.stack([layout_gain_first, layout_gain_second]),
                jnp.stack([layout_shift_first, layout_shift_second]),
            )
        ]
    )
    small = xor_sum(small, "mp", n_mp)
    scattered = (jnp.concatenate([text_qkv_grad_t, text_wout_grad_t[:, None, :]], axis=1),)
    replicated = (
        text_qvbias_grad,
        text_upbias_grad,
        layout_qkv_grad,
        layout_qvbias_grad,
        layout_wout_grad,
        layout_wup_grad,
        layout_upbias_grad,
        layout_wdown_grad,
        small,
    )
    scattered_out = reduce_scattered(scattered, (2,), n_dp, jnp.bfloat16)
    replicated_out = reduce_replicated(replicated, n_dp, jnp.bfloat16)
    qkv_share = jnp.transpose(scattered_out[0][:, :3], (1, 0, 2))
    wout_share = scattered_out[0][:, 3].T
    wdown_share = wdown_share_t.T
    summed = replicated_out[:8]
    small_sum = replicated_out[8]
    sizes = (2 * D, 2 * D, 2 * D, 2 * DL, 2 * DL, 2 * DL)
    shared = []
    offset = 0
    for size in sizes:
        shared.append(small_sum[offset : offset + size].reshape(2, -1))
        offset += size
    return (
        text_final.astype(jnp.bfloat16),
        layout_final.astype(jnp.bfloat16),
        text_dinput,
        layout_dinput,
        qkv_share,
        summed[0],
        wout_share,
        shared[0],
        wup_share,
        summed[1],
        wdown_share,
        shared[1],
        shared[2],
        summed[2],
        summed[3],
        summed[4],
        shared[3],
        summed[5],
        summed[6],
        summed[7],
        shared[4],
        shared[5],
    )


def solution(mesh):
    in_specs = (
        P(("dp", "mp"), None),
        P(("dp", "mp"), None),
        P("dp"),
        P("dp"),
        P(None, None, "mp"),
        P(None, "mp"),
        P("mp", None),
        P(),
        P(None, "mp"),
        P("mp"),
        P("mp", None),
        P(),
        P(),
        P(None, None, "mp"),
        P(None, "mp"),
        P("mp", None),
        P(),
        P(None, "mp"),
        P("mp"),
        P("mp", None),
        P(),
        P(),
        P(("dp", "mp"), None),
        P(("dp", "mp"), None),
    )
    out_specs = (
        P(("dp", "mp"), None),
        P(("dp", "mp"), None),
        P(("dp", "mp"), None),
        P(("dp", "mp"), None),
        P(None, "dp", "mp"),
        P(None, "mp"),
        P("mp", "dp"),
        P(),
        P("dp", "mp"),
        P("mp"),
        P("mp", "dp"),
        P(),
        P(),
        P(None, None, "mp"),
        P(None, "mp"),
        P("mp", None),
        P(),
        P(None, "mp"),
        P("mp"),
        P("mp", None),
        P(),
        P(),
    )
    return jax.shard_map(layer_body, mesh=mesh, in_specs=in_specs, out_specs=out_specs, check_vma=False)
```

```python
import jax
import jax.numpy as jnp
from jax import lax
from jax.sharding import PartitionSpec as P


D = 768
H = 12
DL = 192
WINDOW = 512


EPSILON = 1e-05
MASKED = -1000000000.0


def layer_norm(values, gain, shift):
    centered = values - jnp.mean(values, axis=-1, keepdims=True)
    variance = jnp.mean(centered * centered, axis=-1, keepdims=True)
    return centered * lax.rsqrt(variance + EPSILON) * gain + shift


def gelu(values):
    return 0.5 * values * (1.0 + lax.erf(values * 0.7071067811865476))


def project_path(rows, weight_qkv, biases):
    joined = jnp.einsum("rd,kde->kre", rows, weight_qkv, preferred_element_type=jnp.float32)
    queries = (joined[0] + biases[0]).astype(jnp.bfloat16)
    key_rows = joined[1].astype(jnp.bfloat16)
    value_rows = (joined[2] + biases[1]).astype(jnp.bfloat16)
    return (queries, key_rows, value_rows)


def blocked(values, head_size):
    return values.reshape(-1, WINDOW, values.shape[-1] // head_size, head_size)


def unblocked(values):
    return values.reshape(-1, values.shape[-2] * values.shape[-1])


def coupled_scores(text_queries, text_keys, layout_queries, layout_keys, usable):
    scores = jnp.einsum(
        "qhd,khd->hqk", text_queries, text_keys, preferred_element_type=jnp.float32
    ) * (D // H) ** (-0.5)
    scores = scores + jnp.einsum(
        "qhd,khd->hqk", layout_queries, layout_keys, preferred_element_type=jnp.float32
    ) * (DL // H) ** (-0.5)
    return jnp.where(usable[None, None, :], scores, MASKED)


def attend_window(pieces):
    text_queries, text_keys, text_values, layout_queries, layout_keys, layout_values, usable = (
        pieces
    )
    scores = coupled_scores(text_queries, text_keys, layout_queries, layout_keys, usable)
    peak = jnp.max(scores, axis=-1, keepdims=True)
    powers = jnp.exp(scores - peak)
    total = jnp.sum(powers, axis=-1, keepdims=True)
    probs = (powers / total).astype(jnp.bfloat16)
    text_context = jnp.einsum(
        "hqk,khd->qhd", probs, text_values, preferred_element_type=jnp.float32
    ).astype(jnp.bfloat16)
    layout_context = jnp.einsum(
        "hqk,khd->qhd", probs, layout_values, preferred_element_type=jnp.float32
    ).astype(jnp.bfloat16)
    return (text_context, layout_context, peak + jnp.log(total))


def attend_back(pieces):
    (
        text_queries,
        text_keys,
        text_values,
        layout_queries,
        layout_keys,
        layout_values,
        usable,
        log_totals,
        text_cgrad,
        layout_cgrad,
    ) = pieces
    text_scale = (D // H) ** (-0.5)
    layout_scale = (DL // H) ** (-0.5)
    scores = coupled_scores(text_queries, text_keys, layout_queries, layout_keys, usable)
    probs = jnp.exp(scores - log_totals)
    probs_low = probs.astype(jnp.bfloat16)
    probs_grad = jnp.einsum(
        "qhd,khd->hqk", text_cgrad, text_values, preferred_element_type=jnp.float32
    )
    probs_grad = probs_grad + jnp.einsum(
        "qhd,khd->hqk", layout_cgrad, layout_values, preferred_element_type=jnp.float32
    )
    scores_grad = (
        probs * (probs_grad - jnp.sum(probs_grad * probs, axis=-1, keepdims=True))
    ).astype(jnp.bfloat16)
    text_vgrad = jnp.einsum(
        "hqk,qhd->khd", probs_low, text_cgrad, preferred_element_type=jnp.float32
    ).astype(jnp.bfloat16)
    layout_vgrad = jnp.einsum(
        "hqk,qhd->khd", probs_low, layout_cgrad, preferred_element_type=jnp.float32
    ).astype(jnp.bfloat16)
    text_qgrad = (
        jnp.einsum("hqk,khd->qhd", scores_grad, text_keys, preferred_element_type=jnp.float32)
        * text_scale
    ).astype(jnp.bfloat16)
    text_kgrad = (
        jnp.einsum("hqk,qhd->khd", scores_grad, text_queries, preferred_element_type=jnp.float32)
        * text_scale
    ).astype(jnp.bfloat16)
    layout_qgrad = (
        jnp.einsum("hqk,khd->qhd", scores_grad, layout_keys, preferred_element_type=jnp.float32)
        * layout_scale
    ).astype(jnp.bfloat16)
    layout_kgrad = (
        jnp.einsum("hqk,qhd->khd", scores_grad, layout_queries, preferred_element_type=jnp.float32)
        * layout_scale
    ).astype(jnp.bfloat16)
    return (text_qgrad, text_kgrad, text_vgrad, layout_qgrad, layout_kgrad, layout_vgrad)


def feed_forward(full_rows, w_up, up_bias, w_down):
    hidden = jnp.dot(full_rows, w_up, preferred_element_type=jnp.float32) + up_bias
    active, gelu_back = jax.vjp(gelu, hidden)
    active_low = active.astype(jnp.bfloat16)
    return (active_low, gelu_back, jnp.dot(active_low, w_down, preferred_element_type=jnp.float32))


def feed_back(
    full_rows, active_low, gelu_back, full_grad, w_up, w_down, down_spec="rf,rd->fd", up_rows=None, down_rows=None
):
    up_rows = full_rows if up_rows is None else up_rows
    down_rows = full_grad if down_rows is None else down_rows
    grad_down = jnp.einsum(down_spec, active_low, down_rows, preferred_element_type=jnp.float32)
    active_grad = jnp.einsum("rd,fd->rf", full_grad, w_down, preferred_element_type=jnp.float32)
    hidden_grad = gelu_back(active_grad)[0].astype(jnp.bfloat16)
    grad_up = jnp.einsum("rd,rf->df", up_rows, hidden_grad, preferred_element_type=jnp.float32)
    grad_bias = jnp.sum(hidden_grad, axis=0, dtype=jnp.float32)
    normed_part = jnp.einsum("rf,df->rd", hidden_grad, w_up, preferred_element_type=jnp.float32)
    return (grad_up, grad_bias, grad_down, normed_part)


def input_back(rows, weight_qkv, query_grad, key_grad, value_grad, stack_axis=0, grad_rows=None):
    grad_rows = rows if grad_rows is None else grad_rows
    grad_qkv = jnp.stack(
        [
            jnp.einsum("rd,re->de", grad_rows, piece, preferred_element_type=jnp.float32)
            for piece in (query_grad, key_grad, value_grad)
        ],
        axis=stack_axis,
    )
    input_part = jnp.einsum(
        "re,de->rd", query_grad, weight_qkv[0], preferred_element_type=jnp.float32
    )
    input_part = input_part + jnp.einsum(
        "re,de->rd", key_grad, weight_qkv[1], preferred_element_type=jnp.float32
    )
    input_part = input_part + jnp.einsum(
        "re,de->rd", value_grad, weight_qkv[2], preferred_element_type=jnp.float32
    )
    grad_bias = jnp.stack(
        [
            jnp.sum(query_grad, axis=0, dtype=jnp.float32),
            jnp.sum(value_grad, axis=0, dtype=jnp.float32),
        ]
    )
    return (grad_qkv, grad_bias, input_part)


def xor_sum(values, axis, size):
    step = 1
    while step < size:
        values = values + lax.ppermute(
            values, axis, [(i, i ^ step) for i in range(size)]
        )
        step *= 2
    return values


def xor_exchange(values, step, size):
    return lax.ppermute(values, "dp", [(i, i ^ step) for i in range(size)])


def bit_orders(bits, colours):
    if bits <= 1:
        return [list(range(bits))] * colours
    main = list(range(bits - 1))
    orders = []
    for colour in range(colours):
        shift = colour % len(main)
        orders.append(main[shift:] + main[:shift] + [bits - 1])
    return orders


def halve(chunk, order, me, size, wire):
    for bit in order:
        mine = (me >> bit) & 1
        keep = lax.dynamic_index_in_dim(chunk, mine, axis=0, keepdims=False)
        send = lax.dynamic_index_in_dim(chunk, 1 - mine, axis=0, keepdims=False)
        received = xor_exchange(send.astype(wire), 1 << bit, size)
        chunk = keep + received.astype(chunk.dtype)
    return chunk


def double(block, order, me, size, bits):
    held = []
    for bit in reversed(order):
        other = xor_exchange(block, 1 << bit, size)
        mine = (me >> bit) & 1
        block = jnp.where(mine == 0, jnp.stack([block, other]), jnp.stack([other, block]))
        held.insert(0, bit)
    canonical = list(range(bits - 1, -1, -1))
    rest = list(range(len(held), block.ndim))
    block = jnp.transpose(block, [held.index(bit) for bit in canonical] + rest)
    return block.reshape((-1,) + block.shape[len(held) + 1 :])


def ordered(piece, order, size, bits):
    shaped = piece.reshape((2,) * bits + (piece.shape[0] // size,) + piece.shape[1:])
    canonical = list(range(bits - 1, -1, -1))
    rest = list(range(bits, shaped.ndim))
    return jnp.transpose(shaped, [canonical.index(bit) for bit in order] + rest)


def chain_orders(size, colours):
    bits = size.bit_length() - 1
    return bit_orders(bits, colours)[:colours]


def permute_columns(values, orders, size):
    bits = size.bit_length() - 1
    colours = len(orders)
    lead = values.shape[:-1]
    n = len(lead)
    per = values.shape[-1] // size
    shaped = values.reshape(lead + (2,) * bits + (colours, per // colours))
    canonical = list(range(bits - 1, -1, -1))
    parts = []
    for colour, order in enumerate(orders):
        part = lax.index_in_dim(shaped, colour, axis=n + bits, keepdims=False)
        axes = list(range(n)) + [n + canonical.index(bit) for bit in order] + [n + bits]
        parts.append(jnp.transpose(part, axes))
    return jnp.stack(parts, axis=n).reshape(values.shape)


def reduce_permuted(grad, orders, size, wire):
    bits = size.bit_length() - 1
    me = lax.axis_index("dp")
    colours = len(orders)
    per = grad.shape[0] // size
    shaped = grad.reshape((colours,) + (2,) * bits + (per // colours,) + grad.shape[1:])
    return jnp.concatenate(
        [halve(shaped[colour], orders[colour], me, size, wire) for colour in range(colours)]
    )


def reduce_replicated(replicated, size, wire, order, lanes=128):
    bits = size.bit_length() - 1
    me = lax.axis_index("dp")
    blocks = []
    for piece in replicated:
        flat = piece.reshape(-1)
        flat = jnp.pad(flat, (0, (-flat.shape[0]) % lanes))
        blocks.append(flat.reshape(-1, lanes))
    joined = jnp.concatenate(blocks)
    rows = joined.shape[0]
    joined = jnp.pad(joined, ((0, (-rows) % (size * 8)), (0, 0)))
    chunk = ordered(joined, order, size, bits)
    block = halve(chunk, order, me, size, wire)
    full = double(block, order, me, size, bits)
    out = []
    offset = 0
    for piece in replicated:
        count = -(-piece.size // lanes)
        out.append(full[offset : offset + count].reshape(-1)[: piece.size].reshape(piece.shape))
        offset += count
    return out


def layer_body(
    text_input,
    layout_input,
    repeated,
    key_mask,
    text_qkv,
    text_qvbias,
    text_wout,
    text_outbias,
    text_wup,
    text_upbias,
    text_wdown,
    text_gains,
    text_shifts,
    layout_qkv,
    layout_qvbias,
    layout_wout,
    layout_outbias,
    layout_wup,
    layout_upbias,
    layout_wdown,
    layout_gains,
    layout_shifts,
    text_cotan,
    layout_cotan,
):
    text_head = D // H
    layout_head = DL // H
    usable_group = jnp.logical_and(key_mask == 1, repeated == 0).reshape(-1, WINDOW)
    text_rows, layout_rows = (
        lax.all_gather(text_input, "mp", axis=0, tiled=True),
        lax.all_gather(layout_input, "mp", axis=0, tiled=True),
    )
    text_queries, text_keys, text_values = project_path(text_rows, text_qkv, text_qvbias)
    layout_queries, layout_keys, layout_values = project_path(
        layout_rows, layout_qkv, layout_qvbias
    )
    blocks = (
        blocked(text_queries, text_head),
        blocked(text_keys, text_head),
        blocked(text_values, text_head),
        blocked(layout_queries, layout_head),
        blocked(layout_keys, layout_head),
        blocked(layout_values, layout_head),
        usable_group,
    )
    text_context, layout_context, log_totals = lax.map(attend_window, blocks)
    text_context = unblocked(text_context)
    layout_context = unblocked(layout_context)
    text_mixed_part = jnp.dot(text_context, text_wout, preferred_element_type=jnp.float32)
    layout_mixed_part = jnp.dot(layout_context, layout_wout, preferred_element_type=jnp.float32)
    text_mixed, layout_mixed = (
        lax.psum_scatter(
            text_mixed_part.astype(jnp.bfloat16), "mp", scatter_dimension=0, tiled=True
        ).astype(jnp.float32),
        lax.psum_scatter(
            layout_mixed_part.astype(jnp.bfloat16), "mp", scatter_dimension=0, tiled=True
        ).astype(jnp.float32),
    )
    text_gain = text_gains.astype(jnp.float32)
    text_shift = text_shifts.astype(jnp.float32)
    layout_gain = layout_gains.astype(jnp.float32)
    layout_shift = layout_shifts.astype(jnp.float32)
    text_normed, text_first_back = jax.vjp(
        layer_norm,
        text_input.astype(jnp.float32) + text_mixed + text_outbias[0],
        text_gain[0],
        text_shift[0],
    )
    layout_normed, layout_first_back = jax.vjp(
        layer_norm,
        layout_input.astype(jnp.float32) + layout_mixed + layout_outbias[0],
        layout_gain[0],
        layout_shift[0],
    )
    text_full, layout_full = (
        lax.all_gather(text_normed.astype(jnp.bfloat16), "mp", axis=0, tiled=True),
        lax.all_gather(layout_normed.astype(jnp.bfloat16), "mp", axis=0, tiled=True),
    )
    text_active, text_gelu_back, text_branch_part = feed_forward(
        text_full, text_wup, text_upbias, text_wdown
    )
    layout_active, layout_gelu_back, layout_branch_part = feed_forward(
        layout_full, layout_wup, layout_upbias, layout_wdown
    )
    text_branch, layout_branch = (
        lax.psum_scatter(
            text_branch_part.astype(jnp.bfloat16), "mp", scatter_dimension=0, tiled=True
        ).astype(jnp.float32),
        lax.psum_scatter(
            layout_branch_part.astype(jnp.bfloat16), "mp", scatter_dimension=0, tiled=True
        ).astype(jnp.float32),
    )
    text_final, text_final_back = jax.vjp(
        layer_norm, text_normed + text_branch + text_outbias[1], text_gain[1], text_shift[1]
    )
    layout_final, layout_final_back = jax.vjp(
        layer_norm,
        layout_normed + layout_branch + layout_outbias[1],
        layout_gain[1],
        layout_shift[1],
    )
    text_sum_grad, text_gain_second, text_shift_second = text_final_back(
        text_cotan.astype(jnp.float32)
    )
    layout_sum_grad, layout_gain_second, layout_shift_second = layout_final_back(
        layout_cotan.astype(jnp.float32)
    )
    text_branch_grad = text_sum_grad.astype(jnp.bfloat16)
    layout_branch_grad = layout_sum_grad.astype(jnp.bfloat16)
    text_full_grad, layout_full_grad = (
        lax.all_gather(text_branch_grad, "mp", axis=0, tiled=True),
        lax.all_gather(layout_branch_grad, "mp", axis=0, tiled=True),
    )
    n_dp = lax.axis_size("dp")
    n_mp = lax.axis_size("mp")
    per_dest = D // n_dp
    ffn_orders = chain_orders(n_dp, 2)
    tail_orders = chain_orders(n_dp, 3 if per_dest % 3 == 0 else 1)
    text_wup_grad, text_upbias_grad, text_wdown_grad_t, text_normed_part = feed_back(
        text_full,
        text_active,
        text_gelu_back,
        text_full_grad,
        text_wup,
        text_wdown,
        "rf,rd->df",
        up_rows=permute_columns(text_full, ffn_orders[:1], n_dp),
        down_rows=permute_columns(text_full_grad, ffn_orders[1:], n_dp),
    )
    wup_share = reduce_permuted(text_wup_grad, ffn_orders[:1], n_dp, jnp.bfloat16)
    wdown_share_t = reduce_permuted(text_wdown_grad_t, ffn_orders[1:], n_dp, jnp.bfloat16)
    layout_wup_grad, layout_upbias_grad, layout_wdown_grad, layout_normed_part = feed_back(
        layout_full, layout_active, layout_gelu_back, layout_full_grad, layout_wup, layout_wdown
    )
    small_early = xor_sum(
        jnp.concatenate(
            [
                jnp.sum(text_branch_grad, axis=0, dtype=jnp.float32),
                text_gain_second,
                text_shift_second,
                jnp.sum(layout_branch_grad, axis=0, dtype=jnp.float32),
                layout_gain_second,
                layout_shift_second,
            ]
        ),
        "mp",
        n_mp,
    )
    early = (text_upbias_grad, layout_wup_grad, layout_upbias_grad, layout_wdown_grad, small_early)
    early_out = reduce_replicated(early, n_dp, jnp.bfloat16, ffn_orders[0])
    text_normed_grad, layout_normed_grad = (
        lax.psum_scatter(
            text_normed_part.astype(jnp.bfloat16), "mp", scatter_dimension=0, tiled=True
        ).astype(jnp.float32),
        lax.psum_scatter(
            layout_normed_part.astype(jnp.bfloat16), "mp", scatter_dimension=0, tiled=True
        ).astype(jnp.float32),
    )
    text_mixed_grad, text_gain_first, text_shift_first = text_first_back(
        text_normed_grad + text_sum_grad
    )
    layout_mixed_grad, layout_gain_first, layout_shift_first = layout_first_back(
        layout_normed_grad + layout_sum_grad
    )
    text_mixed_low = text_mixed_grad.astype(jnp.bfloat16)
    layout_mixed_low = layout_mixed_grad.astype(jnp.bfloat16)
    text_wide_grad, layout_wide_grad = (
        lax.all_gather(text_mixed_low, "mp", axis=0, tiled=True),
        lax.all_gather(layout_mixed_low, "mp", axis=0, tiled=True),
    )
    text_context_grad = jnp.einsum(
        "rd,ed->re", text_wide_grad, text_wout, preferred_element_type=jnp.float32
    ).astype(jnp.bfloat16)
    layout_context_grad = jnp.einsum(
        "rd,ed->re", layout_wide_grad, layout_wout, preferred_element_type=jnp.float32
    ).astype(jnp.bfloat16)
    text_wout_grad_t = jnp.einsum(
        "re,rd->de",
        text_context,
        permute_columns(text_wide_grad, tail_orders, n_dp),
        preferred_element_type=jnp.float32,
    )
    layout_wout_grad = jnp.einsum(
        "re,rd->ed", layout_context, layout_wide_grad, preferred_element_type=jnp.float32
    )
    back_blocks = blocks + (
        log_totals,
        blocked(text_context_grad, text_head),
        blocked(layout_context_grad, layout_head),
    )
    text_qgrad, text_kgrad, text_vgrad, layout_qgrad, layout_kgrad, layout_vgrad = lax.map(
        attend_back, back_blocks
    )
    text_qkv_grad_t, text_qvbias_grad, text_input_part = input_back(
        text_rows,
        text_qkv,
        unblocked(text_qgrad),
        unblocked(text_kgrad),
        unblocked(text_vgrad),
        stack_axis=1,
        grad_rows=permute_columns(text_rows, tail_orders, n_dp),
    )
    layout_qkv_grad, layout_qvbias_grad, layout_input_part = input_back(
        layout_rows,
        layout_qkv,
        unblocked(layout_qgrad),
        unblocked(layout_kgrad),
        unblocked(layout_vgrad),
    )
    text_input_sum, layout_input_sum = (
        lax.psum_scatter(
            text_input_part.astype(jnp.bfloat16), "mp", scatter_dimension=0, tiled=True
        ).astype(jnp.float32),
        lax.psum_scatter(
            layout_input_part.astype(jnp.bfloat16), "mp", scatter_dimension=0, tiled=True
        ).astype(jnp.float32),
    )
    text_dinput = (text_mixed_grad + text_input_sum).astype(jnp.bfloat16)
    layout_dinput = (layout_mixed_grad + layout_input_sum).astype(jnp.bfloat16)
    small_late = xor_sum(
        jnp.concatenate(
            [
                jnp.sum(text_mixed_low, axis=0, dtype=jnp.float32),
                text_gain_first,
                text_shift_first,
                jnp.sum(layout_mixed_low, axis=0, dtype=jnp.float32),
                layout_gain_first,
                layout_shift_first,
            ]
        ),
        "mp",
        n_mp,
    )
    late = (text_qvbias_grad, layout_qkv_grad, layout_qvbias_grad, layout_wout_grad, small_late)
    stacked = jnp.concatenate([text_qkv_grad_t, text_wout_grad_t[:, None, :]], axis=1)
    qkv_out = reduce_permuted(stacked, tail_orders, n_dp, jnp.bfloat16)
    late_out = reduce_replicated(late, n_dp, jnp.bfloat16, tail_orders[-1])
    qkv_share = jnp.transpose(qkv_out[:, :3], (1, 0, 2))
    wout_share = qkv_out[:, 3].T
    wdown_share = wdown_share_t.T
    summed = (
        late_out[0],
        early_out[0],
        late_out[1],
        late_out[2],
        late_out[3],
        early_out[1],
        early_out[2],
        early_out[3],
    )

    def pair(first, second, width, at):
        return jnp.stack([first[at * width : (at + 1) * width], second[at * width : (at + 1) * width]])

    text_small = (late_out[4][: 3 * D], early_out[4][: 3 * D])
    layout_small = (late_out[4][3 * D :], early_out[4][3 * D :])
    shared = [pair(*text_small, D, at) for at in range(3)] + [
        pair(*layout_small, DL, at) for at in range(3)
    ]
    return (
        text_final.astype(jnp.bfloat16),
        layout_final.astype(jnp.bfloat16),
        text_dinput,
        layout_dinput,
        qkv_share,
        summed[0],
        wout_share,
        shared[0],
        wup_share,
        summed[1],
        wdown_share,
        shared[1],
        shared[2],
        summed[2],
        summed[3],
        summed[4],
        shared[3],
        summed[5],
        summed[6],
        summed[7],
        shared[4],
        shared[5],
    )


def solution(mesh):
    in_specs = (
        P(("dp", "mp"), None),
        P(("dp", "mp"), None),
        P("dp"),
        P("dp"),
        P(None, None, "mp"),
        P(None, "mp"),
        P("mp", None),
        P(),
        P(None, "mp"),
        P("mp"),
        P("mp", None),
        P(),
        P(),
        P(None, None, "mp"),
        P(None, "mp"),
        P("mp", None),
        P(),
        P(None, "mp"),
        P("mp"),
        P("mp", None),
        P(),
        P(),
        P(("dp", "mp"), None),
        P(("dp", "mp"), None),
    )
    out_specs = (
        P(("dp", "mp"), None),
        P(("dp", "mp"), None),
        P(("dp", "mp"), None),
        P(("dp", "mp"), None),
        P(None, "dp", "mp"),
        P(None, "mp"),
        P("mp", "dp"),
        P(),
        P("dp", "mp"),
        P("mp"),
        P("mp", "dp"),
        P(),
        P(),
        P(None, None, "mp"),
        P(None, "mp"),
        P("mp", None),
        P(),
        P(None, "mp"),
        P("mp"),
        P("mp", None),
        P(),
        P(),
    )
    return jax.shard_map(layer_body, mesh=mesh, in_specs=in_specs, out_specs=out_specs, check_vma=False)
```

```python
import jax
import jax.numpy as jnp
from jax import lax
from jax.sharding import PartitionSpec as P

D = 768
H = 12
DL = 192
WINDOW = 512


EPSILON = 1e-05
MASKED = -1000000000.0


def layer_norm(values, gain, shift):
    centered = values - jnp.mean(values, axis=-1, keepdims=True)
    variance = jnp.mean(centered * centered, axis=-1, keepdims=True)
    return centered * lax.rsqrt(variance + EPSILON) * gain + shift


def gelu(values):
    return 0.5 * values * (1.0 + lax.erf(values * 0.7071067811865476))


def project_path(rows, weight_qkv, biases):
    joined = jnp.einsum("rd,kde->kre", rows, weight_qkv, preferred_element_type=jnp.float32)
    queries = (joined[0] + biases[0]).astype(jnp.bfloat16)
    key_rows = joined[1].astype(jnp.bfloat16)
    value_rows = (joined[2] + biases[1]).astype(jnp.bfloat16)
    return (queries, key_rows, value_rows)


def blocked(values, head_size):
    return values.reshape(-1, WINDOW, values.shape[-1] // head_size, head_size)


def unblocked(values):
    return values.reshape(-1, values.shape[-2] * values.shape[-1])


def coupled_scores(text_queries, text_keys, layout_queries, layout_keys, usable):
    scores = jnp.einsum(
        "qhd,khd->hqk", text_queries, text_keys, preferred_element_type=jnp.float32
    ) * (D // H) ** (-0.5)
    scores = scores + jnp.einsum(
        "qhd,khd->hqk", layout_queries, layout_keys, preferred_element_type=jnp.float32
    ) * (DL // H) ** (-0.5)
    return jnp.where(usable[None, None, :], scores, MASKED)


def attend_window(pieces):
    text_queries, text_keys, text_values, layout_queries, layout_keys, layout_values, usable = (
        pieces
    )
    scores = coupled_scores(text_queries, text_keys, layout_queries, layout_keys, usable)
    peak = jnp.max(scores, axis=-1, keepdims=True)
    powers = jnp.exp(scores - peak)
    total = jnp.sum(powers, axis=-1, keepdims=True)
    probs = (powers / total).astype(jnp.bfloat16)
    text_context = jnp.einsum(
        "hqk,khd->qhd", probs, text_values, preferred_element_type=jnp.float32
    ).astype(jnp.bfloat16)
    layout_context = jnp.einsum(
        "hqk,khd->qhd", probs, layout_values, preferred_element_type=jnp.float32
    ).astype(jnp.bfloat16)
    return (text_context, layout_context, peak + jnp.log(total))


def attend_back(pieces):
    (
        text_queries,
        text_keys,
        text_values,
        layout_queries,
        layout_keys,
        layout_values,
        usable,
        log_totals,
        text_cgrad,
        layout_cgrad,
    ) = pieces
    text_scale = (D // H) ** (-0.5)
    layout_scale = (DL // H) ** (-0.5)
    scores = coupled_scores(text_queries, text_keys, layout_queries, layout_keys, usable)
    probs = jnp.exp(scores - log_totals)
    probs_low = probs.astype(jnp.bfloat16)
    probs_grad = jnp.einsum(
        "qhd,khd->hqk", text_cgrad, text_values, preferred_element_type=jnp.float32
    )
    probs_grad = probs_grad + jnp.einsum(
        "qhd,khd->hqk", layout_cgrad, layout_values, preferred_element_type=jnp.float32
    )
    scores_grad = (
        probs * (probs_grad - jnp.sum(probs_grad * probs, axis=-1, keepdims=True))
    ).astype(jnp.bfloat16)
    text_vgrad = jnp.einsum(
        "hqk,qhd->khd", probs_low, text_cgrad, preferred_element_type=jnp.float32
    ).astype(jnp.bfloat16)
    layout_vgrad = jnp.einsum(
        "hqk,qhd->khd", probs_low, layout_cgrad, preferred_element_type=jnp.float32
    ).astype(jnp.bfloat16)
    text_qgrad = (
        jnp.einsum("hqk,khd->qhd", scores_grad, text_keys, preferred_element_type=jnp.float32)
        * text_scale
    ).astype(jnp.bfloat16)
    text_kgrad = (
        jnp.einsum("hqk,qhd->khd", scores_grad, text_queries, preferred_element_type=jnp.float32)
        * text_scale
    ).astype(jnp.bfloat16)
    layout_qgrad = (
        jnp.einsum("hqk,khd->qhd", scores_grad, layout_keys, preferred_element_type=jnp.float32)
        * layout_scale
    ).astype(jnp.bfloat16)
    layout_kgrad = (
        jnp.einsum("hqk,qhd->khd", scores_grad, layout_queries, preferred_element_type=jnp.float32)
        * layout_scale
    ).astype(jnp.bfloat16)
    return (text_qgrad, text_kgrad, text_vgrad, layout_qgrad, layout_kgrad, layout_vgrad)


def feed_forward(full_rows, w_up, up_bias, w_down):
    hidden = jnp.dot(full_rows, w_up, preferred_element_type=jnp.float32) + up_bias
    active, gelu_back = jax.vjp(gelu, hidden)
    active_low = active.astype(jnp.bfloat16)
    return (active_low, gelu_back, jnp.dot(active_low, w_down, preferred_element_type=jnp.float32))


def feed_back(
    full_rows, active_low, gelu_back, full_grad, w_up, w_down, down_spec="rf,rd->fd", up_rows=None, down_rows=None
):
    up_rows = full_rows if up_rows is None else up_rows
    down_rows = full_grad if down_rows is None else down_rows
    grad_down = jnp.einsum(down_spec, active_low, down_rows, preferred_element_type=jnp.float32)
    active_grad = jnp.einsum("rd,fd->rf", full_grad, w_down, preferred_element_type=jnp.float32)
    hidden_grad = gelu_back(active_grad)[0].astype(jnp.bfloat16)
    grad_up = jnp.einsum("rd,rf->df", up_rows, hidden_grad, preferred_element_type=jnp.float32)
    grad_bias = jnp.sum(hidden_grad, axis=0, dtype=jnp.float32)
    normed_part = jnp.einsum("rf,df->rd", hidden_grad, w_up, preferred_element_type=jnp.float32)
    return (grad_up, grad_bias, grad_down, normed_part)


def input_back(rows, weight_qkv, query_grad, key_grad, value_grad, stack_axis=0, grad_rows=None):
    grad_rows = rows if grad_rows is None else grad_rows
    grad_qkv = jnp.stack(
        [
            jnp.einsum("rd,re->de", grad_rows, piece, preferred_element_type=jnp.float32)
            for piece in (query_grad, key_grad, value_grad)
        ],
        axis=stack_axis,
    )
    input_part = jnp.einsum(
        "re,de->rd", query_grad, weight_qkv[0], preferred_element_type=jnp.float32
    )
    input_part = input_part + jnp.einsum(
        "re,de->rd", key_grad, weight_qkv[1], preferred_element_type=jnp.float32
    )
    input_part = input_part + jnp.einsum(
        "re,de->rd", value_grad, weight_qkv[2], preferred_element_type=jnp.float32
    )
    grad_bias = jnp.stack(
        [
            jnp.sum(query_grad, axis=0, dtype=jnp.float32),
            jnp.sum(value_grad, axis=0, dtype=jnp.float32),
        ]
    )
    return (grad_qkv, grad_bias, input_part)


def xor_sum(values, axis, size):
    step = 1
    while step < size:
        values = values + lax.ppermute(
            values, axis, [(i, i ^ step) for i in range(size)]
        )
        step *= 2
    return values


def xor_exchange(values, step, size):
    return lax.ppermute(values, "dp", [(i, i ^ step) for i in range(size)])


def bit_orders(bits, colours):
    if bits <= 1:
        return [list(range(bits))] * colours
    main = list(range(bits - 1))
    orders = []
    for colour in range(colours):
        shift = colour % len(main)
        orders.append(main[shift:] + main[:shift] + [bits - 1])
    return orders


def halve(chunk, order, me, size, wire):
    for bit in order:
        mine = (me >> bit) & 1
        keep = lax.dynamic_index_in_dim(chunk, mine, axis=0, keepdims=False)
        send = lax.dynamic_index_in_dim(chunk, 1 - mine, axis=0, keepdims=False)
        chunk = keep + xor_exchange(send.astype(wire), 1 << bit, size).astype(chunk.dtype)
    return chunk


def double(block, order, me, size, bits):
    held = []
    for bit in reversed(order):
        other = xor_exchange(block, 1 << bit, size)
        mine = (me >> bit) & 1
        block = jnp.where(mine == 0, jnp.stack([block, other]), jnp.stack([other, block]))
        held.insert(0, bit)
    canonical = list(range(bits - 1, -1, -1))
    rest = list(range(len(held), block.ndim))
    block = jnp.transpose(block, [held.index(bit) for bit in canonical] + rest)
    return block.reshape((-1,) + block.shape[len(held) + 1 :])


def ordered(piece, order, size, bits):
    shaped = piece.reshape((2,) * bits + (piece.shape[0] // size,) + piece.shape[1:])
    canonical = list(range(bits - 1, -1, -1))
    rest = list(range(bits, shaped.ndim))
    return jnp.transpose(shaped, [canonical.index(bit) for bit in order] + rest)


def chain_orders(size, colours):
    bits = size.bit_length() - 1
    return bit_orders(bits, colours)[:colours]


def permute_columns(values, orders, size):
    bits = size.bit_length() - 1
    colours = len(orders)
    lead = values.shape[:-1]
    n = len(lead)
    per = values.shape[-1] // size
    shaped = values.reshape(lead + (2,) * bits + (colours, per // colours))
    canonical = list(range(bits - 1, -1, -1))
    parts = []
    for colour, order in enumerate(orders):
        part = lax.index_in_dim(shaped, colour, axis=n + bits, keepdims=False)
        axes = list(range(n)) + [n + canonical.index(bit) for bit in order] + [n + bits]
        parts.append(jnp.transpose(part, axes))
    return jnp.stack(parts, axis=n).reshape(values.shape)


def reduce_permuted(grad, orders, size, wire):
    bits = size.bit_length() - 1
    me = lax.axis_index("dp")
    colours = len(orders)
    per = grad.shape[0] // size
    shaped = grad.reshape((colours,) + (2,) * bits + (per // colours,) + grad.shape[1:])
    return jnp.concatenate(
        [halve(shaped[colour], orders[colour], me, size, wire) for colour in range(colours)]
    )


def dp_reduce(scattered, colours_of, replicated, size, wire, lanes=128):
    bits = size.bit_length() - 1
    me = lax.axis_index("dp")
    orders = bit_orders(bits, 3)
    scattered_out = []
    for piece, colour in zip(scattered, colours_of):
        scattered_out.append(reduce_permuted(piece, [orders[colour]], size, wire))
    blocks = []
    for piece in replicated:
        flat = piece.reshape(-1)
        flat = jnp.pad(flat, (0, (-flat.shape[0]) % lanes))
        blocks.append(flat.reshape(-1, lanes))
    joined = jnp.concatenate(blocks)
    rows = joined.shape[0]
    joined = jnp.pad(joined, ((0, (-rows) % (size * 8)), (0, 0)))
    chunk = ordered(joined, orders[0], size, bits)
    block = halve(chunk, orders[0], me, size, wire)
    full = double(block, orders[0], me, size, bits)
    replicated_out = []
    offset = 0
    for piece in replicated:
        count = -(-piece.size // lanes)
        replicated_out.append(
            full[offset : offset + count].reshape(-1)[: piece.size].reshape(piece.shape)
        )
        offset += count
    return scattered_out, replicated_out

def body(
    text_input,
    layout_input,
    repeated,
    key_mask,
    text_qkv,
    text_qvbias,
    text_wout,
    text_outbias,
    text_wup,
    text_upbias,
    text_wdown,
    text_gains,
    text_shifts,
    layout_qkv,
    layout_qvbias,
    layout_wout,
    layout_outbias,
    layout_wup,
    layout_upbias,
    layout_wdown,
    layout_gains,
    layout_shifts,
    text_cotan,
    layout_cotan,
):
    text_head = D // H
    layout_head = DL // H
    usable_group = jnp.logical_and(key_mask == 1, repeated == 0).reshape(-1, WINDOW)
    text_rows, layout_rows = (
        lax.all_gather(text_input, "mp", axis=0, tiled=True),
        lax.all_gather(layout_input, "mp", axis=0, tiled=True),
    )
    text_queries, text_keys, text_values = project_path(text_rows, text_qkv, text_qvbias)
    layout_queries, layout_keys, layout_values = project_path(
        layout_rows, layout_qkv, layout_qvbias
    )
    blocks = (
        blocked(text_queries, text_head),
        blocked(text_keys, text_head),
        blocked(text_values, text_head),
        blocked(layout_queries, layout_head),
        blocked(layout_keys, layout_head),
        blocked(layout_values, layout_head),
        usable_group,
    )
    text_context, layout_context, log_totals = lax.map(attend_window, blocks)
    text_context = unblocked(text_context)
    layout_context = unblocked(layout_context)
    text_mixed_part = jnp.dot(text_context, text_wout, preferred_element_type=jnp.float32)
    layout_mixed_part = jnp.dot(layout_context, layout_wout, preferred_element_type=jnp.float32)
    text_mixed, layout_mixed = (
        lax.psum_scatter(
            text_mixed_part.astype(jnp.bfloat16), "mp", scatter_dimension=0, tiled=True
        ).astype(jnp.float32),
        lax.psum_scatter(
            layout_mixed_part.astype(jnp.bfloat16), "mp", scatter_dimension=0, tiled=True
        ).astype(jnp.float32),
    )
    text_gain = text_gains.astype(jnp.float32)
    text_shift = text_shifts.astype(jnp.float32)
    layout_gain = layout_gains.astype(jnp.float32)
    layout_shift = layout_shifts.astype(jnp.float32)
    text_normed, text_first_back = jax.vjp(
        layer_norm,
        text_input.astype(jnp.float32) + text_mixed + text_outbias[0],
        text_gain[0],
        text_shift[0],
    )
    layout_normed, layout_first_back = jax.vjp(
        layer_norm,
        layout_input.astype(jnp.float32) + layout_mixed + layout_outbias[0],
        layout_gain[0],
        layout_shift[0],
    )
    text_full, layout_full = (
        lax.all_gather(text_normed.astype(jnp.bfloat16), "mp", axis=0, tiled=True),
        lax.all_gather(layout_normed.astype(jnp.bfloat16), "mp", axis=0, tiled=True),
    )
    text_active, text_gelu_back, text_branch_part = feed_forward(
        text_full, text_wup, text_upbias, text_wdown
    )
    layout_active, layout_gelu_back, layout_branch_part = feed_forward(
        layout_full, layout_wup, layout_upbias, layout_wdown
    )
    text_branch, layout_branch = (
        lax.psum_scatter(
            text_branch_part.astype(jnp.bfloat16), "mp", scatter_dimension=0, tiled=True
        ).astype(jnp.float32),
        lax.psum_scatter(
            layout_branch_part.astype(jnp.bfloat16), "mp", scatter_dimension=0, tiled=True
        ).astype(jnp.float32),
    )
    text_final, text_final_back = jax.vjp(
        layer_norm, text_normed + text_branch + text_outbias[1], text_gain[1], text_shift[1]
    )
    layout_final, layout_final_back = jax.vjp(
        layer_norm,
        layout_normed + layout_branch + layout_outbias[1],
        layout_gain[1],
        layout_shift[1],
    )
    text_sum_grad, text_gain_second, text_shift_second = text_final_back(
        text_cotan.astype(jnp.float32)
    )
    layout_sum_grad, layout_gain_second, layout_shift_second = layout_final_back(
        layout_cotan.astype(jnp.float32)
    )
    text_branch_grad = text_sum_grad.astype(jnp.bfloat16)
    layout_branch_grad = layout_sum_grad.astype(jnp.bfloat16)
    text_full_grad, layout_full_grad = (
        lax.all_gather(text_branch_grad, "mp", axis=0, tiled=True),
        lax.all_gather(layout_branch_grad, "mp", axis=0, tiled=True),
    )
    n_dp = lax.axis_size("dp")
    orders = chain_orders(n_dp, 3)
    text_wup_grad, text_upbias_grad, text_wdown_grad_t, text_normed_part = feed_back(
        text_full,
        text_active,
        text_gelu_back,
        text_full_grad,
        text_wup,
        text_wdown,
        "rf,rd->df",
        up_rows=permute_columns(text_full, [orders[0]], n_dp),
        down_rows=permute_columns(text_full_grad, [orders[1]], n_dp),
    )
    layout_wup_grad, layout_upbias_grad, layout_wdown_grad, layout_normed_part = feed_back(
        layout_full, layout_active, layout_gelu_back, layout_full_grad, layout_wup, layout_wdown
    )
    text_normed_grad, layout_normed_grad = (
        lax.psum_scatter(
            text_normed_part.astype(jnp.bfloat16), "mp", scatter_dimension=0, tiled=True
        ).astype(jnp.float32),
        lax.psum_scatter(
            layout_normed_part.astype(jnp.bfloat16), "mp", scatter_dimension=0, tiled=True
        ).astype(jnp.float32),
    )
    text_mixed_grad, text_gain_first, text_shift_first = text_first_back(
        text_normed_grad + text_sum_grad
    )
    layout_mixed_grad, layout_gain_first, layout_shift_first = layout_first_back(
        layout_normed_grad + layout_sum_grad
    )
    text_mixed_low = text_mixed_grad.astype(jnp.bfloat16)
    layout_mixed_low = layout_mixed_grad.astype(jnp.bfloat16)
    text_wide_grad, layout_wide_grad = (
        lax.all_gather(text_mixed_low, "mp", axis=0, tiled=True),
        lax.all_gather(layout_mixed_low, "mp", axis=0, tiled=True),
    )
    text_wout_grad_t = jnp.einsum(
        "re,rd->de",
        text_context,
        permute_columns(text_wide_grad, [orders[2]], n_dp),
        preferred_element_type=jnp.float32,
    )
    layout_wout_grad = jnp.einsum(
        "re,rd->ed", layout_context, layout_wide_grad, preferred_element_type=jnp.float32
    )
    text_context_grad = jnp.einsum(
        "rd,ed->re", text_wide_grad, text_wout, preferred_element_type=jnp.float32
    ).astype(jnp.bfloat16)
    layout_context_grad = jnp.einsum(
        "rd,ed->re", layout_wide_grad, layout_wout, preferred_element_type=jnp.float32
    ).astype(jnp.bfloat16)
    back_blocks = blocks + (
        log_totals,
        blocked(text_context_grad, text_head),
        blocked(layout_context_grad, layout_head),
    )
    text_qgrad, text_kgrad, text_vgrad, layout_qgrad, layout_kgrad, layout_vgrad = lax.map(
        attend_back, back_blocks
    )
    text_qkv_grad_t, text_qvbias_grad, text_input_part = input_back(
        text_rows,
        text_qkv,
        unblocked(text_qgrad),
        unblocked(text_kgrad),
        unblocked(text_vgrad),
        stack_axis=1,
        grad_rows=permute_columns(text_rows, [orders[2]], n_dp),
    )
    layout_qkv_grad, layout_qvbias_grad, layout_input_part = input_back(
        layout_rows,
        layout_qkv,
        unblocked(layout_qgrad),
        unblocked(layout_kgrad),
        unblocked(layout_vgrad),
    )
    text_input_sum, layout_input_sum = (
        lax.psum_scatter(
            text_input_part.astype(jnp.bfloat16), "mp", scatter_dimension=0, tiled=True
        ).astype(jnp.float32),
        lax.psum_scatter(
            layout_input_part.astype(jnp.bfloat16), "mp", scatter_dimension=0, tiled=True
        ).astype(jnp.float32),
    )
    text_dinput = (text_mixed_grad + text_input_sum).astype(jnp.bfloat16)
    layout_dinput = (layout_mixed_grad + layout_input_sum).astype(jnp.bfloat16)
    n_mp = lax.axis_size("mp")
    small = jnp.concatenate(
        [
            part.reshape(-1)
            for part in (
                jnp.stack(
                    [
                        jnp.sum(text_mixed_low, axis=0, dtype=jnp.float32),
                        jnp.sum(text_branch_grad, axis=0, dtype=jnp.float32),
                    ]
                ),
                jnp.stack([text_gain_first, text_gain_second]),
                jnp.stack([text_shift_first, text_shift_second]),
                jnp.stack(
                    [
                        jnp.sum(layout_mixed_low, axis=0, dtype=jnp.float32),
                        jnp.sum(layout_branch_grad, axis=0, dtype=jnp.float32),
                    ]
                ),
                jnp.stack([layout_gain_first, layout_gain_second]),
                jnp.stack([layout_shift_first, layout_shift_second]),
            )
        ]
    )
    small = xor_sum(small, "mp", n_mp)
    scattered = (
        jnp.concatenate([text_qkv_grad_t, text_wout_grad_t[:, None, :]], axis=1),
        text_wup_grad,
        text_wdown_grad_t,
    )
    replicated = (
        text_qvbias_grad,
        text_upbias_grad,
        layout_qkv_grad,
        layout_qvbias_grad,
        layout_wout_grad,
        layout_wup_grad,
        layout_upbias_grad,
        layout_wdown_grad,
        small,
    )
    scattered, replicated = lax.optimization_barrier((scattered, replicated))
    scattered_out, replicated_out = dp_reduce(
        scattered, (2, 0, 1), replicated, n_dp, jnp.bfloat16
    )
    qkv_share = jnp.transpose(scattered_out[0][:, :3], (1, 0, 2))
    wout_share = scattered_out[0][:, 3].T
    wup_share = scattered_out[1]
    wdown_share = scattered_out[2].T
    summed = replicated_out[:8]
    small_sum = replicated_out[8]
    sizes = (2 * D, 2 * D, 2 * D, 2 * DL, 2 * DL, 2 * DL)
    shared = []
    offset = 0
    for size in sizes:
        shared.append(small_sum[offset : offset + size].reshape(2, -1))
        offset += size
    return (
        text_final.astype(jnp.bfloat16),
        layout_final.astype(jnp.bfloat16),
        text_dinput,
        layout_dinput,
        qkv_share,
        summed[0],
        wout_share,
        shared[0],
        wup_share,
        summed[1],
        wdown_share,
        shared[1],
        shared[2],
        summed[2],
        summed[3],
        summed[4],
        shared[3],
        summed[5],
        summed[6],
        summed[7],
        shared[4],
        shared[5],
    )


def solution(mesh):
    in_specs = (
        P(("dp", "mp"), None),
        P(("dp", "mp"), None),
        P("dp"),
        P("dp"),
        P(None, None, "mp"),
        P(None, "mp"),
        P("mp", None),
        P(),
        P(None, "mp"),
        P("mp"),
        P("mp", None),
        P(),
        P(),
        P(None, None, "mp"),
        P(None, "mp"),
        P("mp", None),
        P(),
        P(None, "mp"),
        P("mp"),
        P("mp", None),
        P(),
        P(),
        P(("dp", "mp"), None),
        P(("dp", "mp"), None),
    )
    out_specs = (
        P(("dp", "mp"), None),
        P(("dp", "mp"), None),
        P(("dp", "mp"), None),
        P(("dp", "mp"), None),
        P(None, "dp", "mp"),
        P(None, "mp"),
        P("mp", "dp"),
        P(),
        P("dp", "mp"),
        P("mp"),
        P("mp", "dp"),
        P(),
        P(),
        P(None, None, "mp"),
        P(None, "mp"),
        P("mp", None),
        P(),
        P(None, "mp"),
        P("mp"),
        P("mp", None),
        P(),
        P(),
    )
    return jax.shard_map(body, mesh=mesh, in_specs=in_specs, out_specs=out_specs, check_vma=False)
```

```python
import jax
import jax.numpy as jnp
from jax import lax
from jax.sharding import PartitionSpec as P

D = 768
H = 12
DL = 192
WINDOW = 512


EPSILON = 1e-05
MASKED = -1000000000.0


def layer_norm(values, gain, shift):
    centered = values - jnp.mean(values, axis=-1, keepdims=True)
    variance = jnp.mean(centered * centered, axis=-1, keepdims=True)
    return centered * lax.rsqrt(variance + EPSILON) * gain + shift


def gelu(values):
    return 0.5 * values * (1.0 + lax.erf(values * 0.7071067811865476))


def project_path(rows, weight_qkv, biases):
    joined = jnp.einsum("rd,kde->kre", rows, weight_qkv, preferred_element_type=jnp.float32)
    queries = (joined[0] + biases[0]).astype(jnp.bfloat16)
    key_rows = joined[1].astype(jnp.bfloat16)
    value_rows = (joined[2] + biases[1]).astype(jnp.bfloat16)
    return (queries, key_rows, value_rows)


def blocked(values, head_size):
    return values.reshape(-1, WINDOW, values.shape[-1] // head_size, head_size)


def unblocked(values):
    return values.reshape(-1, values.shape[-2] * values.shape[-1])


def coupled_scores(text_queries, text_keys, layout_queries, layout_keys, usable):
    scores = jnp.einsum(
        "qhd,khd->hqk", text_queries, text_keys, preferred_element_type=jnp.float32
    ) * (D // H) ** (-0.5)
    scores = scores + jnp.einsum(
        "qhd,khd->hqk", layout_queries, layout_keys, preferred_element_type=jnp.float32
    ) * (DL // H) ** (-0.5)
    return jnp.where(usable[None, None, :], scores, MASKED)


def attend_window(pieces):
    text_queries, text_keys, text_values, layout_queries, layout_keys, layout_values, usable = (
        pieces
    )
    scores = coupled_scores(text_queries, text_keys, layout_queries, layout_keys, usable)
    peak = jnp.max(scores, axis=-1, keepdims=True)
    powers = jnp.exp(scores - peak)
    total = jnp.sum(powers, axis=-1, keepdims=True)
    probs = (powers / total).astype(jnp.bfloat16)
    text_context = jnp.einsum(
        "hqk,khd->qhd", probs, text_values, preferred_element_type=jnp.float32
    ).astype(jnp.bfloat16)
    layout_context = jnp.einsum(
        "hqk,khd->qhd", probs, layout_values, preferred_element_type=jnp.float32
    ).astype(jnp.bfloat16)
    return (text_context, layout_context, peak + jnp.log(total))


def attend_back(pieces):
    (
        text_queries,
        text_keys,
        text_values,
        layout_queries,
        layout_keys,
        layout_values,
        usable,
        log_totals,
        text_cgrad,
        layout_cgrad,
    ) = pieces
    text_scale = (D // H) ** (-0.5)
    layout_scale = (DL // H) ** (-0.5)
    scores = coupled_scores(text_queries, text_keys, layout_queries, layout_keys, usable)
    probs = jnp.exp(scores - log_totals)
    probs_low = probs.astype(jnp.bfloat16)
    probs_grad = jnp.einsum(
        "qhd,khd->hqk", text_cgrad, text_values, preferred_element_type=jnp.float32
    )
    probs_grad = probs_grad + jnp.einsum(
        "qhd,khd->hqk", layout_cgrad, layout_values, preferred_element_type=jnp.float32
    )
    scores_grad = (
        probs * (probs_grad - jnp.sum(probs_grad * probs, axis=-1, keepdims=True))
    ).astype(jnp.bfloat16)
    text_vgrad = jnp.einsum(
        "hqk,qhd->khd", probs_low, text_cgrad, preferred_element_type=jnp.float32
    ).astype(jnp.bfloat16)
    layout_vgrad = jnp.einsum(
        "hqk,qhd->khd", probs_low, layout_cgrad, preferred_element_type=jnp.float32
    ).astype(jnp.bfloat16)
    text_qgrad = (
        jnp.einsum("hqk,khd->qhd", scores_grad, text_keys, preferred_element_type=jnp.float32)
        * text_scale
    ).astype(jnp.bfloat16)
    text_kgrad = (
        jnp.einsum("hqk,qhd->khd", scores_grad, text_queries, preferred_element_type=jnp.float32)
        * text_scale
    ).astype(jnp.bfloat16)
    layout_qgrad = (
        jnp.einsum("hqk,khd->qhd", scores_grad, layout_keys, preferred_element_type=jnp.float32)
        * layout_scale
    ).astype(jnp.bfloat16)
    layout_kgrad = (
        jnp.einsum("hqk,qhd->khd", scores_grad, layout_queries, preferred_element_type=jnp.float32)
        * layout_scale
    ).astype(jnp.bfloat16)
    return (text_qgrad, text_kgrad, text_vgrad, layout_qgrad, layout_kgrad, layout_vgrad)


def feed_forward(full_rows, w_up, up_bias, w_down):
    hidden = jnp.dot(full_rows, w_up, preferred_element_type=jnp.float32) + up_bias
    active, gelu_back = jax.vjp(gelu, hidden)
    active_low = active.astype(jnp.bfloat16)
    return (active_low, gelu_back, jnp.dot(active_low, w_down, preferred_element_type=jnp.float32))


def feed_back(full_rows, active_low, gelu_back, full_grad, w_up, w_down, down_spec="rf,rd->fd"):
    grad_down = jnp.einsum(down_spec, active_low, full_grad, preferred_element_type=jnp.float32)
    active_grad = jnp.einsum("rd,fd->rf", full_grad, w_down, preferred_element_type=jnp.float32)
    hidden_grad = gelu_back(active_grad)[0].astype(jnp.bfloat16)
    grad_up = jnp.einsum("rd,rf->df", full_rows, hidden_grad, preferred_element_type=jnp.float32)
    grad_bias = jnp.sum(hidden_grad, axis=0, dtype=jnp.float32)
    normed_part = jnp.einsum("rf,df->rd", hidden_grad, w_up, preferred_element_type=jnp.float32)
    return (grad_up, grad_bias, grad_down, normed_part)


def input_back(rows, weight_qkv, query_grad, key_grad, value_grad, stack_axis=0):
    grad_qkv = jnp.stack(
        [
            jnp.einsum("rd,re->de", rows, piece, preferred_element_type=jnp.float32)
            for piece in (query_grad, key_grad, value_grad)
        ],
        axis=stack_axis,
    )
    input_part = jnp.einsum(
        "re,de->rd", query_grad, weight_qkv[0], preferred_element_type=jnp.float32
    )
    input_part = input_part + jnp.einsum(
        "re,de->rd", key_grad, weight_qkv[1], preferred_element_type=jnp.float32
    )
    input_part = input_part + jnp.einsum(
        "re,de->rd", value_grad, weight_qkv[2], preferred_element_type=jnp.float32
    )
    grad_bias = jnp.stack(
        [
            jnp.sum(query_grad, axis=0, dtype=jnp.float32),
            jnp.sum(value_grad, axis=0, dtype=jnp.float32),
        ]
    )
    return (grad_qkv, grad_bias, input_part)


def xor_sum(values, axis, size):
    step = 1
    while step < size:
        values = values + lax.ppermute(
            values, axis, [(i, i ^ step) for i in range(size)]
        )
        step *= 2
    return values


def xor_exchange(values, step, size):
    return lax.ppermute(values, "dp", [(i, i ^ step) for i in range(size)])


def bit_orders(bits, colours):
    if bits <= 1:
        return [list(range(bits))] * colours
    main = list(range(bits - 1))
    orders = []
    for colour in range(colours):
        shift = colour % len(main)
        orders.append(main[shift:] + main[:shift] + [bits - 1])
    return orders


def halve(chunk, order, me, size, wire):
    for bit in order:
        mine = (me >> bit) & 1
        keep = lax.dynamic_index_in_dim(chunk, mine, axis=0, keepdims=False)
        send = lax.dynamic_index_in_dim(chunk, 1 - mine, axis=0, keepdims=False)
        chunk = keep + xor_exchange(send.astype(wire), 1 << bit, size).astype(chunk.dtype)
    return chunk


def double(block, order, me, size, bits):
    held = []
    for bit in reversed(order):
        other = xor_exchange(block, 1 << bit, size)
        mine = (me >> bit) & 1
        block = jnp.where(mine == 0, jnp.stack([block, other]), jnp.stack([other, block]))
        held.insert(0, bit)
    canonical = list(range(bits - 1, -1, -1))
    rest = list(range(len(held), block.ndim))
    block = jnp.transpose(block, [held.index(bit) for bit in canonical] + rest)
    return block.reshape((-1,) + block.shape[len(held) + 1 :])


def ordered(piece, order, size, bits):
    shaped = piece.reshape((2,) * bits + (piece.shape[0] // size,) + piece.shape[1:])
    canonical = list(range(bits - 1, -1, -1))
    rest = list(range(bits, shaped.ndim))
    return jnp.transpose(shaped, [canonical.index(bit) for bit in order] + rest)


def dp_reduce(scattered, colours_of, replicated, size, wire, lanes=128):
    bits = size.bit_length() - 1
    me = lax.axis_index("dp")
    orders = bit_orders(bits, 3)
    scattered_out = []
    for piece, colour in zip(scattered, colours_of):
        chunk = ordered(piece, orders[colour], size, bits)
        scattered_out.append(halve(chunk, orders[colour], me, size, wire))
    blocks = []
    for piece in replicated:
        flat = piece.reshape(-1)
        flat = jnp.pad(flat, (0, (-flat.shape[0]) % lanes))
        blocks.append(flat.reshape(-1, lanes))
    joined = jnp.concatenate(blocks)
    rows = joined.shape[0]
    joined = jnp.pad(joined, ((0, (-rows) % (size * 8)), (0, 0)))
    chunk = ordered(joined, orders[0], size, bits)
    block = halve(chunk, orders[0], me, size, wire)
    full = double(block, orders[0], me, size, bits)
    replicated_out = []
    offset = 0
    for piece in replicated:
        count = -(-piece.size // lanes)
        replicated_out.append(
            full[offset : offset + count].reshape(-1)[: piece.size].reshape(piece.shape)
        )
        offset += count
    return scattered_out, replicated_out

def body(
    text_input,
    layout_input,
    repeated,
    key_mask,
    text_qkv,
    text_qvbias,
    text_wout,
    text_outbias,
    text_wup,
    text_upbias,
    text_wdown,
    text_gains,
    text_shifts,
    layout_qkv,
    layout_qvbias,
    layout_wout,
    layout_outbias,
    layout_wup,
    layout_upbias,
    layout_wdown,
    layout_gains,
    layout_shifts,
    text_cotan,
    layout_cotan,
):
    text_head = D // H
    layout_head = DL // H
    usable_group = jnp.logical_and(key_mask == 1, repeated == 0).reshape(-1, WINDOW)
    text_rows, layout_rows = (
        lax.all_gather(text_input, "mp", axis=0, tiled=True),
        lax.all_gather(layout_input, "mp", axis=0, tiled=True),
    )
    text_queries, text_keys, text_values = project_path(text_rows, text_qkv, text_qvbias)
    layout_queries, layout_keys, layout_values = project_path(
        layout_rows, layout_qkv, layout_qvbias
    )
    blocks = (
        blocked(text_queries, text_head),
        blocked(text_keys, text_head),
        blocked(text_values, text_head),
        blocked(layout_queries, layout_head),
        blocked(layout_keys, layout_head),
        blocked(layout_values, layout_head),
        usable_group,
    )
    text_context, layout_context, log_totals = jax.vmap(attend_window)(blocks)
    text_context = unblocked(text_context)
    layout_context = unblocked(layout_context)
    text_mixed_part = jnp.dot(text_context, text_wout, preferred_element_type=jnp.float32)
    layout_mixed_part = jnp.dot(layout_context, layout_wout, preferred_element_type=jnp.float32)
    text_mixed, layout_mixed = (
        lax.psum_scatter(
            text_mixed_part.astype(jnp.bfloat16), "mp", scatter_dimension=0, tiled=True
        ).astype(jnp.float32),
        lax.psum_scatter(
            layout_mixed_part.astype(jnp.bfloat16), "mp", scatter_dimension=0, tiled=True
        ).astype(jnp.float32),
    )
    text_gain = text_gains.astype(jnp.float32)
    text_shift = text_shifts.astype(jnp.float32)
    layout_gain = layout_gains.astype(jnp.float32)
    layout_shift = layout_shifts.astype(jnp.float32)
    text_normed, text_first_back = jax.vjp(
        layer_norm,
        text_input.astype(jnp.float32) + text_mixed + text_outbias[0],
        text_gain[0],
        text_shift[0],
    )
    layout_normed, layout_first_back = jax.vjp(
        layer_norm,
        layout_input.astype(jnp.float32) + layout_mixed + layout_outbias[0],
        layout_gain[0],
        layout_shift[0],
    )
    text_full, layout_full = (
        lax.all_gather(text_normed.astype(jnp.bfloat16), "mp", axis=0, tiled=True),
        lax.all_gather(layout_normed.astype(jnp.bfloat16), "mp", axis=0, tiled=True),
    )
    text_active, text_gelu_back, text_branch_part = feed_forward(
        text_full, text_wup, text_upbias, text_wdown
    )
    layout_active, layout_gelu_back, layout_branch_part = feed_forward(
        layout_full, layout_wup, layout_upbias, layout_wdown
    )
    text_branch, layout_branch = (
        lax.psum_scatter(
            text_branch_part.astype(jnp.bfloat16), "mp", scatter_dimension=0, tiled=True
        ).astype(jnp.float32),
        lax.psum_scatter(
            layout_branch_part.astype(jnp.bfloat16), "mp", scatter_dimension=0, tiled=True
        ).astype(jnp.float32),
    )
    text_final, text_final_back = jax.vjp(
        layer_norm, text_normed + text_branch + text_outbias[1], text_gain[1], text_shift[1]
    )
    layout_final, layout_final_back = jax.vjp(
        layer_norm,
        layout_normed + layout_branch + layout_outbias[1],
        layout_gain[1],
        layout_shift[1],
    )
    text_sum_grad, text_gain_second, text_shift_second = text_final_back(
        text_cotan.astype(jnp.float32)
    )
    layout_sum_grad, layout_gain_second, layout_shift_second = layout_final_back(
        layout_cotan.astype(jnp.float32)
    )
    text_branch_grad = text_sum_grad.astype(jnp.bfloat16)
    layout_branch_grad = layout_sum_grad.astype(jnp.bfloat16)
    text_full_grad, layout_full_grad = (
        lax.all_gather(text_branch_grad, "mp", axis=0, tiled=True),
        lax.all_gather(layout_branch_grad, "mp", axis=0, tiled=True),
    )
    text_wup_grad, text_upbias_grad, text_wdown_grad_t, text_normed_part = feed_back(
        text_full, text_active, text_gelu_back, text_full_grad, text_wup, text_wdown, "rf,rd->df"
    )
    layout_wup_grad, layout_upbias_grad, layout_wdown_grad, layout_normed_part = feed_back(
        layout_full, layout_active, layout_gelu_back, layout_full_grad, layout_wup, layout_wdown
    )
    text_normed_grad, layout_normed_grad = (
        lax.psum_scatter(
            text_normed_part.astype(jnp.bfloat16), "mp", scatter_dimension=0, tiled=True
        ).astype(jnp.float32),
        lax.psum_scatter(
            layout_normed_part.astype(jnp.bfloat16), "mp", scatter_dimension=0, tiled=True
        ).astype(jnp.float32),
    )
    text_mixed_grad, text_gain_first, text_shift_first = text_first_back(
        text_normed_grad + text_sum_grad
    )
    layout_mixed_grad, layout_gain_first, layout_shift_first = layout_first_back(
        layout_normed_grad + layout_sum_grad
    )
    text_mixed_low = text_mixed_grad.astype(jnp.bfloat16)
    layout_mixed_low = layout_mixed_grad.astype(jnp.bfloat16)
    text_wide_grad, layout_wide_grad = (
        lax.all_gather(text_mixed_low, "mp", axis=0, tiled=True),
        lax.all_gather(layout_mixed_low, "mp", axis=0, tiled=True),
    )
    text_wout_grad_t = jnp.einsum(
        "re,rd->de", text_context, text_wide_grad, preferred_element_type=jnp.float32
    )
    layout_wout_grad = jnp.einsum(
        "re,rd->ed", layout_context, layout_wide_grad, preferred_element_type=jnp.float32
    )
    text_context_grad = jnp.einsum(
        "rd,ed->re", text_wide_grad, text_wout, preferred_element_type=jnp.float32
    ).astype(jnp.bfloat16)
    layout_context_grad = jnp.einsum(
        "rd,ed->re", layout_wide_grad, layout_wout, preferred_element_type=jnp.float32
    ).astype(jnp.bfloat16)
    back_blocks = blocks + (
        log_totals,
        blocked(text_context_grad, text_head),
        blocked(layout_context_grad, layout_head),
    )
    text_qgrad, text_kgrad, text_vgrad, layout_qgrad, layout_kgrad, layout_vgrad = jax.vmap(attend_back)(
        back_blocks
    )
    text_qkv_grad_t, text_qvbias_grad, text_input_part = input_back(
        text_rows,
        text_qkv,
        unblocked(text_qgrad),
        unblocked(text_kgrad),
        unblocked(text_vgrad),
        stack_axis=1,
    )
    layout_qkv_grad, layout_qvbias_grad, layout_input_part = input_back(
        layout_rows,
        layout_qkv,
        unblocked(layout_qgrad),
        unblocked(layout_kgrad),
        unblocked(layout_vgrad),
    )
    text_input_sum, layout_input_sum = (
        lax.psum_scatter(
            text_input_part.astype(jnp.bfloat16), "mp", scatter_dimension=0, tiled=True
        ).astype(jnp.float32),
        lax.psum_scatter(
            layout_input_part.astype(jnp.bfloat16), "mp", scatter_dimension=0, tiled=True
        ).astype(jnp.float32),
    )
    text_dinput = (text_mixed_grad + text_input_sum).astype(jnp.bfloat16)
    layout_dinput = (layout_mixed_grad + layout_input_sum).astype(jnp.bfloat16)
    n_dp = lax.axis_size("dp")
    n_mp = lax.axis_size("mp")
    small = jnp.concatenate(
        [
            part.reshape(-1)
            for part in (
                jnp.stack(
                    [
                        jnp.sum(text_mixed_low, axis=0, dtype=jnp.float32),
                        jnp.sum(text_branch_grad, axis=0, dtype=jnp.float32),
                    ]
                ),
                jnp.stack([text_gain_first, text_gain_second]),
                jnp.stack([text_shift_first, text_shift_second]),
                jnp.stack(
                    [
                        jnp.sum(layout_mixed_low, axis=0, dtype=jnp.float32),
                        jnp.sum(layout_branch_grad, axis=0, dtype=jnp.float32),
                    ]
                ),
                jnp.stack([layout_gain_first, layout_gain_second]),
                jnp.stack([layout_shift_first, layout_shift_second]),
            )
        ]
    )
    small = xor_sum(small, "mp", n_mp)
    scattered = (
        jnp.concatenate([text_qkv_grad_t, text_wout_grad_t[:, None, :]], axis=1),
        text_wup_grad,
        text_wdown_grad_t,
    )
    replicated = (
        text_qvbias_grad,
        text_upbias_grad,
        layout_qkv_grad,
        layout_qvbias_grad,
        layout_wout_grad,
        layout_wup_grad,
        layout_upbias_grad,
        layout_wdown_grad,
        small,
    )
    scattered, replicated = lax.optimization_barrier((scattered, replicated))
    scattered_out, replicated_out = dp_reduce(
        scattered, (2, 0, 1), replicated, n_dp, jnp.bfloat16
    )
    qkv_share = jnp.transpose(scattered_out[0][:, :3], (1, 0, 2))
    wout_share = scattered_out[0][:, 3].T
    wup_share = scattered_out[1]
    wdown_share = scattered_out[2].T
    summed = replicated_out[:8]
    small_sum = replicated_out[8]
    sizes = (2 * D, 2 * D, 2 * D, 2 * DL, 2 * DL, 2 * DL)
    shared = []
    offset = 0
    for size in sizes:
        shared.append(small_sum[offset : offset + size].reshape(2, -1))
        offset += size
    return (
        text_final.astype(jnp.bfloat16),
        layout_final.astype(jnp.bfloat16),
        text_dinput,
        layout_dinput,
        qkv_share,
        summed[0],
        wout_share,
        shared[0],
        wup_share,
        summed[1],
        wdown_share,
        shared[1],
        shared[2],
        summed[2],
        summed[3],
        summed[4],
        shared[3],
        summed[5],
        summed[6],
        summed[7],
        shared[4],
        shared[5],
    )


def solution(mesh):
    in_specs = (
        P(("dp", "mp"), None),
        P(("dp", "mp"), None),
        P("dp"),
        P("dp"),
        P(None, None, "mp"),
        P(None, "mp"),
        P("mp", None),
        P(),
        P(None, "mp"),
        P("mp"),
        P("mp", None),
        P(),
        P(),
        P(None, None, "mp"),
        P(None, "mp"),
        P("mp", None),
        P(),
        P(None, "mp"),
        P("mp"),
        P("mp", None),
        P(),
        P(),
        P(("dp", "mp"), None),
        P(("dp", "mp"), None),
    )
    out_specs = (
        P(("dp", "mp"), None),
        P(("dp", "mp"), None),
        P(("dp", "mp"), None),
        P(("dp", "mp"), None),
        P(None, "dp", "mp"),
        P(None, "mp"),
        P("mp", "dp"),
        P(),
        P("dp", "mp"),
        P("mp"),
        P("mp", "dp"),
        P(),
        P(),
        P(None, None, "mp"),
        P(None, "mp"),
        P("mp", None),
        P(),
        P(None, "mp"),
        P("mp"),
        P("mp", None),
        P(),
        P(),
    )
    return jax.shard_map(body, mesh=mesh, in_specs=in_specs, out_specs=out_specs, check_vma=False)
```

```python
import jax
import jax.numpy as jnp
from jax import lax
from jax.sharding import PartitionSpec as P

D = 768
H = 12
DL = 192
WINDOW = 512


EPSILON = 1e-05
MASKED = -1000000000.0


def layer_norm(values, gain, shift):
    centered = values - jnp.mean(values, axis=-1, keepdims=True)
    variance = jnp.mean(centered * centered, axis=-1, keepdims=True)
    return centered * lax.rsqrt(variance + EPSILON) * gain + shift


def gelu(values):
    return 0.5 * values * (1.0 + lax.erf(values * 0.7071067811865476))


def project_path(rows, weight_qkv, biases):
    joined = jnp.einsum("rd,kde->kre", rows, weight_qkv, preferred_element_type=jnp.float32)
    queries = (joined[0] + biases[0]).astype(jnp.bfloat16)
    key_rows = joined[1].astype(jnp.bfloat16)
    value_rows = (joined[2] + biases[1]).astype(jnp.bfloat16)
    return (queries, key_rows, value_rows)


def blocked(values, head_size):
    return values.reshape(-1, WINDOW, values.shape[-1] // head_size, head_size)


def unblocked(values):
    return values.reshape(-1, values.shape[-2] * values.shape[-1])


def coupled_scores(text_queries, text_keys, layout_queries, layout_keys, usable):
    scores = jnp.einsum(
        "qhd,khd->hqk", text_queries, text_keys, preferred_element_type=jnp.float32
    ) * (D // H) ** (-0.5)
    scores = scores + jnp.einsum(
        "qhd,khd->hqk", layout_queries, layout_keys, preferred_element_type=jnp.float32
    ) * (DL // H) ** (-0.5)
    return jnp.where(usable[None, None, :], scores, MASKED)


def attend_window(pieces):
    text_queries, text_keys, text_values, layout_queries, layout_keys, layout_values, usable = (
        pieces
    )
    scores = coupled_scores(text_queries, text_keys, layout_queries, layout_keys, usable)
    peak = jnp.max(scores, axis=-1, keepdims=True)
    powers = jnp.exp(scores - peak)
    total = jnp.sum(powers, axis=-1, keepdims=True)
    probs = (powers / total).astype(jnp.bfloat16)
    text_context = jnp.einsum(
        "hqk,khd->qhd", probs, text_values, preferred_element_type=jnp.float32
    ).astype(jnp.bfloat16)
    layout_context = jnp.einsum(
        "hqk,khd->qhd", probs, layout_values, preferred_element_type=jnp.float32
    ).astype(jnp.bfloat16)
    return (text_context, layout_context, peak + jnp.log(total))


def attend_back(pieces):
    (
        text_queries,
        text_keys,
        text_values,
        layout_queries,
        layout_keys,
        layout_values,
        usable,
        log_totals,
        text_cgrad,
        layout_cgrad,
    ) = pieces
    text_scale = (D // H) ** (-0.5)
    layout_scale = (DL // H) ** (-0.5)
    scores = coupled_scores(text_queries, text_keys, layout_queries, layout_keys, usable)
    probs = jnp.exp(scores - log_totals)
    probs_low = probs.astype(jnp.bfloat16)
    probs_grad = jnp.einsum(
        "qhd,khd->hqk", text_cgrad, text_values, preferred_element_type=jnp.float32
    )
    probs_grad = probs_grad + jnp.einsum(
        "qhd,khd->hqk", layout_cgrad, layout_values, preferred_element_type=jnp.float32
    )
    scores_grad = (
        probs * (probs_grad - jnp.sum(probs_grad * probs, axis=-1, keepdims=True))
    ).astype(jnp.bfloat16)
    text_vgrad = jnp.einsum(
        "hqk,qhd->khd", probs_low, text_cgrad, preferred_element_type=jnp.float32
    ).astype(jnp.bfloat16)
    layout_vgrad = jnp.einsum(
        "hqk,qhd->khd", probs_low, layout_cgrad, preferred_element_type=jnp.float32
    ).astype(jnp.bfloat16)
    text_qgrad = (
        jnp.einsum("hqk,khd->qhd", scores_grad, text_keys, preferred_element_type=jnp.float32)
        * text_scale
    ).astype(jnp.bfloat16)
    text_kgrad = (
        jnp.einsum("hqk,qhd->khd", scores_grad, text_queries, preferred_element_type=jnp.float32)
        * text_scale
    ).astype(jnp.bfloat16)
    layout_qgrad = (
        jnp.einsum("hqk,khd->qhd", scores_grad, layout_keys, preferred_element_type=jnp.float32)
        * layout_scale
    ).astype(jnp.bfloat16)
    layout_kgrad = (
        jnp.einsum("hqk,qhd->khd", scores_grad, layout_queries, preferred_element_type=jnp.float32)
        * layout_scale
    ).astype(jnp.bfloat16)
    return (text_qgrad, text_kgrad, text_vgrad, layout_qgrad, layout_kgrad, layout_vgrad)


def feed_forward(full_rows, w_up, up_bias, w_down):
    hidden = jnp.dot(full_rows, w_up, preferred_element_type=jnp.float32) + up_bias
    active, gelu_back = jax.vjp(gelu, hidden)
    active_low = active.astype(jnp.bfloat16)
    return (active_low, gelu_back, jnp.dot(active_low, w_down, preferred_element_type=jnp.float32))


def feed_back(full_rows, active_low, gelu_back, full_grad, w_up, w_down, down_spec="rf,rd->fd"):
    grad_down = jnp.einsum(down_spec, active_low, full_grad, preferred_element_type=jnp.float32)
    active_grad = jnp.einsum("rd,fd->rf", full_grad, w_down, preferred_element_type=jnp.float32)
    hidden_grad = gelu_back(active_grad)[0].astype(jnp.bfloat16)
    grad_up = jnp.einsum("rd,rf->df", full_rows, hidden_grad, preferred_element_type=jnp.float32)
    grad_bias = jnp.sum(hidden_grad, axis=0, dtype=jnp.float32)
    normed_part = jnp.einsum("rf,df->rd", hidden_grad, w_up, preferred_element_type=jnp.float32)
    return (grad_up, grad_bias, grad_down, normed_part)


def input_back(rows, weight_qkv, query_grad, key_grad, value_grad, stack_axis=0):
    grad_qkv = jnp.stack(
        [
            jnp.einsum("rd,re->de", rows, piece, preferred_element_type=jnp.float32)
            for piece in (query_grad, key_grad, value_grad)
        ],
        axis=stack_axis,
    )
    input_part = jnp.einsum(
        "re,de->rd", query_grad, weight_qkv[0], preferred_element_type=jnp.float32
    )
    input_part = input_part + jnp.einsum(
        "re,de->rd", key_grad, weight_qkv[1], preferred_element_type=jnp.float32
    )
    input_part = input_part + jnp.einsum(
        "re,de->rd", value_grad, weight_qkv[2], preferred_element_type=jnp.float32
    )
    grad_bias = jnp.stack(
        [
            jnp.sum(query_grad, axis=0, dtype=jnp.float32),
            jnp.sum(value_grad, axis=0, dtype=jnp.float32),
        ]
    )
    return (grad_qkv, grad_bias, input_part)


def xor_sum(values, axis, size):
    step = 1
    while step < size:
        values = values + lax.ppermute(
            values, axis, [(i, i ^ step) for i in range(size)]
        )
        step *= 2
    return values


def xor_exchange(values, step, size):
    return lax.ppermute(values, "dp", [(i, i ^ step) for i in range(size)])


def bit_orders(bits, colours):
    if bits <= 1:
        return [list(range(bits))] * colours
    main = list(range(bits - 1))
    orders = []
    for colour in range(colours):
        shift = colour % len(main)
        orders.append(main[shift:] + main[:shift] + [bits - 1])
    return orders


def halve(chunk, order, me, size, wire):
    for bit in order:
        mine = (me >> bit) & 1
        keep = lax.dynamic_index_in_dim(chunk, mine, axis=0, keepdims=False)
        send = lax.dynamic_index_in_dim(chunk, 1 - mine, axis=0, keepdims=False)
        chunk = keep + xor_exchange(send.astype(wire), 1 << bit, size).astype(chunk.dtype)
    return chunk


def double(block, order, me, size, bits):
    held = []
    for bit in reversed(order):
        other = xor_exchange(block, 1 << bit, size)
        mine = (me >> bit) & 1
        block = jnp.where(mine == 0, jnp.stack([block, other]), jnp.stack([other, block]))
        held.insert(0, bit)
    canonical = list(range(bits - 1, -1, -1))
    rest = list(range(len(held), block.ndim))
    block = jnp.transpose(block, [held.index(bit) for bit in canonical] + rest)
    return block.reshape((-1,) + block.shape[len(held) + 1 :])


def ordered(piece, order, size, bits):
    shaped = piece.reshape((2,) * bits + (piece.shape[0] // size,) + piece.shape[1:])
    canonical = list(range(bits - 1, -1, -1))
    rest = list(range(bits, shaped.ndim))
    return jnp.transpose(shaped, [canonical.index(bit) for bit in order] + rest)


def dp_reduce(scattered, colours_of, replicated, size, wire, lanes=128):
    bits = size.bit_length() - 1
    me = lax.axis_index("dp")
    orders = bit_orders(bits, 3)
    scattered_out = []
    for piece, colour in zip(scattered, colours_of):
        chunk = ordered(piece, orders[colour], size, bits)
        scattered_out.append(halve(chunk, orders[colour], me, size, wire))
    if not replicated:
        return scattered_out, []
    blocks = []
    for piece in replicated:
        flat = piece.reshape(-1)
        flat = jnp.pad(flat, (0, (-flat.shape[0]) % lanes))
        blocks.append(flat.reshape(-1, lanes))
    joined = jnp.concatenate(blocks)
    rows = joined.shape[0]
    joined = jnp.pad(joined, ((0, (-rows) % (size * 8)), (0, 0)))
    chunk = ordered(joined, orders[0], size, bits)
    block = halve(chunk, orders[0], me, size, wire)
    full = double(block, orders[0], me, size, bits)
    replicated_out = []
    offset = 0
    for piece in replicated:
        count = -(-piece.size // lanes)
        replicated_out.append(
            full[offset : offset + count].reshape(-1)[: piece.size].reshape(piece.shape)
        )
        offset += count
    return scattered_out, replicated_out

def body(
    text_input,
    layout_input,
    repeated,
    key_mask,
    text_qkv,
    text_qvbias,
    text_wout,
    text_outbias,
    text_wup,
    text_upbias,
    text_wdown,
    text_gains,
    text_shifts,
    layout_qkv,
    layout_qvbias,
    layout_wout,
    layout_outbias,
    layout_wup,
    layout_upbias,
    layout_wdown,
    layout_gains,
    layout_shifts,
    text_cotan,
    layout_cotan,
):
    text_head = D // H
    layout_head = DL // H
    usable_group = jnp.logical_and(key_mask == 1, repeated == 0).reshape(-1, WINDOW)
    text_rows, layout_rows = (
        lax.all_gather(text_input, "mp", axis=0, tiled=True),
        lax.all_gather(layout_input, "mp", axis=0, tiled=True),
    )
    text_queries, text_keys, text_values = project_path(text_rows, text_qkv, text_qvbias)
    layout_queries, layout_keys, layout_values = project_path(
        layout_rows, layout_qkv, layout_qvbias
    )
    blocks = (
        blocked(text_queries, text_head),
        blocked(text_keys, text_head),
        blocked(text_values, text_head),
        blocked(layout_queries, layout_head),
        blocked(layout_keys, layout_head),
        blocked(layout_values, layout_head),
        usable_group,
    )
    text_context, layout_context, log_totals = lax.map(attend_window, blocks)
    text_context = unblocked(text_context)
    layout_context = unblocked(layout_context)
    text_mixed_part = jnp.dot(text_context, text_wout, preferred_element_type=jnp.float32)
    layout_mixed_part = jnp.dot(layout_context, layout_wout, preferred_element_type=jnp.float32)
    text_mixed, layout_mixed = (
        lax.psum_scatter(
            text_mixed_part.astype(jnp.bfloat16), "mp", scatter_dimension=0, tiled=True
        ).astype(jnp.float32),
        lax.psum_scatter(
            layout_mixed_part.astype(jnp.bfloat16), "mp", scatter_dimension=0, tiled=True
        ).astype(jnp.float32),
    )
    text_gain = text_gains.astype(jnp.float32)
    text_shift = text_shifts.astype(jnp.float32)
    layout_gain = layout_gains.astype(jnp.float32)
    layout_shift = layout_shifts.astype(jnp.float32)
    text_normed, text_first_back = jax.vjp(
        layer_norm,
        text_input.astype(jnp.float32) + text_mixed + text_outbias[0],
        text_gain[0],
        text_shift[0],
    )
    layout_normed, layout_first_back = jax.vjp(
        layer_norm,
        layout_input.astype(jnp.float32) + layout_mixed + layout_outbias[0],
        layout_gain[0],
        layout_shift[0],
    )
    text_full, layout_full = (
        lax.all_gather(text_normed.astype(jnp.bfloat16), "mp", axis=0, tiled=True),
        lax.all_gather(layout_normed.astype(jnp.bfloat16), "mp", axis=0, tiled=True),
    )
    text_active, text_gelu_back, text_branch_part = feed_forward(
        text_full, text_wup, text_upbias, text_wdown
    )
    layout_active, layout_gelu_back, layout_branch_part = feed_forward(
        layout_full, layout_wup, layout_upbias, layout_wdown
    )
    text_branch, layout_branch = (
        lax.psum_scatter(
            text_branch_part.astype(jnp.bfloat16), "mp", scatter_dimension=0, tiled=True
        ).astype(jnp.float32),
        lax.psum_scatter(
            layout_branch_part.astype(jnp.bfloat16), "mp", scatter_dimension=0, tiled=True
        ).astype(jnp.float32),
    )
    text_final, text_final_back = jax.vjp(
        layer_norm, text_normed + text_branch + text_outbias[1], text_gain[1], text_shift[1]
    )
    layout_final, layout_final_back = jax.vjp(
        layer_norm,
        layout_normed + layout_branch + layout_outbias[1],
        layout_gain[1],
        layout_shift[1],
    )
    text_sum_grad, text_gain_second, text_shift_second = text_final_back(
        text_cotan.astype(jnp.float32)
    )
    layout_sum_grad, layout_gain_second, layout_shift_second = layout_final_back(
        layout_cotan.astype(jnp.float32)
    )
    text_branch_grad = text_sum_grad.astype(jnp.bfloat16)
    layout_branch_grad = layout_sum_grad.astype(jnp.bfloat16)
    text_full_grad, layout_full_grad = (
        lax.all_gather(text_branch_grad, "mp", axis=0, tiled=True),
        lax.all_gather(layout_branch_grad, "mp", axis=0, tiled=True),
    )
    text_wup_grad, text_upbias_grad, text_wdown_grad_t, text_normed_part = feed_back(
        text_full, text_active, text_gelu_back, text_full_grad, text_wup, text_wdown, "rf,rd->df"
    )
    layout_wup_grad, layout_upbias_grad, layout_wdown_grad, layout_normed_part = feed_back(
        layout_full, layout_active, layout_gelu_back, layout_full_grad, layout_wup, layout_wdown
    )
    text_normed_grad, layout_normed_grad = (
        lax.psum_scatter(
            text_normed_part.astype(jnp.bfloat16), "mp", scatter_dimension=0, tiled=True
        ).astype(jnp.float32),
        lax.psum_scatter(
            layout_normed_part.astype(jnp.bfloat16), "mp", scatter_dimension=0, tiled=True
        ).astype(jnp.float32),
    )
    text_mixed_grad, text_gain_first, text_shift_first = text_first_back(
        text_normed_grad + text_sum_grad
    )
    layout_mixed_grad, layout_gain_first, layout_shift_first = layout_first_back(
        layout_normed_grad + layout_sum_grad
    )
    text_mixed_low = text_mixed_grad.astype(jnp.bfloat16)
    layout_mixed_low = layout_mixed_grad.astype(jnp.bfloat16)
    text_wide_grad, layout_wide_grad = (
        lax.all_gather(text_mixed_low, "mp", axis=0, tiled=True),
        lax.all_gather(layout_mixed_low, "mp", axis=0, tiled=True),
    )
    text_wout_grad_t = jnp.einsum(
        "re,rd->de", text_context, text_wide_grad, preferred_element_type=jnp.float32
    )
    layout_wout_grad = jnp.einsum(
        "re,rd->ed", layout_context, layout_wide_grad, preferred_element_type=jnp.float32
    )
    text_context_grad = jnp.einsum(
        "rd,ed->re", text_wide_grad, text_wout, preferred_element_type=jnp.float32
    ).astype(jnp.bfloat16)
    layout_context_grad = jnp.einsum(
        "rd,ed->re", layout_wide_grad, layout_wout, preferred_element_type=jnp.float32
    ).astype(jnp.bfloat16)
    back_blocks = blocks + (
        log_totals,
        blocked(text_context_grad, text_head),
        blocked(layout_context_grad, layout_head),
    )
    text_qgrad, text_kgrad, text_vgrad, layout_qgrad, layout_kgrad, layout_vgrad = lax.map(
        attend_back, back_blocks
    )
    (text_wup_grad, text_wdown_grad_t), attended = lax.optimization_barrier(
        (
            (text_wup_grad, text_wdown_grad_t),
            (text_qgrad, text_kgrad, text_vgrad, layout_qgrad, layout_kgrad, layout_vgrad),
        )
    )
    text_qgrad, text_kgrad, text_vgrad, layout_qgrad, layout_kgrad, layout_vgrad = attended
    n_dp = lax.axis_size("dp")
    ffn_out, _ = dp_reduce((text_wup_grad, text_wdown_grad_t), (0, 1), (), n_dp, jnp.bfloat16)
    text_qkv_grad_t, text_qvbias_grad, text_input_part = input_back(
        text_rows,
        text_qkv,
        unblocked(text_qgrad),
        unblocked(text_kgrad),
        unblocked(text_vgrad),
        stack_axis=1,
    )
    layout_qkv_grad, layout_qvbias_grad, layout_input_part = input_back(
        layout_rows,
        layout_qkv,
        unblocked(layout_qgrad),
        unblocked(layout_kgrad),
        unblocked(layout_vgrad),
    )
    text_input_sum, layout_input_sum = (
        lax.psum_scatter(
            text_input_part.astype(jnp.bfloat16), "mp", scatter_dimension=0, tiled=True
        ).astype(jnp.float32),
        lax.psum_scatter(
            layout_input_part.astype(jnp.bfloat16), "mp", scatter_dimension=0, tiled=True
        ).astype(jnp.float32),
    )
    text_dinput = (text_mixed_grad + text_input_sum).astype(jnp.bfloat16)
    layout_dinput = (layout_mixed_grad + layout_input_sum).astype(jnp.bfloat16)
    n_mp = lax.axis_size("mp")
    small = jnp.concatenate(
        [
            part.reshape(-1)
            for part in (
                jnp.stack(
                    [
                        jnp.sum(text_mixed_low, axis=0, dtype=jnp.float32),
                        jnp.sum(text_branch_grad, axis=0, dtype=jnp.float32),
                    ]
                ),
                jnp.stack([text_gain_first, text_gain_second]),
                jnp.stack([text_shift_first, text_shift_second]),
                jnp.stack(
                    [
                        jnp.sum(layout_mixed_low, axis=0, dtype=jnp.float32),
                        jnp.sum(layout_branch_grad, axis=0, dtype=jnp.float32),
                    ]
                ),
                jnp.stack([layout_gain_first, layout_gain_second]),
                jnp.stack([layout_shift_first, layout_shift_second]),
            )
        ]
    )
    small = xor_sum(small, "mp", n_mp)
    scattered = (jnp.concatenate([text_qkv_grad_t, text_wout_grad_t[:, None, :]], axis=1),)
    replicated = (
        text_qvbias_grad,
        text_upbias_grad,
        layout_qkv_grad,
        layout_qvbias_grad,
        layout_wout_grad,
        layout_wup_grad,
        layout_upbias_grad,
        layout_wdown_grad,
        small,
    )
    scattered, replicated = lax.optimization_barrier((scattered, replicated))
    scattered_out, replicated_out = dp_reduce(
        scattered, (2,), replicated, n_dp, jnp.bfloat16
    )
    qkv_share = jnp.transpose(scattered_out[0][:, :3], (1, 0, 2))
    wout_share = scattered_out[0][:, 3].T
    wup_share = ffn_out[0]
    wdown_share = ffn_out[1].T
    summed = replicated_out[:8]
    small_sum = replicated_out[8]
    sizes = (2 * D, 2 * D, 2 * D, 2 * DL, 2 * DL, 2 * DL)
    shared = []
    offset = 0
    for size in sizes:
        shared.append(small_sum[offset : offset + size].reshape(2, -1))
        offset += size
    return (
        text_final.astype(jnp.bfloat16),
        layout_final.astype(jnp.bfloat16),
        text_dinput,
        layout_dinput,
        qkv_share,
        summed[0],
        wout_share,
        shared[0],
        wup_share,
        summed[1],
        wdown_share,
        shared[1],
        shared[2],
        summed[2],
        summed[3],
        summed[4],
        shared[3],
        summed[5],
        summed[6],
        summed[7],
        shared[4],
        shared[5],
    )


def solution(mesh):
    in_specs = (
        P(("dp", "mp"), None),
        P(("dp", "mp"), None),
        P("dp"),
        P("dp"),
        P(None, None, "mp"),
        P(None, "mp"),
        P("mp", None),
        P(),
        P(None, "mp"),
        P("mp"),
        P("mp", None),
        P(),
        P(),
        P(None, None, "mp"),
        P(None, "mp"),
        P("mp", None),
        P(),
        P(None, "mp"),
        P("mp"),
        P("mp", None),
        P(),
        P(),
        P(("dp", "mp"), None),
        P(("dp", "mp"), None),
    )
    out_specs = (
        P(("dp", "mp"), None),
        P(("dp", "mp"), None),
        P(("dp", "mp"), None),
        P(("dp", "mp"), None),
        P(None, "dp", "mp"),
        P(None, "mp"),
        P("mp", "dp"),
        P(),
        P("dp", "mp"),
        P("mp"),
        P("mp", "dp"),
        P(),
        P(),
        P(None, None, "mp"),
        P(None, "mp"),
        P("mp", None),
        P(),
        P(None, "mp"),
        P("mp"),
        P("mp", None),
        P(),
        P(),
    )
    return jax.shard_map(body, mesh=mesh, in_specs=in_specs, out_specs=out_specs, check_vma=False)
```

```python
import jax
import jax.numpy as jnp
from jax import lax
from jax.sharding import PartitionSpec as P

D = 768
H = 12
DL = 192
WINDOW = 512


EPSILON = 1e-05
MASKED = -1000000000.0


def layer_norm(values, gain, shift):
    centered = values - jnp.mean(values, axis=-1, keepdims=True)
    variance = jnp.mean(centered * centered, axis=-1, keepdims=True)
    return centered * lax.rsqrt(variance + EPSILON) * gain + shift


def gelu(values):
    return 0.5 * values * (1.0 + lax.erf(values * 0.7071067811865476))


def project_path(rows, weight_qkv, biases):
    joined = jnp.einsum("rd,kde->kre", rows, weight_qkv, preferred_element_type=jnp.float32)
    queries = (joined[0] + biases[0]).astype(jnp.bfloat16)
    key_rows = joined[1].astype(jnp.bfloat16)
    value_rows = (joined[2] + biases[1]).astype(jnp.bfloat16)
    return (queries, key_rows, value_rows)


def blocked(values, head_size):
    return values.reshape(-1, WINDOW, values.shape[-1] // head_size, head_size)


def unblocked(values):
    return values.reshape(-1, values.shape[-2] * values.shape[-1])


def coupled_scores(text_queries, text_keys, layout_queries, layout_keys, usable):
    scores = jnp.einsum(
        "qhd,khd->hqk", text_queries, text_keys, preferred_element_type=jnp.float32
    ) * (D // H) ** (-0.5)
    scores = scores + jnp.einsum(
        "qhd,khd->hqk", layout_queries, layout_keys, preferred_element_type=jnp.float32
    ) * (DL // H) ** (-0.5)
    return jnp.where(usable[None, None, :], scores, MASKED)


def attend_window(pieces):
    text_queries, text_keys, text_values, layout_queries, layout_keys, layout_values, usable = (
        pieces
    )
    scores = coupled_scores(text_queries, text_keys, layout_queries, layout_keys, usable)
    peak = jnp.max(scores, axis=-1, keepdims=True)
    powers = jnp.exp(scores - peak)
    total = jnp.sum(powers, axis=-1, keepdims=True)
    probs = (powers / total).astype(jnp.bfloat16)
    text_context = jnp.einsum(
        "hqk,khd->qhd", probs, text_values, preferred_element_type=jnp.float32
    ).astype(jnp.bfloat16)
    layout_context = jnp.einsum(
        "hqk,khd->qhd", probs, layout_values, preferred_element_type=jnp.float32
    ).astype(jnp.bfloat16)
    return (text_context, layout_context, peak + jnp.log(total))


def attend_back(pieces):
    (
        text_queries,
        text_keys,
        text_values,
        layout_queries,
        layout_keys,
        layout_values,
        usable,
        log_totals,
        text_cgrad,
        layout_cgrad,
    ) = pieces
    text_scale = (D // H) ** (-0.5)
    layout_scale = (DL // H) ** (-0.5)
    scores = coupled_scores(text_queries, text_keys, layout_queries, layout_keys, usable)
    probs = jnp.exp(scores - log_totals)
    probs_low = probs.astype(jnp.bfloat16)
    probs_grad = jnp.einsum(
        "qhd,khd->hqk", text_cgrad, text_values, preferred_element_type=jnp.float32
    )
    probs_grad = probs_grad + jnp.einsum(
        "qhd,khd->hqk", layout_cgrad, layout_values, preferred_element_type=jnp.float32
    )
    scores_grad = (
        probs * (probs_grad - jnp.sum(probs_grad * probs, axis=-1, keepdims=True))
    ).astype(jnp.bfloat16)
    text_vgrad = jnp.einsum(
        "hqk,qhd->khd", probs_low, text_cgrad, preferred_element_type=jnp.float32
    ).astype(jnp.bfloat16)
    layout_vgrad = jnp.einsum(
        "hqk,qhd->khd", probs_low, layout_cgrad, preferred_element_type=jnp.float32
    ).astype(jnp.bfloat16)
    text_qgrad = (
        jnp.einsum("hqk,khd->qhd", scores_grad, text_keys, preferred_element_type=jnp.float32)
        * text_scale
    ).astype(jnp.bfloat16)
    text_kgrad = (
        jnp.einsum("hqk,qhd->khd", scores_grad, text_queries, preferred_element_type=jnp.float32)
        * text_scale
    ).astype(jnp.bfloat16)
    layout_qgrad = (
        jnp.einsum("hqk,khd->qhd", scores_grad, layout_keys, preferred_element_type=jnp.float32)
        * layout_scale
    ).astype(jnp.bfloat16)
    layout_kgrad = (
        jnp.einsum("hqk,qhd->khd", scores_grad, layout_queries, preferred_element_type=jnp.float32)
        * layout_scale
    ).astype(jnp.bfloat16)
    return (text_qgrad, text_kgrad, text_vgrad, layout_qgrad, layout_kgrad, layout_vgrad)


def feed_forward(full_rows, w_up, up_bias, w_down):
    hidden = jnp.dot(full_rows, w_up, preferred_element_type=jnp.float32) + up_bias
    active, gelu_back = jax.vjp(gelu, hidden)
    active_low = active.astype(jnp.bfloat16)
    return (active_low, gelu_back, jnp.dot(active_low, w_down, preferred_element_type=jnp.float32))


def feed_back(full_rows, active_low, gelu_back, full_grad, w_up, w_down, down_spec="rf,rd->fd"):
    grad_down = jnp.einsum(down_spec, active_low, full_grad, preferred_element_type=jnp.float32)
    active_grad = jnp.einsum("rd,fd->rf", full_grad, w_down, preferred_element_type=jnp.float32)
    hidden_grad = gelu_back(active_grad)[0].astype(jnp.bfloat16)
    grad_up = jnp.einsum("rd,rf->df", full_rows, hidden_grad, preferred_element_type=jnp.float32)
    grad_bias = jnp.sum(hidden_grad, axis=0, dtype=jnp.float32)
    normed_part = jnp.einsum("rf,df->rd", hidden_grad, w_up, preferred_element_type=jnp.float32)
    return (grad_up, grad_bias, grad_down, normed_part)


def input_back(rows, weight_qkv, query_grad, key_grad, value_grad, stack_axis=0):
    grad_qkv = jnp.stack(
        [
            jnp.einsum("rd,re->de", rows, piece, preferred_element_type=jnp.float32)
            for piece in (query_grad, key_grad, value_grad)
        ],
        axis=stack_axis,
    )
    input_part = jnp.einsum(
        "re,de->rd", query_grad, weight_qkv[0], preferred_element_type=jnp.float32
    )
    input_part = input_part + jnp.einsum(
        "re,de->rd", key_grad, weight_qkv[1], preferred_element_type=jnp.float32
    )
    input_part = input_part + jnp.einsum(
        "re,de->rd", value_grad, weight_qkv[2], preferred_element_type=jnp.float32
    )
    grad_bias = jnp.stack(
        [
            jnp.sum(query_grad, axis=0, dtype=jnp.float32),
            jnp.sum(value_grad, axis=0, dtype=jnp.float32),
        ]
    )
    return (grad_qkv, grad_bias, input_part)


def xor_sum(values, axis, size):
    step = 1
    while step < size:
        values = values + lax.ppermute(
            values, axis, [(i, i ^ step) for i in range(size)]
        )
        step *= 2
    return values


def xor_exchange(values, step, size):
    return lax.ppermute(values, "dp", [(i, i ^ step) for i in range(size)])


def bit_orders(bits, colours):
    if bits <= 1:
        return [list(range(bits))] * colours
    main = list(range(bits - 1))
    orders = []
    for colour in range(colours):
        shift = colour % len(main)
        orders.append(main[shift:] + main[:shift] + [bits - 1])
    return orders


def halve(chunk, order, me, size, wire):
    for bit in order:
        mine = (me >> bit) & 1
        keep = lax.dynamic_index_in_dim(chunk, mine, axis=0, keepdims=False)
        send = lax.dynamic_index_in_dim(chunk, 1 - mine, axis=0, keepdims=False)
        chunk = keep + xor_exchange(send.astype(wire), 1 << bit, size).astype(chunk.dtype)
    return chunk


def double(block, order, me, size, bits):
    held = []
    for bit in reversed(order):
        other = xor_exchange(block, 1 << bit, size)
        mine = (me >> bit) & 1
        block = jnp.where(mine == 0, jnp.stack([block, other]), jnp.stack([other, block]))
        held.insert(0, bit)
    canonical = list(range(bits - 1, -1, -1))
    rest = list(range(len(held), block.ndim))
    block = jnp.transpose(block, [held.index(bit) for bit in canonical] + rest)
    return block.reshape((-1,) + block.shape[len(held) + 1 :])


def ordered(piece, order, size, bits):
    shaped = piece.reshape((2,) * bits + (piece.shape[0] // size,) + piece.shape[1:])
    canonical = list(range(bits - 1, -1, -1))
    rest = list(range(bits, shaped.ndim))
    return jnp.transpose(shaped, [canonical.index(bit) for bit in order] + rest)


def dp_reduce(scattered, colours_of, replicated, size, wire, rider=1):
    bits = size.bit_length() - 1
    me = lax.axis_index("dp")
    orders = bit_orders(bits, 3)
    host = scattered[rider]
    lanes = host.shape[-1]
    blocks = []
    for piece in replicated:
        flat = piece.reshape(-1)
        flat = jnp.pad(flat, (0, (-flat.shape[0]) % lanes))
        blocks.append(flat.reshape(-1, lanes))
    joined = jnp.concatenate(blocks)
    rows = joined.shape[0]
    joined = jnp.pad(joined, ((0, (-rows) % size), (0, 0)))
    extra = joined.shape[0] // size
    own = host.shape[0] // size
    carried = jnp.concatenate(
        [host.reshape(size, own, lanes), joined.reshape(size, extra, lanes)], axis=1
    ).reshape(size * (own + extra), lanes)
    pieces = list(scattered)
    pieces[rider] = carried
    scattered_out = []
    for piece, colour in zip(pieces, colours_of):
        chunk = ordered(piece, orders[colour], size, bits)
        scattered_out.append(halve(chunk, orders[colour], me, size, wire))
    block = scattered_out[rider][own:]
    scattered_out[rider] = scattered_out[rider][:own]
    full = double(block, orders[colours_of[rider]], me, size, bits).reshape(-1, lanes)
    replicated_out = []
    offset = 0
    for piece in replicated:
        count = -(-piece.size // lanes)
        replicated_out.append(
            full[offset : offset + count].reshape(-1)[: piece.size].reshape(piece.shape)
        )
        offset += count
    return scattered_out, replicated_out


def body(
    text_input,
    layout_input,
    repeated,
    key_mask,
    text_qkv,
    text_qvbias,
    text_wout,
    text_outbias,
    text_wup,
    text_upbias,
    text_wdown,
    text_gains,
    text_shifts,
    layout_qkv,
    layout_qvbias,
    layout_wout,
    layout_outbias,
    layout_wup,
    layout_upbias,
    layout_wdown,
    layout_gains,
    layout_shifts,
    text_cotan,
    layout_cotan,
):
    text_head = D // H
    layout_head = DL // H
    usable_group = jnp.logical_and(key_mask == 1, repeated == 0).reshape(-1, WINDOW)
    text_rows, layout_rows = (
        lax.all_gather(text_input, "mp", axis=0, tiled=True),
        lax.all_gather(layout_input, "mp", axis=0, tiled=True),
    )
    text_queries, text_keys, text_values = project_path(text_rows, text_qkv, text_qvbias)
    layout_queries, layout_keys, layout_values = project_path(
        layout_rows, layout_qkv, layout_qvbias
    )
    blocks = (
        blocked(text_queries, text_head),
        blocked(text_keys, text_head),
        blocked(text_values, text_head),
        blocked(layout_queries, layout_head),
        blocked(layout_keys, layout_head),
        blocked(layout_values, layout_head),
        usable_group,
    )
    text_context, layout_context, log_totals = lax.map(attend_window, blocks)
    text_context = unblocked(text_context)
    layout_context = unblocked(layout_context)
    text_mixed_part = jnp.dot(text_context, text_wout, preferred_element_type=jnp.float32)
    layout_mixed_part = jnp.dot(layout_context, layout_wout, preferred_element_type=jnp.float32)
    text_mixed, layout_mixed = (
        lax.psum_scatter(
            text_mixed_part.astype(jnp.bfloat16), "mp", scatter_dimension=0, tiled=True
        ).astype(jnp.float32),
        lax.psum_scatter(
            layout_mixed_part.astype(jnp.bfloat16), "mp", scatter_dimension=0, tiled=True
        ).astype(jnp.float32),
    )
    text_gain = text_gains.astype(jnp.float32)
    text_shift = text_shifts.astype(jnp.float32)
    layout_gain = layout_gains.astype(jnp.float32)
    layout_shift = layout_shifts.astype(jnp.float32)
    text_normed, text_first_back = jax.vjp(
        layer_norm,
        text_input.astype(jnp.float32) + text_mixed + text_outbias[0],
        text_gain[0],
        text_shift[0],
    )
    layout_normed, layout_first_back = jax.vjp(
        layer_norm,
        layout_input.astype(jnp.float32) + layout_mixed + layout_outbias[0],
        layout_gain[0],
        layout_shift[0],
    )
    text_full, layout_full = (
        lax.all_gather(text_normed.astype(jnp.bfloat16), "mp", axis=0, tiled=True),
        lax.all_gather(layout_normed.astype(jnp.bfloat16), "mp", axis=0, tiled=True),
    )
    text_active, text_gelu_back, text_branch_part = feed_forward(
        text_full, text_wup, text_upbias, text_wdown
    )
    layout_active, layout_gelu_back, layout_branch_part = feed_forward(
        layout_full, layout_wup, layout_upbias, layout_wdown
    )
    text_branch, layout_branch = (
        lax.psum_scatter(
            text_branch_part.astype(jnp.bfloat16), "mp", scatter_dimension=0, tiled=True
        ).astype(jnp.float32),
        lax.psum_scatter(
            layout_branch_part.astype(jnp.bfloat16), "mp", scatter_dimension=0, tiled=True
        ).astype(jnp.float32),
    )
    text_final, text_final_back = jax.vjp(
        layer_norm, text_normed + text_branch + text_outbias[1], text_gain[1], text_shift[1]
    )
    layout_final, layout_final_back = jax.vjp(
        layer_norm,
        layout_normed + layout_branch + layout_outbias[1],
        layout_gain[1],
        layout_shift[1],
    )
    text_sum_grad, text_gain_second, text_shift_second = text_final_back(
        text_cotan.astype(jnp.float32)
    )
    layout_sum_grad, layout_gain_second, layout_shift_second = layout_final_back(
        layout_cotan.astype(jnp.float32)
    )
    text_branch_grad = text_sum_grad.astype(jnp.bfloat16)
    layout_branch_grad = layout_sum_grad.astype(jnp.bfloat16)
    text_full_grad, layout_full_grad = (
        lax.all_gather(text_branch_grad, "mp", axis=0, tiled=True),
        lax.all_gather(layout_branch_grad, "mp", axis=0, tiled=True),
    )
    text_wup_grad, text_upbias_grad, text_wdown_grad_t, text_normed_part = feed_back(
        text_full, text_active, text_gelu_back, text_full_grad, text_wup, text_wdown, "rf,rd->df"
    )
    layout_wup_grad, layout_upbias_grad, layout_wdown_grad, layout_normed_part = feed_back(
        layout_full, layout_active, layout_gelu_back, layout_full_grad, layout_wup, layout_wdown
    )
    text_normed_grad, layout_normed_grad = (
        lax.psum_scatter(
            text_normed_part.astype(jnp.bfloat16), "mp", scatter_dimension=0, tiled=True
        ).astype(jnp.float32),
        lax.psum_scatter(
            layout_normed_part.astype(jnp.bfloat16), "mp", scatter_dimension=0, tiled=True
        ).astype(jnp.float32),
    )
    text_mixed_grad, text_gain_first, text_shift_first = text_first_back(
        text_normed_grad + text_sum_grad
    )
    layout_mixed_grad, layout_gain_first, layout_shift_first = layout_first_back(
        layout_normed_grad + layout_sum_grad
    )
    text_mixed_low = text_mixed_grad.astype(jnp.bfloat16)
    layout_mixed_low = layout_mixed_grad.astype(jnp.bfloat16)
    text_wide_grad, layout_wide_grad = (
        lax.all_gather(text_mixed_low, "mp", axis=0, tiled=True),
        lax.all_gather(layout_mixed_low, "mp", axis=0, tiled=True),
    )
    text_wout_grad_t = jnp.einsum(
        "re,rd->de", text_context, text_wide_grad, preferred_element_type=jnp.float32
    )
    layout_wout_grad = jnp.einsum(
        "re,rd->ed", layout_context, layout_wide_grad, preferred_element_type=jnp.float32
    )
    text_context_grad = jnp.einsum(
        "rd,ed->re", text_wide_grad, text_wout, preferred_element_type=jnp.float32
    ).astype(jnp.bfloat16)
    layout_context_grad = jnp.einsum(
        "rd,ed->re", layout_wide_grad, layout_wout, preferred_element_type=jnp.float32
    ).astype(jnp.bfloat16)
    back_blocks = blocks + (
        log_totals,
        blocked(text_context_grad, text_head),
        blocked(layout_context_grad, layout_head),
    )
    text_qgrad, text_kgrad, text_vgrad, layout_qgrad, layout_kgrad, layout_vgrad = lax.map(
        attend_back, back_blocks
    )
    text_qkv_grad_t, text_qvbias_grad, text_input_part = input_back(
        text_rows,
        text_qkv,
        unblocked(text_qgrad),
        unblocked(text_kgrad),
        unblocked(text_vgrad),
        stack_axis=1,
    )
    layout_qkv_grad, layout_qvbias_grad, layout_input_part = input_back(
        layout_rows,
        layout_qkv,
        unblocked(layout_qgrad),
        unblocked(layout_kgrad),
        unblocked(layout_vgrad),
    )
    text_input_sum, layout_input_sum = (
        lax.psum_scatter(
            text_input_part.astype(jnp.bfloat16), "mp", scatter_dimension=0, tiled=True
        ).astype(jnp.float32),
        lax.psum_scatter(
            layout_input_part.astype(jnp.bfloat16), "mp", scatter_dimension=0, tiled=True
        ).astype(jnp.float32),
    )
    text_dinput = (text_mixed_grad + text_input_sum).astype(jnp.bfloat16)
    layout_dinput = (layout_mixed_grad + layout_input_sum).astype(jnp.bfloat16)
    n_dp = lax.axis_size("dp")
    n_mp = lax.axis_size("mp")
    small = jnp.concatenate(
        [
            part.reshape(-1)
            for part in (
                jnp.stack(
                    [
                        jnp.sum(text_mixed_low, axis=0, dtype=jnp.float32),
                        jnp.sum(text_branch_grad, axis=0, dtype=jnp.float32),
                    ]
                ),
                jnp.stack([text_gain_first, text_gain_second]),
                jnp.stack([text_shift_first, text_shift_second]),
                jnp.stack(
                    [
                        jnp.sum(layout_mixed_low, axis=0, dtype=jnp.float32),
                        jnp.sum(layout_branch_grad, axis=0, dtype=jnp.float32),
                    ]
                ),
                jnp.stack([layout_gain_first, layout_gain_second]),
                jnp.stack([layout_shift_first, layout_shift_second]),
            )
        ]
    )
    small = xor_sum(small, "mp", n_mp)
    scattered = (
        jnp.concatenate([text_qkv_grad_t, text_wout_grad_t[:, None, :]], axis=1),
        text_wup_grad,
        text_wdown_grad_t,
    )
    replicated = (
        text_qvbias_grad,
        text_upbias_grad,
        layout_qkv_grad,
        layout_qvbias_grad,
        layout_wout_grad,
        layout_wup_grad,
        layout_upbias_grad,
        layout_wdown_grad,
        small,
    )
    scattered, replicated = lax.optimization_barrier((scattered, replicated))
    scattered_out, replicated_out = dp_reduce(
        scattered, (2, 0, 1), replicated, n_dp, jnp.bfloat16
    )
    qkv_share = jnp.transpose(scattered_out[0][:, :3], (1, 0, 2))
    wout_share = scattered_out[0][:, 3].T
    wup_share = scattered_out[1]
    wdown_share = scattered_out[2].T
    summed = replicated_out[:8]
    small_sum = replicated_out[8]
    sizes = (2 * D, 2 * D, 2 * D, 2 * DL, 2 * DL, 2 * DL)
    shared = []
    offset = 0
    for size in sizes:
        shared.append(small_sum[offset : offset + size].reshape(2, -1))
        offset += size
    return (
        text_final.astype(jnp.bfloat16),
        layout_final.astype(jnp.bfloat16),
        text_dinput,
        layout_dinput,
        qkv_share,
        summed[0],
        wout_share,
        shared[0],
        wup_share,
        summed[1],
        wdown_share,
        shared[1],
        shared[2],
        summed[2],
        summed[3],
        summed[4],
        shared[3],
        summed[5],
        summed[6],
        summed[7],
        shared[4],
        shared[5],
    )


def solution(mesh):
    in_specs = (
        P(("dp", "mp"), None),
        P(("dp", "mp"), None),
        P("dp"),
        P("dp"),
        P(None, None, "mp"),
        P(None, "mp"),
        P("mp", None),
        P(),
        P(None, "mp"),
        P("mp"),
        P("mp", None),
        P(),
        P(),
        P(None, None, "mp"),
        P(None, "mp"),
        P("mp", None),
        P(),
        P(None, "mp"),
        P("mp"),
        P("mp", None),
        P(),
        P(),
        P(("dp", "mp"), None),
        P(("dp", "mp"), None),
    )
    out_specs = (
        P(("dp", "mp"), None),
        P(("dp", "mp"), None),
        P(("dp", "mp"), None),
        P(("dp", "mp"), None),
        P(None, "dp", "mp"),
        P(None, "mp"),
        P("mp", "dp"),
        P(),
        P("dp", "mp"),
        P("mp"),
        P("mp", "dp"),
        P(),
        P(),
        P(None, None, "mp"),
        P(None, "mp"),
        P("mp", None),
        P(),
        P(None, "mp"),
        P("mp"),
        P("mp", None),
        P(),
        P(),
    )
    return jax.shard_map(body, mesh=mesh, in_specs=in_specs, out_specs=out_specs, check_vma=False)
```

```python
import jax
import jax.numpy as jnp
from jax import lax
from jax.sharding import PartitionSpec as P


D = 768
H = 12
DL = 192
WINDOW = 512


EPSILON = 1e-05
MASKED = -1000000000.0


def layer_norm(values, gain, shift):
    centered = values - jnp.mean(values, axis=-1, keepdims=True)
    variance = jnp.mean(centered * centered, axis=-1, keepdims=True)
    return centered * lax.rsqrt(variance + EPSILON) * gain + shift


def gelu(values):
    return 0.5 * values * (1.0 + lax.erf(values * 0.7071067811865476))


def project_path(rows, weight_qkv, biases):
    joined = jnp.einsum("rd,kde->kre", rows, weight_qkv, preferred_element_type=jnp.float32)
    queries = (joined[0] + biases[0]).astype(jnp.bfloat16)
    key_rows = joined[1].astype(jnp.bfloat16)
    value_rows = (joined[2] + biases[1]).astype(jnp.bfloat16)
    return (queries, key_rows, value_rows)


def blocked(values, head_size):
    return values.reshape(-1, WINDOW, values.shape[-1] // head_size, head_size)


def unblocked(values):
    return values.reshape(-1, values.shape[-2] * values.shape[-1])


def coupled_scores(text_queries, text_keys, layout_queries, layout_keys, usable):
    scores = jnp.einsum(
        "qhd,khd->hqk", text_queries, text_keys, preferred_element_type=jnp.float32
    ) * (D // H) ** (-0.5)
    scores = scores + jnp.einsum(
        "qhd,khd->hqk", layout_queries, layout_keys, preferred_element_type=jnp.float32
    ) * (DL // H) ** (-0.5)
    return jnp.where(usable[None, None, :], scores, MASKED)


def attend_window(pieces):
    text_queries, text_keys, text_values, layout_queries, layout_keys, layout_values, usable = (
        pieces
    )
    scores = coupled_scores(text_queries, text_keys, layout_queries, layout_keys, usable)
    peak = jnp.max(scores, axis=-1, keepdims=True)
    powers = jnp.exp(scores - peak)
    total = jnp.sum(powers, axis=-1, keepdims=True)
    probs = (powers / total).astype(jnp.bfloat16)
    text_context = jnp.einsum(
        "hqk,khd->qhd", probs, text_values, preferred_element_type=jnp.float32
    ).astype(jnp.bfloat16)
    layout_context = jnp.einsum(
        "hqk,khd->qhd", probs, layout_values, preferred_element_type=jnp.float32
    ).astype(jnp.bfloat16)
    return (text_context, layout_context, peak + jnp.log(total))


def attend_back(pieces):
    (
        text_queries,
        text_keys,
        text_values,
        layout_queries,
        layout_keys,
        layout_values,
        usable,
        log_totals,
        text_cgrad,
        layout_cgrad,
    ) = pieces
    text_scale = (D // H) ** (-0.5)
    layout_scale = (DL // H) ** (-0.5)
    scores = coupled_scores(text_queries, text_keys, layout_queries, layout_keys, usable)
    probs = jnp.exp(scores - log_totals)
    probs_low = probs.astype(jnp.bfloat16)
    probs_grad = jnp.einsum(
        "qhd,khd->hqk", text_cgrad, text_values, preferred_element_type=jnp.float32
    )
    probs_grad = probs_grad + jnp.einsum(
        "qhd,khd->hqk", layout_cgrad, layout_values, preferred_element_type=jnp.float32
    )
    scores_grad = (
        probs * (probs_grad - jnp.sum(probs_grad * probs, axis=-1, keepdims=True))
    ).astype(jnp.bfloat16)
    text_vgrad = jnp.einsum(
        "hqk,qhd->khd", probs_low, text_cgrad, preferred_element_type=jnp.float32
    ).astype(jnp.bfloat16)
    layout_vgrad = jnp.einsum(
        "hqk,qhd->khd", probs_low, layout_cgrad, preferred_element_type=jnp.float32
    ).astype(jnp.bfloat16)
    text_qgrad = (
        jnp.einsum("hqk,khd->qhd", scores_grad, text_keys, preferred_element_type=jnp.float32)
        * text_scale
    ).astype(jnp.bfloat16)
    text_kgrad = (
        jnp.einsum("hqk,qhd->khd", scores_grad, text_queries, preferred_element_type=jnp.float32)
        * text_scale
    ).astype(jnp.bfloat16)
    layout_qgrad = (
        jnp.einsum("hqk,khd->qhd", scores_grad, layout_keys, preferred_element_type=jnp.float32)
        * layout_scale
    ).astype(jnp.bfloat16)
    layout_kgrad = (
        jnp.einsum("hqk,qhd->khd", scores_grad, layout_queries, preferred_element_type=jnp.float32)
        * layout_scale
    ).astype(jnp.bfloat16)
    return (text_qgrad, text_kgrad, text_vgrad, layout_qgrad, layout_kgrad, layout_vgrad)


def feed_forward(full_rows, w_up, up_bias, w_down):
    hidden = jnp.dot(full_rows, w_up, preferred_element_type=jnp.float32) + up_bias
    active, gelu_back = jax.vjp(gelu, hidden)
    active_low = active.astype(jnp.bfloat16)
    return (active_low, gelu_back, jnp.dot(active_low, w_down, preferred_element_type=jnp.float32))


def feed_back(full_rows, active_low, gelu_back, full_grad, w_up, w_down, down_spec="rf,rd->fd"):
    grad_down = jnp.einsum(down_spec, active_low, full_grad, preferred_element_type=jnp.float32)
    active_grad = jnp.einsum("rd,fd->rf", full_grad, w_down, preferred_element_type=jnp.float32)
    hidden_grad = gelu_back(active_grad)[0].astype(jnp.bfloat16)
    grad_up = jnp.einsum("rd,rf->df", full_rows, hidden_grad, preferred_element_type=jnp.float32)
    grad_bias = jnp.sum(hidden_grad, axis=0, dtype=jnp.float32)
    normed_part = jnp.einsum("rf,df->rd", hidden_grad, w_up, preferred_element_type=jnp.float32)
    return (grad_up, grad_bias, grad_down, normed_part)


def input_back(rows, weight_qkv, query_grad, key_grad, value_grad, stack_axis=0):
    grad_qkv = jnp.stack(
        [
            jnp.einsum("rd,re->de", rows, piece, preferred_element_type=jnp.float32)
            for piece in (query_grad, key_grad, value_grad)
        ],
        axis=stack_axis,
    )
    input_part = jnp.einsum(
        "re,de->rd", query_grad, weight_qkv[0], preferred_element_type=jnp.float32
    )
    input_part = input_part + jnp.einsum(
        "re,de->rd", key_grad, weight_qkv[1], preferred_element_type=jnp.float32
    )
    input_part = input_part + jnp.einsum(
        "re,de->rd", value_grad, weight_qkv[2], preferred_element_type=jnp.float32
    )
    grad_bias = jnp.stack(
        [
            jnp.sum(query_grad, axis=0, dtype=jnp.float32),
            jnp.sum(value_grad, axis=0, dtype=jnp.float32),
        ]
    )
    return (grad_qkv, grad_bias, input_part)


def xor_sum(values, axis, size):
    step = 1
    while step < size:
        values = values + lax.ppermute(
            values, axis, [(i, i ^ step) for i in range(size)]
        )
        step *= 2
    return values


def xor_exchange(values, step, size):
    return lax.ppermute(values, "dp", [(i, i ^ step) for i in range(size)])


def bit_orders(bits, colours):
    if bits <= 1:
        return [list(range(bits))] * colours
    main = list(range(bits - 1))
    orders = []
    for colour in range(colours):
        shift = colour % len(main)
        orders.append(main[shift:] + main[:shift] + [bits - 1])
    return orders


def halve(chunk, order, me, size, wire):
    for bit in order:
        mine = (me >> bit) & 1
        keep = lax.dynamic_index_in_dim(chunk, mine, axis=0, keepdims=False)
        send = lax.dynamic_index_in_dim(chunk, 1 - mine, axis=0, keepdims=False)
        received = xor_exchange(send.astype(wire), 1 << bit, size)
        chunk = keep + received.astype(chunk.dtype)
    return chunk


def double(block, order, me, size, bits):
    held = []
    for bit in reversed(order):
        other = xor_exchange(block, 1 << bit, size)
        mine = (me >> bit) & 1
        block = jnp.where(mine == 0, jnp.stack([block, other]), jnp.stack([other, block]))
        held.insert(0, bit)
    canonical = list(range(bits - 1, -1, -1))
    rest = list(range(len(held), block.ndim))
    block = jnp.transpose(block, [held.index(bit) for bit in canonical] + rest)
    return block.reshape((-1,) + block.shape[len(held) + 1 :])


def ordered(piece, order, size, bits):
    shaped = piece.reshape((2,) * bits + (piece.shape[0] // size,) + piece.shape[1:])
    canonical = list(range(bits - 1, -1, -1))
    rest = list(range(bits, shaped.ndim))
    return jnp.transpose(shaped, [canonical.index(bit) for bit in order] + rest)


def dp_reduce(scattered, colours_of, replicated, size, wire, lanes=128):
    bits = size.bit_length() - 1
    me = lax.axis_index("dp")
    orders = bit_orders(bits, 3)
    scattered_out = []
    for piece, colour in zip(scattered, colours_of):
        chunk = ordered(piece, orders[colour], size, bits)
        scattered_out.append(halve(chunk, orders[colour], me, size, wire))
    if not replicated:
        return scattered_out, []
    blocks = []
    for piece in replicated:
        flat = piece.reshape(-1)
        flat = jnp.pad(flat, (0, (-flat.shape[0]) % lanes))
        blocks.append(flat.reshape(-1, lanes))
    joined = jnp.concatenate(blocks)
    rows = joined.shape[0]
    joined = jnp.pad(joined, ((0, (-rows) % (size * 8)), (0, 0)))
    chunk = ordered(joined, orders[2], size, bits)
    block = halve(chunk, orders[2], me, size, wire)
    full = double(block, orders[2], me, size, bits)
    replicated_out = []
    offset = 0
    for piece in replicated:
        count = -(-piece.size // lanes)
        replicated_out.append(
            full[offset : offset + count].reshape(-1)[: piece.size].reshape(piece.shape)
        )
        offset += count
    return scattered_out, replicated_out


def layer_body(
    text_input,
    layout_input,
    repeated,
    key_mask,
    text_qkv,
    text_qvbias,
    text_wout,
    text_outbias,
    text_wup,
    text_upbias,
    text_wdown,
    text_gains,
    text_shifts,
    layout_qkv,
    layout_qvbias,
    layout_wout,
    layout_outbias,
    layout_wup,
    layout_upbias,
    layout_wdown,
    layout_gains,
    layout_shifts,
    text_cotan,
    layout_cotan,
):
    text_head = D // H
    layout_head = DL // H
    usable_group = jnp.logical_and(key_mask == 1, repeated == 0).reshape(-1, WINDOW)
    text_rows, layout_rows = (
        lax.all_gather(text_input, "mp", axis=0, tiled=True),
        lax.all_gather(layout_input, "mp", axis=0, tiled=True),
    )
    text_queries, text_keys, text_values = project_path(text_rows, text_qkv, text_qvbias)
    layout_queries, layout_keys, layout_values = project_path(
        layout_rows, layout_qkv, layout_qvbias
    )
    blocks = (
        blocked(text_queries, text_head),
        blocked(text_keys, text_head),
        blocked(text_values, text_head),
        blocked(layout_queries, layout_head),
        blocked(layout_keys, layout_head),
        blocked(layout_values, layout_head),
        usable_group,
    )
    text_context, layout_context, log_totals = lax.map(attend_window, blocks)
    text_context = unblocked(text_context)
    layout_context = unblocked(layout_context)
    text_mixed_part = jnp.dot(text_context, text_wout, preferred_element_type=jnp.float32)
    layout_mixed_part = jnp.dot(layout_context, layout_wout, preferred_element_type=jnp.float32)
    text_mixed, layout_mixed = (
        lax.psum_scatter(
            text_mixed_part.astype(jnp.bfloat16), "mp", scatter_dimension=0, tiled=True
        ).astype(jnp.float32),
        lax.psum_scatter(
            layout_mixed_part.astype(jnp.bfloat16), "mp", scatter_dimension=0, tiled=True
        ).astype(jnp.float32),
    )
    text_gain = text_gains.astype(jnp.float32)
    text_shift = text_shifts.astype(jnp.float32)
    layout_gain = layout_gains.astype(jnp.float32)
    layout_shift = layout_shifts.astype(jnp.float32)
    text_normed, text_first_back = jax.vjp(
        layer_norm,
        text_input.astype(jnp.float32) + text_mixed + text_outbias[0],
        text_gain[0],
        text_shift[0],
    )
    layout_normed, layout_first_back = jax.vjp(
        layer_norm,
        layout_input.astype(jnp.float32) + layout_mixed + layout_outbias[0],
        layout_gain[0],
        layout_shift[0],
    )
    text_full, layout_full = (
        lax.all_gather(text_normed.astype(jnp.bfloat16), "mp", axis=0, tiled=True),
        lax.all_gather(layout_normed.astype(jnp.bfloat16), "mp", axis=0, tiled=True),
    )
    text_active, text_gelu_back, text_branch_part = feed_forward(
        text_full, text_wup, text_upbias, text_wdown
    )
    layout_active, layout_gelu_back, layout_branch_part = feed_forward(
        layout_full, layout_wup, layout_upbias, layout_wdown
    )
    text_branch, layout_branch = (
        lax.psum_scatter(
            text_branch_part.astype(jnp.bfloat16), "mp", scatter_dimension=0, tiled=True
        ).astype(jnp.float32),
        lax.psum_scatter(
            layout_branch_part.astype(jnp.bfloat16), "mp", scatter_dimension=0, tiled=True
        ).astype(jnp.float32),
    )
    text_final, text_final_back = jax.vjp(
        layer_norm, text_normed + text_branch + text_outbias[1], text_gain[1], text_shift[1]
    )
    layout_final, layout_final_back = jax.vjp(
        layer_norm,
        layout_normed + layout_branch + layout_outbias[1],
        layout_gain[1],
        layout_shift[1],
    )
    text_sum_grad, text_gain_second, text_shift_second = text_final_back(
        text_cotan.astype(jnp.float32)
    )
    layout_sum_grad, layout_gain_second, layout_shift_second = layout_final_back(
        layout_cotan.astype(jnp.float32)
    )
    text_branch_grad = text_sum_grad.astype(jnp.bfloat16)
    layout_branch_grad = layout_sum_grad.astype(jnp.bfloat16)
    text_full_grad, layout_full_grad = (
        lax.all_gather(text_branch_grad, "mp", axis=0, tiled=True),
        lax.all_gather(layout_branch_grad, "mp", axis=0, tiled=True),
    )
    text_wup_grad, text_upbias_grad, text_wdown_grad_t, text_normed_part = feed_back(
        text_full, text_active, text_gelu_back, text_full_grad, text_wup, text_wdown, "rf,rd->df"
    )
    layout_wup_grad, layout_upbias_grad, layout_wdown_grad, layout_normed_part = feed_back(
        layout_full, layout_active, layout_gelu_back, layout_full_grad, layout_wup, layout_wdown
    )
    text_normed_grad, layout_normed_grad = (
        lax.psum_scatter(
            text_normed_part.astype(jnp.bfloat16), "mp", scatter_dimension=0, tiled=True
        ).astype(jnp.float32),
        lax.psum_scatter(
            layout_normed_part.astype(jnp.bfloat16), "mp", scatter_dimension=0, tiled=True
        ).astype(jnp.float32),
    )
    text_mixed_grad, text_gain_first, text_shift_first = text_first_back(
        text_normed_grad + text_sum_grad
    )
    layout_mixed_grad, layout_gain_first, layout_shift_first = layout_first_back(
        layout_normed_grad + layout_sum_grad
    )
    text_mixed_low = text_mixed_grad.astype(jnp.bfloat16)
    layout_mixed_low = layout_mixed_grad.astype(jnp.bfloat16)
    text_wide_grad, layout_wide_grad = (
        lax.all_gather(text_mixed_low, "mp", axis=0, tiled=True),
        lax.all_gather(layout_mixed_low, "mp", axis=0, tiled=True),
    )
    text_wout_grad_t = jnp.einsum(
        "re,rd->de", text_context, text_wide_grad, preferred_element_type=jnp.float32
    )
    layout_wout_grad = jnp.einsum(
        "re,rd->ed", layout_context, layout_wide_grad, preferred_element_type=jnp.float32
    )
    text_context_grad = jnp.einsum(
        "rd,ed->re", text_wide_grad, text_wout, preferred_element_type=jnp.float32
    ).astype(jnp.bfloat16)
    layout_context_grad = jnp.einsum(
        "rd,ed->re", layout_wide_grad, layout_wout, preferred_element_type=jnp.float32
    ).astype(jnp.bfloat16)
    back_blocks = blocks + (
        log_totals,
        blocked(text_context_grad, text_head),
        blocked(layout_context_grad, layout_head),
    )
    text_qgrad, text_kgrad, text_vgrad, layout_qgrad, layout_kgrad, layout_vgrad = lax.map(
        attend_back, back_blocks
    )
    (text_wup_grad, text_wdown_grad_t), attended = lax.optimization_barrier(
        (
            (text_wup_grad, text_wdown_grad_t),
            (text_qgrad, text_kgrad, text_vgrad, layout_qgrad, layout_kgrad, layout_vgrad),
        )
    )
    text_qgrad, text_kgrad, text_vgrad, layout_qgrad, layout_kgrad, layout_vgrad = attended
    n_dp = lax.axis_size("dp")
    ffn_out, _ = dp_reduce((text_wup_grad, text_wdown_grad_t), (0, 1), (), n_dp, jnp.bfloat16)
    text_qkv_grad_t, text_qvbias_grad, text_input_part = input_back(
        text_rows,
        text_qkv,
        unblocked(text_qgrad),
        unblocked(text_kgrad),
        unblocked(text_vgrad),
        stack_axis=1,
    )
    layout_qkv_grad, layout_qvbias_grad, layout_input_part = input_back(
        layout_rows,
        layout_qkv,
        unblocked(layout_qgrad),
        unblocked(layout_kgrad),
        unblocked(layout_vgrad),
    )
    text_input_sum, layout_input_sum = (
        lax.psum_scatter(
            text_input_part.astype(jnp.bfloat16), "mp", scatter_dimension=0, tiled=True
        ).astype(jnp.float32),
        lax.psum_scatter(
            layout_input_part.astype(jnp.bfloat16), "mp", scatter_dimension=0, tiled=True
        ).astype(jnp.float32),
    )
    text_dinput = (text_mixed_grad + text_input_sum).astype(jnp.bfloat16)
    layout_dinput = (layout_mixed_grad + layout_input_sum).astype(jnp.bfloat16)
    n_mp = lax.axis_size("mp")
    small = jnp.concatenate(
        [
            part.reshape(-1)
            for part in (
                jnp.stack(
                    [
                        jnp.sum(text_mixed_low, axis=0, dtype=jnp.float32),
                        jnp.sum(text_branch_grad, axis=0, dtype=jnp.float32),
                    ]
                ),
                jnp.stack([text_gain_first, text_gain_second]),
                jnp.stack([text_shift_first, text_shift_second]),
                jnp.stack(
                    [
                        jnp.sum(layout_mixed_low, axis=0, dtype=jnp.float32),
                        jnp.sum(layout_branch_grad, axis=0, dtype=jnp.float32),
                    ]
                ),
                jnp.stack([layout_gain_first, layout_gain_second]),
                jnp.stack([layout_shift_first, layout_shift_second]),
            )
        ]
    )
    small = xor_sum(small, "mp", n_mp)
    scattered = (jnp.concatenate([text_qkv_grad_t, text_wout_grad_t[:, None, :]], axis=1),)
    replicated = (
        text_qvbias_grad,
        text_upbias_grad,
        layout_qkv_grad,
        layout_qvbias_grad,
        layout_wout_grad,
        layout_wup_grad,
        layout_upbias_grad,
        layout_wdown_grad,
        small,
    )
    scattered, replicated = lax.optimization_barrier((scattered, replicated))
    scattered_out, replicated_out = dp_reduce(
        scattered, (2,), replicated, n_dp, jnp.bfloat16
    )
    qkv_share = jnp.transpose(scattered_out[0][:, :3], (1, 0, 2))
    wout_share = scattered_out[0][:, 3].T
    wup_share = ffn_out[0]
    wdown_share = ffn_out[1].T
    summed = replicated_out[:8]
    small_sum = replicated_out[8]
    sizes = (2 * D, 2 * D, 2 * D, 2 * DL, 2 * DL, 2 * DL)
    shared = []
    offset = 0
    for size in sizes:
        shared.append(small_sum[offset : offset + size].reshape(2, -1))
        offset += size
    return (
        text_final.astype(jnp.bfloat16),
        layout_final.astype(jnp.bfloat16),
        text_dinput,
        layout_dinput,
        qkv_share,
        summed[0],
        wout_share,
        shared[0],
        wup_share,
        summed[1],
        wdown_share,
        shared[1],
        shared[2],
        summed[2],
        summed[3],
        summed[4],
        shared[3],
        summed[5],
        summed[6],
        summed[7],
        shared[4],
        shared[5],
    )


def solution(mesh):
    in_specs = (
        P(("dp", "mp"), None),
        P(("dp", "mp"), None),
        P("dp"),
        P("dp"),
        P(None, None, "mp"),
        P(None, "mp"),
        P("mp", None),
        P(),
        P(None, "mp"),
        P("mp"),
        P("mp", None),
        P(),
        P(),
        P(None, None, "mp"),
        P(None, "mp"),
        P("mp", None),
        P(),
        P(None, "mp"),
        P("mp"),
        P("mp", None),
        P(),
        P(),
        P(("dp", "mp"), None),
        P(("dp", "mp"), None),
    )
    out_specs = (
        P(("dp", "mp"), None),
        P(("dp", "mp"), None),
        P(("dp", "mp"), None),
        P(("dp", "mp"), None),
        P(None, "dp", "mp"),
        P(None, "mp"),
        P("mp", "dp"),
        P(),
        P("dp", "mp"),
        P("mp"),
        P("mp", "dp"),
        P(),
        P(),
        P(None, None, "mp"),
        P(None, "mp"),
        P("mp", None),
        P(),
        P(None, "mp"),
        P("mp"),
        P("mp", None),
        P(),
        P(),
    )
    return jax.shard_map(layer_body, mesh=mesh, in_specs=in_specs, out_specs=out_specs, check_vma=False)
```

```python
import jax
import jax.numpy as jnp
from jax import lax
from jax.sharding import PartitionSpec as P

D = 768
H = 12
DL = 192
WINDOW = 512


EPSILON = 1e-05
MASKED = -1000000000.0


def layer_norm(values, gain, shift):
    centered = values - jnp.mean(values, axis=-1, keepdims=True)
    variance = jnp.mean(centered * centered, axis=-1, keepdims=True)
    return centered * lax.rsqrt(variance + EPSILON) * gain + shift


def gelu(values):
    return 0.5 * values * (1.0 + lax.erf(values * 0.7071067811865476))


def project_path(rows, weight_qkv, biases):
    joined = jnp.einsum("rd,kde->kre", rows, weight_qkv, preferred_element_type=jnp.float32)
    queries = (joined[0] + biases[0]).astype(jnp.bfloat16)
    key_rows = joined[1].astype(jnp.bfloat16)
    value_rows = (joined[2] + biases[1]).astype(jnp.bfloat16)
    return (queries, key_rows, value_rows)


def blocked(values, head_size):
    return values.reshape(-1, WINDOW, values.shape[-1] // head_size, head_size)


def unblocked(values):
    return values.reshape(-1, values.shape[-2] * values.shape[-1])


def coupled_scores(text_queries, text_keys, layout_queries, layout_keys, usable):
    scores = jnp.einsum(
        "qhd,khd->hqk", text_queries, text_keys, preferred_element_type=jnp.float32
    ) * (D // H) ** (-0.5)
    scores = scores + jnp.einsum(
        "qhd,khd->hqk", layout_queries, layout_keys, preferred_element_type=jnp.float32
    ) * (DL // H) ** (-0.5)
    return jnp.where(usable[None, None, :], scores, MASKED)


def attend_window(pieces):
    text_queries, text_keys, text_values, layout_queries, layout_keys, layout_values, usable = (
        pieces
    )
    scores = coupled_scores(text_queries, text_keys, layout_queries, layout_keys, usable)
    peak = jnp.max(scores, axis=-1, keepdims=True)
    powers = jnp.exp(scores - peak)
    total = jnp.sum(powers, axis=-1, keepdims=True)
    probs = (powers / total).astype(jnp.bfloat16)
    text_context = jnp.einsum(
        "hqk,khd->qhd", probs, text_values, preferred_element_type=jnp.float32
    ).astype(jnp.bfloat16)
    layout_context = jnp.einsum(
        "hqk,khd->qhd", probs, layout_values, preferred_element_type=jnp.float32
    ).astype(jnp.bfloat16)
    return (text_context, layout_context, peak + jnp.log(total))


def attend_back(pieces):
    (
        text_queries,
        text_keys,
        text_values,
        layout_queries,
        layout_keys,
        layout_values,
        usable,
        log_totals,
        text_cgrad,
        layout_cgrad,
    ) = pieces
    text_scale = (D // H) ** (-0.5)
    layout_scale = (DL // H) ** (-0.5)
    scores = coupled_scores(text_queries, text_keys, layout_queries, layout_keys, usable)
    probs = jnp.exp(scores - log_totals)
    probs_low = probs.astype(jnp.bfloat16)
    probs_grad = jnp.einsum(
        "qhd,khd->hqk", text_cgrad, text_values, preferred_element_type=jnp.float32
    )
    probs_grad = probs_grad + jnp.einsum(
        "qhd,khd->hqk", layout_cgrad, layout_values, preferred_element_type=jnp.float32
    )
    scores_grad = (
        probs * (probs_grad - jnp.sum(probs_grad * probs, axis=-1, keepdims=True))
    ).astype(jnp.bfloat16)
    text_vgrad = jnp.einsum(
        "hqk,qhd->khd", probs_low, text_cgrad, preferred_element_type=jnp.float32
    ).astype(jnp.bfloat16)
    layout_vgrad = jnp.einsum(
        "hqk,qhd->khd", probs_low, layout_cgrad, preferred_element_type=jnp.float32
    ).astype(jnp.bfloat16)
    text_qgrad = (
        jnp.einsum("hqk,khd->qhd", scores_grad, text_keys, preferred_element_type=jnp.float32)
        * text_scale
    ).astype(jnp.bfloat16)
    text_kgrad = (
        jnp.einsum("hqk,qhd->khd", scores_grad, text_queries, preferred_element_type=jnp.float32)
        * text_scale
    ).astype(jnp.bfloat16)
    layout_qgrad = (
        jnp.einsum("hqk,khd->qhd", scores_grad, layout_keys, preferred_element_type=jnp.float32)
        * layout_scale
    ).astype(jnp.bfloat16)
    layout_kgrad = (
        jnp.einsum("hqk,qhd->khd", scores_grad, layout_queries, preferred_element_type=jnp.float32)
        * layout_scale
    ).astype(jnp.bfloat16)
    return (text_qgrad, text_kgrad, text_vgrad, layout_qgrad, layout_kgrad, layout_vgrad)


def feed_forward(full_rows, w_up, up_bias, w_down):
    hidden = jnp.dot(full_rows, w_up, preferred_element_type=jnp.float32) + up_bias
    active, gelu_back = jax.vjp(gelu, hidden)
    active_low = active.astype(jnp.bfloat16)
    return (active_low, gelu_back, jnp.dot(active_low, w_down, preferred_element_type=jnp.float32))


def feed_back(full_rows, active_low, gelu_back, full_grad, w_up, w_down, down_spec="rf,rd->fd"):
    grad_down = jnp.einsum(down_spec, active_low, full_grad, preferred_element_type=jnp.float32)
    active_grad = jnp.einsum("rd,fd->rf", full_grad, w_down, preferred_element_type=jnp.float32)
    hidden_grad = gelu_back(active_grad)[0].astype(jnp.bfloat16)
    grad_up = jnp.einsum("rd,rf->df", full_rows, hidden_grad, preferred_element_type=jnp.float32)
    grad_bias = jnp.sum(hidden_grad, axis=0, dtype=jnp.float32)
    normed_part = jnp.einsum("rf,df->rd", hidden_grad, w_up, preferred_element_type=jnp.float32)
    return (grad_up, grad_bias, grad_down, normed_part)


def input_back(rows, weight_qkv, query_grad, key_grad, value_grad, stack_axis=0):
    grad_qkv = jnp.stack(
        [
            jnp.einsum("rd,re->de", rows, piece, preferred_element_type=jnp.float32)
            for piece in (query_grad, key_grad, value_grad)
        ],
        axis=stack_axis,
    )
    input_part = jnp.einsum(
        "re,de->rd", query_grad, weight_qkv[0], preferred_element_type=jnp.float32
    )
    input_part = input_part + jnp.einsum(
        "re,de->rd", key_grad, weight_qkv[1], preferred_element_type=jnp.float32
    )
    input_part = input_part + jnp.einsum(
        "re,de->rd", value_grad, weight_qkv[2], preferred_element_type=jnp.float32
    )
    grad_bias = jnp.stack(
        [
            jnp.sum(query_grad, axis=0, dtype=jnp.float32),
            jnp.sum(value_grad, axis=0, dtype=jnp.float32),
        ]
    )
    return (grad_qkv, grad_bias, input_part)


def xor_sum(values, axis, size):
    step = 1
    while step < size:
        values = values + lax.ppermute(
            values, axis, [(i, i ^ step) for i in range(size)]
        )
        step *= 2
    return values


def xor_exchange(values, step, size):
    return lax.ppermute(values, "dp", [(i, i ^ step) for i in range(size)])


def bit_orders(bits, colours):
    if bits <= 1:
        return [list(range(bits))] * colours
    main = list(range(bits - 1))
    orders = []
    for colour in range(colours):
        shift = colour % len(main)
        orders.append(main[shift:] + main[:shift] + [bits - 1])
    return orders


def halve(chunk, order, me, size, wire):
    for bit in order:
        mine = (me >> bit) & 1
        keep = lax.dynamic_index_in_dim(chunk, mine, axis=0, keepdims=False)
        send = lax.dynamic_index_in_dim(chunk, 1 - mine, axis=0, keepdims=False)
        chunk = keep + xor_exchange(send.astype(wire), 1 << bit, size).astype(chunk.dtype)
    return chunk


def double(block, order, me, size, bits):
    held = []
    for bit in reversed(order):
        other = xor_exchange(block, 1 << bit, size)
        mine = (me >> bit) & 1
        block = jnp.where(mine == 0, jnp.stack([block, other]), jnp.stack([other, block]))
        held.insert(0, bit)
    canonical = list(range(bits - 1, -1, -1))
    rest = list(range(len(held), block.ndim))
    block = jnp.transpose(block, [held.index(bit) for bit in canonical] + rest)
    return block.reshape((-1,) + block.shape[len(held) + 1 :])


def group_masks(pair):
    high, low = pair
    return [(((t >> 1) & 1) << high) | ((t & 1) << low) for t in range(4)]


def halve_groups(chunk, groups, me, size, wire):
    for group in groups:
        if len(group) == 1:
            chunk = halve(chunk, list(group), me, size, wire)
            continue
        high, low = group
        chunk = chunk.reshape((4,) + chunk.shape[2:])
        mine = ((me >> high) & 1) * 2 + ((me >> low) & 1)
        masks = group_masks(group)
        total = lax.dynamic_index_in_dim(chunk, mine, axis=0, keepdims=False)
        for t in range(1, 4):
            send = lax.dynamic_index_in_dim(chunk, mine ^ t, axis=0, keepdims=False)
            total = total + xor_exchange(send.astype(wire), masks[t], size).astype(chunk.dtype)
        chunk = total
    return chunk


def double_groups(block, groups, me, size, bits):
    held = []
    for group in reversed(groups):
        if len(group) == 1:
            (bit,) = group
            other = xor_exchange(block, 1 << bit, size)
            mine = (me >> bit) & 1
            block = jnp.where(mine == 0, jnp.stack([block, other]), jnp.stack([other, block]))
            held.insert(0, bit)
            continue
        high, low = group
        masks = group_masks(group)
        mine = ((me >> high) & 1) * 2 + ((me >> low) & 1)
        pieces = jnp.stack([block] + [xor_exchange(block, masks[t], size) for t in range(1, 4)])
        block = jnp.take(pieces, jnp.arange(4) ^ mine, axis=0)
        block = block.reshape((2, 2) + block.shape[1:])
        held = [high, low] + held
    canonical = list(range(bits - 1, -1, -1))
    rest = list(range(len(held), block.ndim))
    block = jnp.transpose(block, [held.index(bit) for bit in canonical] + rest)
    return block.reshape((-1,) + block.shape[len(held) + 1 :])


def ordered(piece, order, size, bits):
    shaped = piece.reshape((2,) * bits + (piece.shape[0] // size,) + piece.shape[1:])
    canonical = list(range(bits - 1, -1, -1))
    rest = list(range(bits, shaped.ndim))
    return jnp.transpose(shaped, [canonical.index(bit) for bit in order] + rest)


def dp_reduce(scattered, colours_of, replicated, size, wire, lanes=128):
    bits = size.bit_length() - 1
    me = lax.axis_index("dp")
    orders = bit_orders(bits, 3)
    scattered_out = []
    for piece, colour in zip(scattered, colours_of):
        chunk = ordered(piece, orders[colour], size, bits)
        scattered_out.append(halve(chunk, orders[colour], me, size, wire))
    if not replicated:
        return scattered_out, []
    blocks = []
    for piece in replicated:
        flat = piece.reshape(-1)
        flat = jnp.pad(flat, (0, (-flat.shape[0]) % lanes))
        blocks.append(flat.reshape(-1, lanes))
    joined = jnp.concatenate(blocks)
    rows = joined.shape[0]
    joined = jnp.pad(joined, ((0, (-rows) % (size * 8)), (0, 0)))
    order = orders[0]
    groups = [(bit,) for bit in order[:-2]] + [tuple(order[-2:])] if bits >= 2 else [(b,) for b in order]
    chunk = ordered(joined, order, size, bits)
    block = halve_groups(chunk, groups, me, size, wire)
    full = double_groups(block, groups, me, size, bits)
    replicated_out = []
    offset = 0
    for piece in replicated:
        count = -(-piece.size // lanes)
        replicated_out.append(
            full[offset : offset + count].reshape(-1)[: piece.size].reshape(piece.shape)
        )
        offset += count
    return scattered_out, replicated_out

def body(
    text_input,
    layout_input,
    repeated,
    key_mask,
    text_qkv,
    text_qvbias,
    text_wout,
    text_outbias,
    text_wup,
    text_upbias,
    text_wdown,
    text_gains,
    text_shifts,
    layout_qkv,
    layout_qvbias,
    layout_wout,
    layout_outbias,
    layout_wup,
    layout_upbias,
    layout_wdown,
    layout_gains,
    layout_shifts,
    text_cotan,
    layout_cotan,
):
    text_head = D // H
    layout_head = DL // H
    usable_group = jnp.logical_and(key_mask == 1, repeated == 0).reshape(-1, WINDOW)
    text_rows, layout_rows = (
        lax.all_gather(text_input, "mp", axis=0, tiled=True),
        lax.all_gather(layout_input, "mp", axis=0, tiled=True),
    )
    text_queries, text_keys, text_values = project_path(text_rows, text_qkv, text_qvbias)
    layout_queries, layout_keys, layout_values = project_path(
        layout_rows, layout_qkv, layout_qvbias
    )
    blocks = (
        blocked(text_queries, text_head),
        blocked(text_keys, text_head),
        blocked(text_values, text_head),
        blocked(layout_queries, layout_head),
        blocked(layout_keys, layout_head),
        blocked(layout_values, layout_head),
        usable_group,
    )
    text_context, layout_context, log_totals = lax.map(attend_window, blocks)
    text_context = unblocked(text_context)
    layout_context = unblocked(layout_context)
    text_mixed_part = jnp.dot(text_context, text_wout, preferred_element_type=jnp.float32)
    layout_mixed_part = jnp.dot(layout_context, layout_wout, preferred_element_type=jnp.float32)
    text_mixed, layout_mixed = (
        lax.psum_scatter(
            text_mixed_part.astype(jnp.bfloat16), "mp", scatter_dimension=0, tiled=True
        ).astype(jnp.float32),
        lax.psum_scatter(
            layout_mixed_part.astype(jnp.bfloat16), "mp", scatter_dimension=0, tiled=True
        ).astype(jnp.float32),
    )
    text_gain = text_gains.astype(jnp.float32)
    text_shift = text_shifts.astype(jnp.float32)
    layout_gain = layout_gains.astype(jnp.float32)
    layout_shift = layout_shifts.astype(jnp.float32)
    text_normed, text_first_back = jax.vjp(
        layer_norm,
        text_input.astype(jnp.float32) + text_mixed + text_outbias[0],
        text_gain[0],
        text_shift[0],
    )
    layout_normed, layout_first_back = jax.vjp(
        layer_norm,
        layout_input.astype(jnp.float32) + layout_mixed + layout_outbias[0],
        layout_gain[0],
        layout_shift[0],
    )
    text_full, layout_full = (
        lax.all_gather(text_normed.astype(jnp.bfloat16), "mp", axis=0, tiled=True),
        lax.all_gather(layout_normed.astype(jnp.bfloat16), "mp", axis=0, tiled=True),
    )
    text_active, text_gelu_back, text_branch_part = feed_forward(
        text_full, text_wup, text_upbias, text_wdown
    )
    layout_active, layout_gelu_back, layout_branch_part = feed_forward(
        layout_full, layout_wup, layout_upbias, layout_wdown
    )
    text_branch, layout_branch = (
        lax.psum_scatter(
            text_branch_part.astype(jnp.bfloat16), "mp", scatter_dimension=0, tiled=True
        ).astype(jnp.float32),
        lax.psum_scatter(
            layout_branch_part.astype(jnp.bfloat16), "mp", scatter_dimension=0, tiled=True
        ).astype(jnp.float32),
    )
    text_final, text_final_back = jax.vjp(
        layer_norm, text_normed + text_branch + text_outbias[1], text_gain[1], text_shift[1]
    )
    layout_final, layout_final_back = jax.vjp(
        layer_norm,
        layout_normed + layout_branch + layout_outbias[1],
        layout_gain[1],
        layout_shift[1],
    )
    text_sum_grad, text_gain_second, text_shift_second = text_final_back(
        text_cotan.astype(jnp.float32)
    )
    layout_sum_grad, layout_gain_second, layout_shift_second = layout_final_back(
        layout_cotan.astype(jnp.float32)
    )
    text_branch_grad = text_sum_grad.astype(jnp.bfloat16)
    layout_branch_grad = layout_sum_grad.astype(jnp.bfloat16)
    text_full_grad, layout_full_grad = (
        lax.all_gather(text_branch_grad, "mp", axis=0, tiled=True),
        lax.all_gather(layout_branch_grad, "mp", axis=0, tiled=True),
    )
    text_wup_grad, text_upbias_grad, text_wdown_grad_t, text_normed_part = feed_back(
        text_full, text_active, text_gelu_back, text_full_grad, text_wup, text_wdown, "rf,rd->df"
    )
    layout_wup_grad, layout_upbias_grad, layout_wdown_grad, layout_normed_part = feed_back(
        layout_full, layout_active, layout_gelu_back, layout_full_grad, layout_wup, layout_wdown
    )
    text_normed_grad, layout_normed_grad = (
        lax.psum_scatter(
            text_normed_part.astype(jnp.bfloat16), "mp", scatter_dimension=0, tiled=True
        ).astype(jnp.float32),
        lax.psum_scatter(
            layout_normed_part.astype(jnp.bfloat16), "mp", scatter_dimension=0, tiled=True
        ).astype(jnp.float32),
    )
    text_mixed_grad, text_gain_first, text_shift_first = text_first_back(
        text_normed_grad + text_sum_grad
    )
    layout_mixed_grad, layout_gain_first, layout_shift_first = layout_first_back(
        layout_normed_grad + layout_sum_grad
    )
    text_mixed_low = text_mixed_grad.astype(jnp.bfloat16)
    layout_mixed_low = layout_mixed_grad.astype(jnp.bfloat16)
    text_wide_grad, layout_wide_grad = (
        lax.all_gather(text_mixed_low, "mp", axis=0, tiled=True),
        lax.all_gather(layout_mixed_low, "mp", axis=0, tiled=True),
    )
    text_wout_grad_t = jnp.einsum(
        "re,rd->de", text_context, text_wide_grad, preferred_element_type=jnp.float32
    )
    layout_wout_grad = jnp.einsum(
        "re,rd->ed", layout_context, layout_wide_grad, preferred_element_type=jnp.float32
    )
    text_context_grad = jnp.einsum(
        "rd,ed->re", text_wide_grad, text_wout, preferred_element_type=jnp.float32
    ).astype(jnp.bfloat16)
    layout_context_grad = jnp.einsum(
        "rd,ed->re", layout_wide_grad, layout_wout, preferred_element_type=jnp.float32
    ).astype(jnp.bfloat16)
    back_blocks = blocks + (
        log_totals,
        blocked(text_context_grad, text_head),
        blocked(layout_context_grad, layout_head),
    )
    text_qgrad, text_kgrad, text_vgrad, layout_qgrad, layout_kgrad, layout_vgrad = lax.map(
        attend_back, back_blocks
    )
    (text_wup_grad, text_wdown_grad_t), attended = lax.optimization_barrier(
        (
            (text_wup_grad, text_wdown_grad_t),
            (text_qgrad, text_kgrad, text_vgrad, layout_qgrad, layout_kgrad, layout_vgrad),
        )
    )
    text_qgrad, text_kgrad, text_vgrad, layout_qgrad, layout_kgrad, layout_vgrad = attended
    n_dp = lax.axis_size("dp")
    ffn_out, _ = dp_reduce((text_wup_grad, text_wdown_grad_t), (0, 1), (), n_dp, jnp.bfloat16)
    text_qkv_grad_t, text_qvbias_grad, text_input_part = input_back(
        text_rows,
        text_qkv,
        unblocked(text_qgrad),
        unblocked(text_kgrad),
        unblocked(text_vgrad),
        stack_axis=1,
    )
    layout_qkv_grad, layout_qvbias_grad, layout_input_part = input_back(
        layout_rows,
        layout_qkv,
        unblocked(layout_qgrad),
        unblocked(layout_kgrad),
        unblocked(layout_vgrad),
    )
    text_input_sum, layout_input_sum = (
        lax.psum_scatter(
            text_input_part.astype(jnp.bfloat16), "mp", scatter_dimension=0, tiled=True
        ).astype(jnp.float32),
        lax.psum_scatter(
            layout_input_part.astype(jnp.bfloat16), "mp", scatter_dimension=0, tiled=True
        ).astype(jnp.float32),
    )
    text_dinput = (text_mixed_grad + text_input_sum).astype(jnp.bfloat16)
    layout_dinput = (layout_mixed_grad + layout_input_sum).astype(jnp.bfloat16)
    n_mp = lax.axis_size("mp")
    small = jnp.concatenate(
        [
            part.reshape(-1)
            for part in (
                jnp.stack(
                    [
                        jnp.sum(text_mixed_low, axis=0, dtype=jnp.float32),
                        jnp.sum(text_branch_grad, axis=0, dtype=jnp.float32),
                    ]
                ),
                jnp.stack([text_gain_first, text_gain_second]),
                jnp.stack([text_shift_first, text_shift_second]),
                jnp.stack(
                    [
                        jnp.sum(layout_mixed_low, axis=0, dtype=jnp.float32),
                        jnp.sum(layout_branch_grad, axis=0, dtype=jnp.float32),
                    ]
                ),
                jnp.stack([layout_gain_first, layout_gain_second]),
                jnp.stack([layout_shift_first, layout_shift_second]),
            )
        ]
    )
    small = xor_sum(small, "mp", n_mp)
    scattered = (jnp.concatenate([text_qkv_grad_t, text_wout_grad_t[:, None, :]], axis=1),)
    replicated = (
        text_qvbias_grad,
        text_upbias_grad,
        layout_qkv_grad,
        layout_qvbias_grad,
        layout_wout_grad,
        layout_wup_grad,
        layout_upbias_grad,
        layout_wdown_grad,
        small,
    )
    scattered, replicated = lax.optimization_barrier((scattered, replicated))
    scattered_out, replicated_out = dp_reduce(
        scattered, (2,), replicated, n_dp, jnp.bfloat16
    )
    qkv_share = jnp.transpose(scattered_out[0][:, :3], (1, 0, 2))
    wout_share = scattered_out[0][:, 3].T
    wup_share = ffn_out[0]
    wdown_share = ffn_out[1].T
    summed = replicated_out[:8]
    small_sum = replicated_out[8]
    sizes = (2 * D, 2 * D, 2 * D, 2 * DL, 2 * DL, 2 * DL)
    shared = []
    offset = 0
    for size in sizes:
        shared.append(small_sum[offset : offset + size].reshape(2, -1))
        offset += size
    return (
        text_final.astype(jnp.bfloat16),
        layout_final.astype(jnp.bfloat16),
        text_dinput,
        layout_dinput,
        qkv_share,
        summed[0],
        wout_share,
        shared[0],
        wup_share,
        summed[1],
        wdown_share,
        shared[1],
        shared[2],
        summed[2],
        summed[3],
        summed[4],
        shared[3],
        summed[5],
        summed[6],
        summed[7],
        shared[4],
        shared[5],
    )


def solution(mesh):
    in_specs = (
        P(("dp", "mp"), None),
        P(("dp", "mp"), None),
        P("dp"),
        P("dp"),
        P(None, None, "mp"),
        P(None, "mp"),
        P("mp", None),
        P(),
        P(None, "mp"),
        P("mp"),
        P("mp", None),
        P(),
        P(),
        P(None, None, "mp"),
        P(None, "mp"),
        P("mp", None),
        P(),
        P(None, "mp"),
        P("mp"),
        P("mp", None),
        P(),
        P(),
        P(("dp", "mp"), None),
        P(("dp", "mp"), None),
    )
    out_specs = (
        P(("dp", "mp"), None),
        P(("dp", "mp"), None),
        P(("dp", "mp"), None),
        P(("dp", "mp"), None),
        P(None, "dp", "mp"),
        P(None, "mp"),
        P("mp", "dp"),
        P(),
        P("dp", "mp"),
        P("mp"),
        P("mp", "dp"),
        P(),
        P(),
        P(None, None, "mp"),
        P(None, "mp"),
        P("mp", None),
        P(),
        P(None, "mp"),
        P("mp"),
        P("mp", None),
        P(),
        P(),
    )
    return jax.shard_map(body, mesh=mesh, in_specs=in_specs, out_specs=out_specs, check_vma=False)
```

```python
import jax
import jax.numpy as jnp
from jax import lax
from jax.sharding import PartitionSpec as P

D = 768
H = 12
DL = 192
WINDOW = 512


EPSILON = 1e-05
MASKED = -1000000000.0


def layer_norm(values, gain, shift):
    centered = values - jnp.mean(values, axis=-1, keepdims=True)
    variance = jnp.mean(centered * centered, axis=-1, keepdims=True)
    return centered * lax.rsqrt(variance + EPSILON) * gain + shift


def gelu(values):
    return 0.5 * values * (1.0 + lax.erf(values * 0.7071067811865476))


def project_path(rows, weight_qkv, biases):
    joined = jnp.einsum("rd,kde->kre", rows, weight_qkv, preferred_element_type=jnp.float32)
    queries = (joined[0] + biases[0]).astype(jnp.bfloat16)
    key_rows = joined[1].astype(jnp.bfloat16)
    value_rows = (joined[2] + biases[1]).astype(jnp.bfloat16)
    return (queries, key_rows, value_rows)


def blocked(values, head_size):
    return values.reshape(-1, WINDOW, values.shape[-1] // head_size, head_size)


def unblocked(values):
    return values.reshape(-1, values.shape[-2] * values.shape[-1])


def coupled_scores(text_queries, text_keys, layout_queries, layout_keys, usable):
    scores = jnp.einsum(
        "qhd,khd->hqk", text_queries, text_keys, preferred_element_type=jnp.float32
    ) * (D // H) ** (-0.5)
    scores = scores + jnp.einsum(
        "qhd,khd->hqk", layout_queries, layout_keys, preferred_element_type=jnp.float32
    ) * (DL // H) ** (-0.5)
    return jnp.where(usable[None, None, :], scores, MASKED)


def attend_window(pieces):
    text_queries, text_keys, text_values, layout_queries, layout_keys, layout_values, usable = (
        pieces
    )
    scores = coupled_scores(text_queries, text_keys, layout_queries, layout_keys, usable)
    peak = jnp.max(scores, axis=-1, keepdims=True)
    powers = jnp.exp(scores - peak)
    total = jnp.sum(powers, axis=-1, keepdims=True)
    probs = (powers / total).astype(jnp.bfloat16)
    text_context = jnp.einsum(
        "hqk,khd->qhd", probs, text_values, preferred_element_type=jnp.float32
    ).astype(jnp.bfloat16)
    layout_context = jnp.einsum(
        "hqk,khd->qhd", probs, layout_values, preferred_element_type=jnp.float32
    ).astype(jnp.bfloat16)
    return (text_context, layout_context, peak + jnp.log(total))


def attend_back(pieces):
    (
        text_queries,
        text_keys,
        text_values,
        layout_queries,
        layout_keys,
        layout_values,
        usable,
        log_totals,
        text_cgrad,
        layout_cgrad,
    ) = pieces
    text_scale = (D // H) ** (-0.5)
    layout_scale = (DL // H) ** (-0.5)
    scores = coupled_scores(text_queries, text_keys, layout_queries, layout_keys, usable)
    probs = jnp.exp(scores - log_totals)
    probs_low = probs.astype(jnp.bfloat16)
    probs_grad = jnp.einsum(
        "qhd,khd->hqk", text_cgrad, text_values, preferred_element_type=jnp.float32
    )
    probs_grad = probs_grad + jnp.einsum(
        "qhd,khd->hqk", layout_cgrad, layout_values, preferred_element_type=jnp.float32
    )
    scores_grad = (
        probs * (probs_grad - jnp.sum(probs_grad * probs, axis=-1, keepdims=True))
    ).astype(jnp.bfloat16)
    text_vgrad = jnp.einsum(
        "hqk,qhd->khd", probs_low, text_cgrad, preferred_element_type=jnp.float32
    ).astype(jnp.bfloat16)
    layout_vgrad = jnp.einsum(
        "hqk,qhd->khd", probs_low, layout_cgrad, preferred_element_type=jnp.float32
    ).astype(jnp.bfloat16)
    text_qgrad = (
        jnp.einsum("hqk,khd->qhd", scores_grad, text_keys, preferred_element_type=jnp.float32)
        * text_scale
    ).astype(jnp.bfloat16)
    text_kgrad = (
        jnp.einsum("hqk,qhd->khd", scores_grad, text_queries, preferred_element_type=jnp.float32)
        * text_scale
    ).astype(jnp.bfloat16)
    layout_qgrad = (
        jnp.einsum("hqk,khd->qhd", scores_grad, layout_keys, preferred_element_type=jnp.float32)
        * layout_scale
    ).astype(jnp.bfloat16)
    layout_kgrad = (
        jnp.einsum("hqk,qhd->khd", scores_grad, layout_queries, preferred_element_type=jnp.float32)
        * layout_scale
    ).astype(jnp.bfloat16)
    return (text_qgrad, text_kgrad, text_vgrad, layout_qgrad, layout_kgrad, layout_vgrad)


def feed_forward(full_rows, w_up, up_bias, w_down):
    hidden = jnp.dot(full_rows, w_up, preferred_element_type=jnp.float32) + up_bias
    active, gelu_back = jax.vjp(gelu, hidden)
    active_low = active.astype(jnp.bfloat16)
    return (active_low, gelu_back, jnp.dot(active_low, w_down, preferred_element_type=jnp.float32))


def feed_back(full_rows, active_low, gelu_back, full_grad, w_up, w_down, down_spec="rf,rd->fd"):
    grad_down = jnp.einsum(down_spec, active_low, full_grad, preferred_element_type=jnp.float32)
    active_grad = jnp.einsum("rd,fd->rf", full_grad, w_down, preferred_element_type=jnp.float32)
    hidden_grad = gelu_back(active_grad)[0].astype(jnp.bfloat16)
    grad_up = jnp.einsum("rd,rf->df", full_rows, hidden_grad, preferred_element_type=jnp.float32)
    grad_bias = jnp.sum(hidden_grad, axis=0, dtype=jnp.float32)
    normed_part = jnp.einsum("rf,df->rd", hidden_grad, w_up, preferred_element_type=jnp.float32)
    return (grad_up, grad_bias, grad_down, normed_part)


def input_back(rows, weight_qkv, query_grad, key_grad, value_grad, stack_axis=0):
    grad_qkv = jnp.stack(
        [
            jnp.einsum("rd,re->de", rows, piece, preferred_element_type=jnp.float32)
            for piece in (query_grad, key_grad, value_grad)
        ],
        axis=stack_axis,
    )
    input_part = jnp.einsum(
        "re,de->rd", query_grad, weight_qkv[0], preferred_element_type=jnp.float32
    )
    input_part = input_part + jnp.einsum(
        "re,de->rd", key_grad, weight_qkv[1], preferred_element_type=jnp.float32
    )
    input_part = input_part + jnp.einsum(
        "re,de->rd", value_grad, weight_qkv[2], preferred_element_type=jnp.float32
    )
    grad_bias = jnp.stack(
        [
            jnp.sum(query_grad, axis=0, dtype=jnp.float32),
            jnp.sum(value_grad, axis=0, dtype=jnp.float32),
        ]
    )
    return (grad_qkv, grad_bias, input_part)


def xor_sum(values, axis, size):
    step = 1
    while step < size:
        values = values + lax.ppermute(
            values, axis, [(i, i ^ step) for i in range(size)]
        )
        step *= 2
    return values


def xor_exchange(values, step, size):
    return lax.ppermute(values, "dp", [(i, i ^ step) for i in range(size)])


def bit_orders(bits, colours):
    if bits <= 1:
        return [list(range(bits))] * colours
    main = list(range(bits - 1))
    orders = []
    for colour in range(colours):
        shift = colour % len(main)
        orders.append(main[shift:] + main[:shift] + [bits - 1])
    return orders


def halve(chunk, order, me, size, wire):
    for bit in order:
        mine = (me >> bit) & 1
        keep = lax.dynamic_index_in_dim(chunk, mine, axis=0, keepdims=False)
        send = lax.dynamic_index_in_dim(chunk, 1 - mine, axis=0, keepdims=False)
        chunk = keep + xor_exchange(send.astype(wire), 1 << bit, size).astype(chunk.dtype)
    return chunk


def double(block, order, me, size, bits):
    held = []
    for bit in reversed(order):
        other = xor_exchange(block, 1 << bit, size)
        mine = (me >> bit) & 1
        block = jnp.where(mine == 0, jnp.stack([block, other]), jnp.stack([other, block]))
        held.insert(0, bit)
    canonical = list(range(bits - 1, -1, -1))
    rest = list(range(len(held), block.ndim))
    block = jnp.transpose(block, [held.index(bit) for bit in canonical] + rest)
    return block.reshape((-1,) + block.shape[len(held) + 1 :])


def group_masks(pair):
    high, low = pair
    return [(((t >> 1) & 1) << high) | ((t & 1) << low) for t in range(4)]


def halve_groups(chunk, groups, me, size, wire):
    for group in groups:
        if len(group) == 1:
            chunk = halve(chunk, list(group), me, size, wire)
            continue
        high, low = group
        chunk = chunk.reshape((4,) + chunk.shape[2:])
        mine = ((me >> high) & 1) * 2 + ((me >> low) & 1)
        masks = group_masks(group)
        total = lax.dynamic_index_in_dim(chunk, mine, axis=0, keepdims=False)
        for t in range(1, 4):
            send = lax.dynamic_index_in_dim(chunk, mine ^ t, axis=0, keepdims=False)
            total = total + xor_exchange(send.astype(wire), masks[t], size).astype(chunk.dtype)
        chunk = total
    return chunk


def double_groups(block, groups, me, size, bits):
    held = []
    for group in reversed(groups):
        if len(group) == 1:
            (bit,) = group
            other = xor_exchange(block, 1 << bit, size)
            mine = (me >> bit) & 1
            block = jnp.where(mine == 0, jnp.stack([block, other]), jnp.stack([other, block]))
            held.insert(0, bit)
            continue
        high, low = group
        masks = group_masks(group)
        mine = ((me >> high) & 1) * 2 + ((me >> low) & 1)
        pieces = jnp.stack([block] + [xor_exchange(block, masks[t], size) for t in range(1, 4)])
        block = jnp.take(pieces, jnp.arange(4) ^ mine, axis=0)
        block = block.reshape((2, 2) + block.shape[1:])
        held = [high, low] + held
    canonical = list(range(bits - 1, -1, -1))
    rest = list(range(len(held), block.ndim))
    block = jnp.transpose(block, [held.index(bit) for bit in canonical] + rest)
    return block.reshape((-1,) + block.shape[len(held) + 1 :])


def ordered(piece, order, size, bits):
    shaped = piece.reshape((2,) * bits + (piece.shape[0] // size,) + piece.shape[1:])
    canonical = list(range(bits - 1, -1, -1))
    rest = list(range(bits, shaped.ndim))
    return jnp.transpose(shaped, [canonical.index(bit) for bit in order] + rest)


def dp_reduce(scattered, colours_of, replicated, size, wire, lanes=128):
    bits = size.bit_length() - 1
    me = lax.axis_index("dp")
    orders = bit_orders(bits, 3)
    scattered_out = []
    for piece, colour in zip(scattered, colours_of):
        chunk = ordered(piece, orders[colour], size, bits)
        scattered_out.append(halve(chunk, orders[colour], me, size, wire))
    if not replicated:
        return scattered_out, []
    blocks = []
    for piece in replicated:
        flat = piece.reshape(-1)
        flat = jnp.pad(flat, (0, (-flat.shape[0]) % lanes))
        blocks.append(flat.reshape(-1, lanes))
    joined = jnp.concatenate(blocks)
    rows = joined.shape[0]
    joined = jnp.pad(joined, ((0, (-rows) % (size * 8)), (0, 0)))
    order = orders[0][-2:] + orders[0][:-2] if bits >= 2 else orders[0]
    groups = [tuple(order[:2])] + [(bit,) for bit in order[2:]] if bits >= 2 else [(order[0],)]
    chunk = ordered(joined, order, size, bits)
    block = halve_groups(chunk, groups, me, size, wire)
    full = double_groups(block, groups, me, size, bits)
    replicated_out = []
    offset = 0
    for piece in replicated:
        count = -(-piece.size // lanes)
        replicated_out.append(
            full[offset : offset + count].reshape(-1)[: piece.size].reshape(piece.shape)
        )
        offset += count
    return scattered_out, replicated_out

def body(
    text_input,
    layout_input,
    repeated,
    key_mask,
    text_qkv,
    text_qvbias,
    text_wout,
    text_outbias,
    text_wup,
    text_upbias,
    text_wdown,
    text_gains,
    text_shifts,
    layout_qkv,
    layout_qvbias,
    layout_wout,
    layout_outbias,
    layout_wup,
    layout_upbias,
    layout_wdown,
    layout_gains,
    layout_shifts,
    text_cotan,
    layout_cotan,
):
    text_head = D // H
    layout_head = DL // H
    usable_group = jnp.logical_and(key_mask == 1, repeated == 0).reshape(-1, WINDOW)
    text_rows, layout_rows = (
        lax.all_gather(text_input, "mp", axis=0, tiled=True),
        lax.all_gather(layout_input, "mp", axis=0, tiled=True),
    )
    text_queries, text_keys, text_values = project_path(text_rows, text_qkv, text_qvbias)
    layout_queries, layout_keys, layout_values = project_path(
        layout_rows, layout_qkv, layout_qvbias
    )
    blocks = (
        blocked(text_queries, text_head),
        blocked(text_keys, text_head),
        blocked(text_values, text_head),
        blocked(layout_queries, layout_head),
        blocked(layout_keys, layout_head),
        blocked(layout_values, layout_head),
        usable_group,
    )
    text_context, layout_context, log_totals = lax.map(attend_window, blocks)
    text_context = unblocked(text_context)
    layout_context = unblocked(layout_context)
    text_mixed_part = jnp.dot(text_context, text_wout, preferred_element_type=jnp.float32)
    layout_mixed_part = jnp.dot(layout_context, layout_wout, preferred_element_type=jnp.float32)
    text_mixed, layout_mixed = (
        lax.psum_scatter(
            text_mixed_part.astype(jnp.bfloat16), "mp", scatter_dimension=0, tiled=True
        ).astype(jnp.float32),
        lax.psum_scatter(
            layout_mixed_part.astype(jnp.bfloat16), "mp", scatter_dimension=0, tiled=True
        ).astype(jnp.float32),
    )
    text_gain = text_gains.astype(jnp.float32)
    text_shift = text_shifts.astype(jnp.float32)
    layout_gain = layout_gains.astype(jnp.float32)
    layout_shift = layout_shifts.astype(jnp.float32)
    text_normed, text_first_back = jax.vjp(
        layer_norm,
        text_input.astype(jnp.float32) + text_mixed + text_outbias[0],
        text_gain[0],
        text_shift[0],
    )
    layout_normed, layout_first_back = jax.vjp(
        layer_norm,
        layout_input.astype(jnp.float32) + layout_mixed + layout_outbias[0],
        layout_gain[0],
        layout_shift[0],
    )
    text_full, layout_full = (
        lax.all_gather(text_normed.astype(jnp.bfloat16), "mp", axis=0, tiled=True),
        lax.all_gather(layout_normed.astype(jnp.bfloat16), "mp", axis=0, tiled=True),
    )
    text_active, text_gelu_back, text_branch_part = feed_forward(
        text_full, text_wup, text_upbias, text_wdown
    )
    layout_active, layout_gelu_back, layout_branch_part = feed_forward(
        layout_full, layout_wup, layout_upbias, layout_wdown
    )
    text_branch, layout_branch = (
        lax.psum_scatter(
            text_branch_part.astype(jnp.bfloat16), "mp", scatter_dimension=0, tiled=True
        ).astype(jnp.float32),
        lax.psum_scatter(
            layout_branch_part.astype(jnp.bfloat16), "mp", scatter_dimension=0, tiled=True
        ).astype(jnp.float32),
    )
    text_final, text_final_back = jax.vjp(
        layer_norm, text_normed + text_branch + text_outbias[1], text_gain[1], text_shift[1]
    )
    layout_final, layout_final_back = jax.vjp(
        layer_norm,
        layout_normed + layout_branch + layout_outbias[1],
        layout_gain[1],
        layout_shift[1],
    )
    text_sum_grad, text_gain_second, text_shift_second = text_final_back(
        text_cotan.astype(jnp.float32)
    )
    layout_sum_grad, layout_gain_second, layout_shift_second = layout_final_back(
        layout_cotan.astype(jnp.float32)
    )
    text_branch_grad = text_sum_grad.astype(jnp.bfloat16)
    layout_branch_grad = layout_sum_grad.astype(jnp.bfloat16)
    text_full_grad, layout_full_grad = (
        lax.all_gather(text_branch_grad, "mp", axis=0, tiled=True),
        lax.all_gather(layout_branch_grad, "mp", axis=0, tiled=True),
    )
    text_wup_grad, text_upbias_grad, text_wdown_grad_t, text_normed_part = feed_back(
        text_full, text_active, text_gelu_back, text_full_grad, text_wup, text_wdown, "rf,rd->df"
    )
    layout_wup_grad, layout_upbias_grad, layout_wdown_grad, layout_normed_part = feed_back(
        layout_full, layout_active, layout_gelu_back, layout_full_grad, layout_wup, layout_wdown
    )
    text_normed_grad, layout_normed_grad = (
        lax.psum_scatter(
            text_normed_part.astype(jnp.bfloat16), "mp", scatter_dimension=0, tiled=True
        ).astype(jnp.float32),
        lax.psum_scatter(
            layout_normed_part.astype(jnp.bfloat16), "mp", scatter_dimension=0, tiled=True
        ).astype(jnp.float32),
    )
    text_mixed_grad, text_gain_first, text_shift_first = text_first_back(
        text_normed_grad + text_sum_grad
    )
    layout_mixed_grad, layout_gain_first, layout_shift_first = layout_first_back(
        layout_normed_grad + layout_sum_grad
    )
    text_mixed_low = text_mixed_grad.astype(jnp.bfloat16)
    layout_mixed_low = layout_mixed_grad.astype(jnp.bfloat16)
    text_wide_grad, layout_wide_grad = (
        lax.all_gather(text_mixed_low, "mp", axis=0, tiled=True),
        lax.all_gather(layout_mixed_low, "mp", axis=0, tiled=True),
    )
    text_wout_grad_t = jnp.einsum(
        "re,rd->de", text_context, text_wide_grad, preferred_element_type=jnp.float32
    )
    layout_wout_grad = jnp.einsum(
        "re,rd->ed", layout_context, layout_wide_grad, preferred_element_type=jnp.float32
    )
    text_context_grad = jnp.einsum(
        "rd,ed->re", text_wide_grad, text_wout, preferred_element_type=jnp.float32
    ).astype(jnp.bfloat16)
    layout_context_grad = jnp.einsum(
        "rd,ed->re", layout_wide_grad, layout_wout, preferred_element_type=jnp.float32
    ).astype(jnp.bfloat16)
    back_blocks = blocks + (
        log_totals,
        blocked(text_context_grad, text_head),
        blocked(layout_context_grad, layout_head),
    )
    text_qgrad, text_kgrad, text_vgrad, layout_qgrad, layout_kgrad, layout_vgrad = lax.map(
        attend_back, back_blocks
    )
    (text_wup_grad, text_wdown_grad_t), attended = lax.optimization_barrier(
        (
            (text_wup_grad, text_wdown_grad_t),
            (text_qgrad, text_kgrad, text_vgrad, layout_qgrad, layout_kgrad, layout_vgrad),
        )
    )
    text_qgrad, text_kgrad, text_vgrad, layout_qgrad, layout_kgrad, layout_vgrad = attended
    n_dp = lax.axis_size("dp")
    ffn_out, _ = dp_reduce((text_wup_grad, text_wdown_grad_t), (0, 1), (), n_dp, jnp.bfloat16)
    text_qkv_grad_t, text_qvbias_grad, text_input_part = input_back(
        text_rows,
        text_qkv,
        unblocked(text_qgrad),
        unblocked(text_kgrad),
        unblocked(text_vgrad),
        stack_axis=1,
    )
    layout_qkv_grad, layout_qvbias_grad, layout_input_part = input_back(
        layout_rows,
        layout_qkv,
        unblocked(layout_qgrad),
        unblocked(layout_kgrad),
        unblocked(layout_vgrad),
    )
    text_input_sum, layout_input_sum = (
        lax.psum_scatter(
            text_input_part.astype(jnp.bfloat16), "mp", scatter_dimension=0, tiled=True
        ).astype(jnp.float32),
        lax.psum_scatter(
            layout_input_part.astype(jnp.bfloat16), "mp", scatter_dimension=0, tiled=True
        ).astype(jnp.float32),
    )
    text_dinput = (text_mixed_grad + text_input_sum).astype(jnp.bfloat16)
    layout_dinput = (layout_mixed_grad + layout_input_sum).astype(jnp.bfloat16)
    n_mp = lax.axis_size("mp")
    small = jnp.concatenate(
        [
            part.reshape(-1)
            for part in (
                jnp.stack(
                    [
                        jnp.sum(text_mixed_low, axis=0, dtype=jnp.float32),
                        jnp.sum(text_branch_grad, axis=0, dtype=jnp.float32),
                    ]
                ),
                jnp.stack([text_gain_first, text_gain_second]),
                jnp.stack([text_shift_first, text_shift_second]),
                jnp.stack(
                    [
                        jnp.sum(layout_mixed_low, axis=0, dtype=jnp.float32),
                        jnp.sum(layout_branch_grad, axis=0, dtype=jnp.float32),
                    ]
                ),
                jnp.stack([layout_gain_first, layout_gain_second]),
                jnp.stack([layout_shift_first, layout_shift_second]),
            )
        ]
    )
    small = xor_sum(small, "mp", n_mp)
    scattered = (jnp.concatenate([text_qkv_grad_t, text_wout_grad_t[:, None, :]], axis=1),)
    replicated = (
        text_qvbias_grad,
        text_upbias_grad,
        layout_qkv_grad,
        layout_qvbias_grad,
        layout_wout_grad,
        layout_wup_grad,
        layout_upbias_grad,
        layout_wdown_grad,
        small,
    )
    scattered, replicated = lax.optimization_barrier((scattered, replicated))
    scattered_out, replicated_out = dp_reduce(
        scattered, (2,), replicated, n_dp, jnp.bfloat16
    )
    qkv_share = jnp.transpose(scattered_out[0][:, :3], (1, 0, 2))
    wout_share = scattered_out[0][:, 3].T
    wup_share = ffn_out[0]
    wdown_share = ffn_out[1].T
    summed = replicated_out[:8]
    small_sum = replicated_out[8]
    sizes = (2 * D, 2 * D, 2 * D, 2 * DL, 2 * DL, 2 * DL)
    shared = []
    offset = 0
    for size in sizes:
        shared.append(small_sum[offset : offset + size].reshape(2, -1))
        offset += size
    return (
        text_final.astype(jnp.bfloat16),
        layout_final.astype(jnp.bfloat16),
        text_dinput,
        layout_dinput,
        qkv_share,
        summed[0],
        wout_share,
        shared[0],
        wup_share,
        summed[1],
        wdown_share,
        shared[1],
        shared[2],
        summed[2],
        summed[3],
        summed[4],
        shared[3],
        summed[5],
        summed[6],
        summed[7],
        shared[4],
        shared[5],
    )


def solution(mesh):
    in_specs = (
        P(("dp", "mp"), None),
        P(("dp", "mp"), None),
        P("dp"),
        P("dp"),
        P(None, None, "mp"),
        P(None, "mp"),
        P("mp", None),
        P(),
        P(None, "mp"),
        P("mp"),
        P("mp", None),
        P(),
        P(),
        P(None, None, "mp"),
        P(None, "mp"),
        P("mp", None),
        P(),
        P(None, "mp"),
        P("mp"),
        P("mp", None),
        P(),
        P(),
        P(("dp", "mp"), None),
        P(("dp", "mp"), None),
    )
    out_specs = (
        P(("dp", "mp"), None),
        P(("dp", "mp"), None),
        P(("dp", "mp"), None),
        P(("dp", "mp"), None),
        P(None, "dp", "mp"),
        P(None, "mp"),
        P("mp", "dp"),
        P(),
        P("dp", "mp"),
        P("mp"),
        P("mp", "dp"),
        P(),
        P(),
        P(None, None, "mp"),
        P(None, "mp"),
        P("mp", None),
        P(),
        P(None, "mp"),
        P("mp"),
        P("mp", None),
        P(),
        P(),
    )
    return jax.shard_map(body, mesh=mesh, in_specs=in_specs, out_specs=out_specs, check_vma=False)
```
